128 devices in a mesh: scan: 8 (over z, x_lo), det: 16 (over y, x_hi, core).
Axes of the slice: x: 4 (x_hi: 2, x_lo: 2; x = x_hi * 2 + x_lo), y: 4, z: 4, core: 2. Of those that a mesh axis runs over, the one named last changes fastest.
Arguments:
- frames: bfloat16 [16, 1024, 16384], P('det', 'scan'), may hold values from -6 to 6
- offsets: int32 [16384, 2], P(('scan', 'det')), may hold values from -32 to 32
- bright: int32 [16384], P(('scan', 'det')), may hold values from 0 to 1, as said below
- aberration: float32 [2], replicated, may hold values from 0.5 to 2
Outputs:
- tiles: float32 [16, 8, 160], P('det', 'scan')
The draws below stay inside these ranges and needn't reach their ends.
Inputs may be any that keep to these rules, and one draw needn't show every extreme that they name: bright[k] is 1 exactly where (k // 128 - a)^2 + (k % 128 - b)^2 <= R^2 and 0 elsewhere, for one centre with whole a in 62 .. 66 and whole b in 62 .. 66, and one whole radius R in 40 .. 56, all ranges inclusive; so at least one pixel is 1.
All inputs are finite; a program needn't handle non-finite values.
Results may differ from the reference program's by a relative error of at most 0.0023.
Values may be sent and summed in bfloat16 or wider, within the bound.
No kernel may reach another device: no remote copies, remote signals or barrier semaphores. Data moves between devices by JAX's collectives and lax.ppermute only.
A program may use at most 128 MiB of HBM per device.

```python
import math
import jax
import jax.numpy as jnp
from jax import lax

SR = 16
SC = 1024
DROWS = 128
DCOLS = 128
HALO = 16
MAXSHIFT = 32
NDET = 16384
TILE = 128
N_SCAN = 8


def draw_bright(key, part):
    key_radius, key_row, key_col = jax.random.split(key, 3)
    radius = jax.random.randint(key_radius, (), DROWS * 5 // 16, DROWS * 7 // 16 + 1)
    centre_row = DROWS // 2 + jax.random.randint(key_row, (), -2, 3)
    centre_col = DCOLS // 2 + jax.random.randint(key_col, (), -2, 3)
    pixel_index = jnp.arange(NDET, dtype=jnp.int32)
    det_row = pixel_index // DCOLS
    det_col = pixel_index % DCOLS
    distance = (det_row - centre_row) * (det_row - centre_row) + (det_col - centre_col) * (det_col - centre_col)
    return (distance <= radius * radius).astype(jnp.int32)


def with_ends(result, key, low, high):
    spot = [jax.random.randint(jax.random.fold_in(key, axis), (), 0, length) for axis, length in enumerate(result.shape)]
    widest = result.shape.index(max(result.shape))
    beside = spot[:widest] + [(spot[widest] + 1) % result.shape[widest]] + spot[widest + 1:]
    return result.at[tuple(spot)].set(low).at[tuple(beside)].set(high)


def levels(own_key, shape, cuts, smallest, high):
    loudness = 1.0
    for dim, shards_of in cuts:
        steps = jax.random.uniform(jax.random.fold_in(jax.random.fold_in(own_key, 6), dim), (shards_of,), jnp.float32, smallest / len(cuts), high / len(cuts))
        loudness = loudness * jnp.repeat(jnp.exp(steps), shape[dim] // shards_of).reshape((-1,) + (1,) * (len(shape) - 1 - dim))
    return loudness


def gaussian(rng, shape, scale, reach, cuts=(), kind=jnp.bfloat16):
    result = scale * jax.random.normal(rng, shape, jnp.float32)
    if cuts:
        result = result * levels(rng, shape, cuts, -0.22, 0.18)
    return jnp.clip(result, -reach, reach).astype(kind)


def setup_inputs(seed: int = 0) -> dict:
    splits = jax.random.split(jax.random.key(seed), 5)
    frames = gaussian(splits[0], (SR, SC, NDET), 1.0, 6.0, ((0, 16), (1, 8)))
    offsets = with_ends(jax.random.randint(splits[1], (NDET, 2), 0 - MAXSHIFT, MAXSHIFT + 1), jax.random.fold_in(splits[1], 1), 0 - MAXSHIFT, MAXSHIFT).astype(jnp.int32)
    bright = draw_bright(jax.random.fold_in(splits[4], 71), 0)
    aberration = jnp.clip(jax.random.uniform(splits[3], (2,), jnp.float32, 0.5, 2.0), 0.5, 2.0)
    return {"frames": frames, "offsets": offsets, "bright": bright, "aberration": aberration}


TWO_PI = 2.0 * math.pi
EXACT_PRECISION = lax.Precision.HIGHEST

def phase_angles(first, second_operand, modulus):
    product = jnp.mod(first[:, None] * second_operand[None, :], modulus)
    return TWO_PI / modulus * product.astype(jnp.float32)

def signed_frequency(length):
    position = jnp.arange(length, dtype=jnp.int32)
    folded = jnp.where(position < length // 2, position, position - length)
    return 2.0 * folded.astype(jnp.float32) / length

def pixel_phase(pixel_index, shifts, aberration):
    freq_rows = signed_frequency(SR)[:, None, None]
    freq_cols = signed_frequency(SC)[None, :, None]
    half_rows = DROWS // 2
    half_cols = DCOLS // 2
    tilt_x = ((pixel_index // DCOLS - half_rows).astype(jnp.float32) / half_rows)[None, None, :]
    tilt_y = ((pixel_index % DCOLS - half_cols).astype(jnp.float32) / half_cols)[None, None, :]
    ramp_rows = jnp.mod(jnp.arange(SR, dtype=jnp.int32)[:, None] * shifts[:, 0][None, :], SR)
    ramp_cols = jnp.mod(jnp.arange(SC, dtype=jnp.int32)[:, None] * shifts[:, 1][None, :], SC)
    shift_phase = TWO_PI / SR * ramp_rows.astype(jnp.float32)[:, None, :] + TWO_PI / SC * ramp_cols.astype(jnp.float32)[None, :, :]
    tilt_sq = tilt_x * tilt_x + tilt_y * tilt_y
    tilt_dot = tilt_x * freq_rows + tilt_y * freq_cols
    moved_x = freq_rows + tilt_x
    moved_y = freq_cols + tilt_y
    moved_sq = moved_x * moved_x + moved_y * moved_y
    lens_phase = math.pi * (aberration[0] * (freq_rows * freq_rows + freq_cols * freq_cols) + aberration[1] * (moved_sq * moved_sq - tilt_sq * tilt_sq - 4.0 * tilt_sq * tilt_dot))
    return shift_phase - lens_phase

def window_weights(width):
    position = jnp.arange(width, dtype=jnp.int32)
    nearest = jnp.minimum(position, width - 1 - position)
    ramped = 0.3 + 0.35 * (1.0 - jnp.cos(math.pi * (nearest.astype(jnp.float32) + 0.5) / (2 * HALO)))
    return jnp.where(nearest < 2 * HALO, ramped, jnp.float32(1.0))

def inverse_transform(spec_real, spec_imag, columns, rows):
    col_angles = phase_angles(jnp.arange(SC, dtype=jnp.int32), columns, SC)
    cos_cols = jnp.cos(col_angles)
    sin_cols = jnp.sin(col_angles)
    real_piece = jnp.dot(spec_real, cos_cols, precision=EXACT_PRECISION) - jnp.dot(spec_imag, sin_cols, precision=EXACT_PRECISION)
    imaginary_piece = jnp.dot(spec_real, sin_cols, precision=EXACT_PRECISION) + jnp.dot(spec_imag, cos_cols, precision=EXACT_PRECISION)
    angles_by_row = phase_angles(jnp.arange(SR, dtype=jnp.int32), rows, SR)
    row_cosines = jnp.cos(angles_by_row)
    row_sines = jnp.sin(angles_by_row)
    return jnp.dot(row_cosines.T, real_piece, precision=EXACT_PRECISION) - jnp.dot(row_sines.T, imaginary_piece, precision=EXACT_PRECISION)

def reference(frames, offsets, bright, aberration):
    full_cols = jnp.arange(SC, dtype=jnp.int32)
    col_angles = phase_angles(full_cols, full_cols, SC)
    col_cos = lax.optimization_barrier(jnp.cos(col_angles).astype(jnp.bfloat16)).astype(jnp.float32)
    col_sin = lax.optimization_barrier(jnp.sin(col_angles).astype(jnp.bfloat16)).astype(jnp.float32)
    full_rows = jnp.arange(SR, dtype=jnp.int32)
    angles_by_row = phase_angles(full_rows, full_rows, SR)
    row_cos = jnp.cos(angles_by_row)
    row_sin = jnp.sin(angles_by_row)
    block = DCOLS * math.gcd(DROWS, 8)

    def add_block(carry, index):
        start = (index * block).astype(jnp.int32)
        piece = lax.dynamic_slice_in_dim(frames, start, block, 2).astype(jnp.float32)
        shifts = lax.dynamic_slice_in_dim(offsets, start, block, 0)
        weights = lax.dynamic_slice_in_dim(bright, start, block, 0).astype(jnp.float32)
        pixel_index = start + jnp.arange(block, dtype=jnp.int32)
        real_col = jnp.einsum('rcp,cq->rqp', piece, col_cos, precision=EXACT_PRECISION)
        imag_col = -jnp.einsum('rcp,cq->rqp', piece, col_sin, precision=EXACT_PRECISION)
        real_full = jnp.einsum('rs,rqp->sqp', row_cos, real_col, precision=EXACT_PRECISION) + jnp.einsum('rs,rqp->sqp', row_sin, imag_col, precision=EXACT_PRECISION)
        imag_full = jnp.einsum('rs,rqp->sqp', row_cos, imag_col, precision=EXACT_PRECISION) - jnp.einsum('rs,rqp->sqp', row_sin, real_col, precision=EXACT_PRECISION)
        phase = pixel_phase(pixel_index, shifts, aberration)
        turn_cos = jnp.cos(phase) * weights
        turn_sin = jnp.sin(phase) * weights
        spec_real = lax.optimization_barrier(jnp.sum(real_full * turn_cos - imag_full * turn_sin, axis=2))
        spec_imag = lax.optimization_barrier(jnp.sum(real_full * turn_sin + imag_full * turn_cos, axis=2))
        return ((carry[0] + spec_real, carry[1] + spec_imag), None)
    empty = jnp.zeros((SR, SC), jnp.float32)
    (spec_real, spec_imag), _ = lax.scan(add_block, (empty, empty), jnp.arange(NDET // block, dtype=jnp.int32))
    bright_sum = jnp.sum(bright.astype(jnp.float32))
    width = TILE + 2 * HALO
    tile_index = jnp.arange(N_SCAN, dtype=jnp.int32)
    columns = jnp.mod(tile_index[:, None] * TILE - HALO + jnp.arange(width, dtype=jnp.int32)[None, :], SC).reshape(-1)
    picture = inverse_transform(spec_real, spec_imag, columns, full_rows).reshape(SR, N_SCAN, width)
    return picture * (1.0 / (SR * SC)) / jnp.sqrt(bright_sum) * window_weights(width)[None, None, :]
```

```python
import math

import jax
import jax.numpy as jnp
from jax import lax
from jax.sharding import PartitionSpec as P

SR = 16
SC = 1024
DROWS = 128
DCOLS = 128
HALO = 16


TWO_PI = 2.0 * math.pi
EXACT_PRECISION = lax.Precision.HIGHEST


def phase_angles(first, second_operand, modulus):
    product = jnp.mod(first[:, None] * second_operand[None, :], modulus)
    return TWO_PI / modulus * product.astype(jnp.float32)


def signed_frequency(length):
    position = jnp.arange(length, dtype=jnp.int32)
    folded = jnp.where(position < length // 2, position, position - length)
    return 2.0 * folded.astype(jnp.float32) / length


def pixel_phase(pixel_index, shifts, aberration):
    freq_rows = signed_frequency(SR)[:, None, None]
    freq_cols = signed_frequency(SC)[None, :, None]
    half_rows = DROWS // 2
    half_cols = DCOLS // 2
    tilt_x = ((pixel_index // DCOLS - half_rows).astype(jnp.float32) / half_rows)[None, None, :]
    tilt_y = ((pixel_index % DCOLS - half_cols).astype(jnp.float32) / half_cols)[None, None, :]
    ramp_rows = jnp.mod(jnp.arange(SR, dtype=jnp.int32)[:, None] * shifts[:, 0][None, :], SR)
    ramp_cols = jnp.mod(jnp.arange(SC, dtype=jnp.int32)[:, None] * shifts[:, 1][None, :], SC)
    shift_phase = (
        TWO_PI / SR * ramp_rows.astype(jnp.float32)[:, None, :]
        + TWO_PI / SC * ramp_cols.astype(jnp.float32)[None, :, :]
    )
    tilt_sq = tilt_x * tilt_x + tilt_y * tilt_y
    tilt_dot = tilt_x * freq_rows + tilt_y * freq_cols
    moved_x = freq_rows + tilt_x
    moved_y = freq_cols + tilt_y
    moved_sq = moved_x * moved_x + moved_y * moved_y
    lens_phase = math.pi * (
        aberration[0] * (freq_rows * freq_rows + freq_cols * freq_cols)
        + aberration[1] * (moved_sq * moved_sq - tilt_sq * tilt_sq - 4.0 * tilt_sq * tilt_dot)
    )
    return shift_phase - lens_phase


def window_weights(width):
    position = jnp.arange(width, dtype=jnp.int32)
    nearest = jnp.minimum(position, width - 1 - position)
    ramped = 0.3 + 0.35 * (
        1.0 - jnp.cos(math.pi * (nearest.astype(jnp.float32) + 0.5) / (2 * HALO))
    )
    return jnp.where(nearest < 2 * HALO, ramped, jnp.float32(1.0))


def inverse_transform(spec_real, spec_imag, columns, rows):
    col_angles = phase_angles(jnp.arange(SC, dtype=jnp.int32), columns, SC)
    cos_cols = jnp.cos(col_angles)
    sin_cols = jnp.sin(col_angles)
    real_piece = jnp.dot(spec_real, cos_cols, precision=EXACT_PRECISION) - jnp.dot(
        spec_imag, sin_cols, precision=EXACT_PRECISION
    )
    imaginary_piece = jnp.dot(spec_real, sin_cols, precision=EXACT_PRECISION) + jnp.dot(
        spec_imag, cos_cols, precision=EXACT_PRECISION
    )
    angles_by_row = phase_angles(jnp.arange(SR, dtype=jnp.int32), rows, SR)
    row_cosines = jnp.cos(angles_by_row)
    row_sines = jnp.sin(angles_by_row)
    return jnp.dot(row_cosines.T, real_piece, precision=EXACT_PRECISION) - jnp.dot(
        row_sines.T, imaginary_piece, precision=EXACT_PRECISION
    )


def local(frames, offsets, bright, aberration):
    scan_size = lax.axis_size("scan")
    det_size = lax.axis_size("det")
    rows_dev, tile, detector = frames.shape
    owned = offsets.shape[0]
    groups = detector // owned
    owner = lax.axis_index("scan") * det_size + lax.axis_index("det")
    blocks = jnp.transpose(frames.reshape(rows_dev * tile, groups, owned), (1, 0, 2))
    arrived = lax.all_to_all(blocks, ("scan", "det"), split_axis=0, concat_axis=0, tiled=True)
    images = arrived.reshape(scan_size, det_size, rows_dev, tile, owned)
    full_cols = jnp.arange(SC, dtype=jnp.int32)
    col_angles = phase_angles(full_cols, full_cols, SC)
    col_cos = jnp.cos(col_angles).astype(jnp.bfloat16)
    col_sin = jnp.sin(col_angles).astype(jnp.bfloat16)
    table = jnp.concatenate([col_cos, -col_sin], axis=1).reshape(scan_size, tile, 2 * SC)
    both_col = jnp.einsum(
        "abrcp,acq->brqp", images, table, preferred_element_type=jnp.float32
    ).reshape(SR, 2 * SC, owned)
    real_col = both_col[:, :SC]
    imag_col = both_col[:, SC:]
    full_rows = jnp.arange(SR, dtype=jnp.int32)
    angles_by_row = phase_angles(full_rows, full_rows, SR)
    row_cos = jnp.cos(angles_by_row)
    row_sin = jnp.sin(angles_by_row)
    real_full = jnp.einsum(
        "rs,rqp->sqp", row_cos, real_col, precision=EXACT_PRECISION
    ) + jnp.einsum("rs,rqp->sqp", row_sin, imag_col, precision=EXACT_PRECISION)
    imag_full = jnp.einsum(
        "rs,rqp->sqp", row_cos, imag_col, precision=EXACT_PRECISION
    ) - jnp.einsum("rs,rqp->sqp", row_sin, real_col, precision=EXACT_PRECISION)
    pixel_index = owner * owned + jnp.arange(owned, dtype=jnp.int32)
    phase = pixel_phase(pixel_index, offsets, aberration)
    weights = bright.astype(jnp.float32)
    turn_cos = jnp.cos(phase) * weights
    turn_sin = jnp.sin(phase) * weights
    spec_real = jnp.sum(real_full * turn_cos - imag_full * turn_sin, axis=2)
    spec_imag = jnp.sum(real_full * turn_sin + imag_full * turn_cos, axis=2)
    packed = jnp.concatenate(
        [spec_real.reshape(-1), spec_imag.reshape(-1), jnp.sum(weights).reshape(1)]
    )
    total = lax.psum(packed, ("scan", "det"))
    spec_real = total[: SR * SC].reshape(SR, SC)
    spec_imag = total[SR * SC : 2 * SR * SC].reshape(SR, SC)
    bright_sum = total[2 * SR * SC]
    width = tile + 2 * HALO
    columns = jnp.mod(
        lax.axis_index("scan") * tile - HALO + jnp.arange(width, dtype=jnp.int32), SC
    )
    rows = lax.axis_index("det") * rows_dev + jnp.arange(rows_dev, dtype=jnp.int32)
    picture = inverse_transform(spec_real, spec_imag, columns, rows)
    return (
        (picture * (1.0 / (SR * SC)) / jnp.sqrt(bright_sum) * window_weights(width)[None, :])
        .reshape(rows_dev, 1, width)
    )


def solution(mesh):
    placed = (P("det", "scan", None), P(("scan", "det"), None), P(("scan", "det")), P())
    return jax.shard_map(
        local, mesh=mesh, in_specs=placed, out_specs=P("det", "scan", None), check_vma=False
    )
```

```python
import math

import jax
import jax.numpy as jnp
from jax import lax
from jax.sharding import PartitionSpec as P

SR = 16
SC = 1024
DROWS = 128
DCOLS = 128
HALO = 16


TWO_PI = 2.0 * math.pi
EXACT_PRECISION = lax.Precision.HIGHEST


def phase_angles(first, second_operand, modulus):
    product = jnp.mod(first[:, None] * second_operand[None, :], modulus)
    return TWO_PI / modulus * product.astype(jnp.float32)


def signed_frequency(length):
    position = jnp.arange(length, dtype=jnp.int32)
    folded = jnp.where(position < length // 2, position, position - length)
    return 2.0 * folded.astype(jnp.float32) / length


def pixel_phase(pixel_index, shifts, aberration):
    freq_rows = signed_frequency(SR)[:, None, None]
    freq_cols = signed_frequency(SC)[None, :, None]
    half_rows = DROWS // 2
    half_cols = DCOLS // 2
    tilt_x = ((pixel_index // DCOLS - half_rows).astype(jnp.float32) / half_rows)[None, None, :]
    tilt_y = ((pixel_index % DCOLS - half_cols).astype(jnp.float32) / half_cols)[None, None, :]
    ramp_rows = jnp.mod(jnp.arange(SR, dtype=jnp.int32)[:, None] * shifts[:, 0][None, :], SR)
    ramp_cols = jnp.mod(jnp.arange(SC, dtype=jnp.int32)[:, None] * shifts[:, 1][None, :], SC)
    shift_phase = (
        TWO_PI / SR * ramp_rows.astype(jnp.float32)[:, None, :]
        + TWO_PI / SC * ramp_cols.astype(jnp.float32)[None, :, :]
    )
    tilt_sq = tilt_x * tilt_x + tilt_y * tilt_y
    tilt_dot = tilt_x * freq_rows + tilt_y * freq_cols
    moved_x = freq_rows + tilt_x
    moved_y = freq_cols + tilt_y
    moved_sq = moved_x * moved_x + moved_y * moved_y
    lens_phase = math.pi * (
        aberration[0] * (freq_rows * freq_rows + freq_cols * freq_cols)
        + aberration[1] * (moved_sq * moved_sq - tilt_sq * tilt_sq - 4.0 * tilt_sq * tilt_dot)
    )
    return shift_phase - lens_phase


def window_weights(width):
    position = jnp.arange(width, dtype=jnp.int32)
    nearest = jnp.minimum(position, width - 1 - position)
    ramped = 0.3 + 0.35 * (
        1.0 - jnp.cos(math.pi * (nearest.astype(jnp.float32) + 0.5) / (2 * HALO))
    )
    return jnp.where(nearest < 2 * HALO, ramped, jnp.float32(1.0))


def inverse_transform(spec_real, spec_imag, columns, rows):
    col_angles = phase_angles(jnp.arange(SC, dtype=jnp.int32), columns, SC)
    cos_cols = jnp.cos(col_angles)
    sin_cols = jnp.sin(col_angles)
    real_piece = jnp.dot(spec_real, cos_cols, precision=EXACT_PRECISION) - jnp.dot(
        spec_imag, sin_cols, precision=EXACT_PRECISION
    )
    imaginary_piece = jnp.dot(spec_real, sin_cols, precision=EXACT_PRECISION) + jnp.dot(
        spec_imag, cos_cols, precision=EXACT_PRECISION
    )
    angles_by_row = phase_angles(jnp.arange(SR, dtype=jnp.int32), rows, SR)
    row_cosines = jnp.cos(angles_by_row)
    row_sines = jnp.sin(angles_by_row)
    return jnp.dot(row_cosines.T, real_piece, precision=EXACT_PRECISION) - jnp.dot(
        row_sines.T, imaginary_piece, precision=EXACT_PRECISION
    )


def butterfly_sum(values, axes, count):
    step = 1
    while step < count:
        values = values + lax.ppermute(values, axes, [(i, i ^ step) for i in range(count)])
        step *= 2
    return values


def local(frames, offsets, bright, aberration):
    scan_size = lax.axis_size("scan")
    det_size = lax.axis_size("det")
    rows_dev, tile, detector = frames.shape
    owned = offsets.shape[0]
    groups = detector // owned
    owner = lax.axis_index("scan") * det_size + lax.axis_index("det")
    blocks = jnp.transpose(frames.reshape(rows_dev * tile, groups, owned), (1, 0, 2))
    arrived = lax.all_to_all(blocks, ("scan", "det"), split_axis=0, concat_axis=0, tiled=True)
    images = arrived.reshape(scan_size, det_size, rows_dev, tile, owned)
    full_cols = jnp.arange(SC, dtype=jnp.int32)
    col_angles = phase_angles(full_cols, full_cols, SC)
    col_cos = jnp.cos(col_angles).astype(jnp.bfloat16)
    col_sin = jnp.sin(col_angles).astype(jnp.bfloat16)
    table = jnp.concatenate([col_cos, -col_sin], axis=1).reshape(scan_size, tile, 2 * SC)
    both_col = jnp.einsum(
        "abrcp,acq->brqp", images, table, preferred_element_type=jnp.float32
    ).reshape(SR, 2 * SC, owned)
    full_rows = jnp.arange(SR, dtype=jnp.int32)
    angles_by_row = phase_angles(full_rows, full_rows, SR)
    row_cos = jnp.cos(angles_by_row)
    row_sin = jnp.sin(angles_by_row)
    mix = jnp.stack(
        [jnp.stack([row_cos, -row_sin], axis=1), jnp.stack([row_sin, row_cos], axis=1)], axis=1
    )
    both_full = jnp.einsum(
        "rkqp,rkjs->jsqp",
        both_col.reshape(SR, 2, SC, owned),
        mix,
        precision=lax.Precision.HIGH,
        preferred_element_type=jnp.float32,
    )
    real_full = both_full[0]
    imag_full = both_full[1]
    pixel_index = owner * owned + jnp.arange(owned, dtype=jnp.int32)
    phase = pixel_phase(pixel_index, offsets, aberration)
    weights = bright.astype(jnp.float32)
    turn_cos = jnp.cos(phase) * weights
    turn_sin = jnp.sin(phase) * weights
    spec_real = jnp.sum(real_full * turn_cos - imag_full * turn_sin, axis=2)
    spec_imag = jnp.sum(real_full * turn_sin + imag_full * turn_cos, axis=2)
    packed = jnp.concatenate(
        [spec_real, spec_imag, jnp.broadcast_to(jnp.sum(weights), (1, SC))], axis=0
    )
    total = butterfly_sum(packed, ("scan", "det"), scan_size * det_size)
    spec_real = total[:SR]
    spec_imag = total[SR : 2 * SR]
    bright_sum = total[2 * SR, 0]
    width = tile + 2 * HALO
    columns = jnp.mod(
        lax.axis_index("scan") * tile - HALO + jnp.arange(width, dtype=jnp.int32), SC
    )
    rows = lax.axis_index("det") * rows_dev + jnp.arange(rows_dev, dtype=jnp.int32)
    picture = inverse_transform(spec_real, spec_imag, columns, rows)
    return (
        (picture * (1.0 / (SR * SC)) / jnp.sqrt(bright_sum) * window_weights(width)[None, :])
        .reshape(rows_dev, 1, width)
    )


def solution(mesh):
    placed = (P("det", "scan", None), P(("scan", "det"), None), P(("scan", "det")), P())
    return jax.shard_map(
        local, mesh=mesh, in_specs=placed, out_specs=P("det", "scan", None), check_vma=False
    )
```

```python
import math

import jax
import jax.numpy as jnp
from jax import lax
from jax.sharding import PartitionSpec as P

SR = 16
SC = 1024
DROWS = 128
DCOLS = 128
HALO = 16


TWO_PI = 2.0 * math.pi
EXACT_PRECISION = lax.Precision.HIGHEST


def phase_angles(first, second_operand, modulus):
    product = jnp.mod(first[:, None] * second_operand[None, :], modulus)
    return TWO_PI / modulus * product.astype(jnp.float32)


def signed_frequency(length):
    position = jnp.arange(length, dtype=jnp.int32)
    folded = jnp.where(position < length // 2, position, position - length)
    return 2.0 * folded.astype(jnp.float32) / length


def pixel_phase(pixel_index, shifts, aberration):
    freq_rows = signed_frequency(SR)[:, None, None]
    freq_cols = signed_frequency(SC)[None, :, None]
    half_rows = DROWS // 2
    half_cols = DCOLS // 2
    tilt_x = ((pixel_index // DCOLS - half_rows).astype(jnp.float32) / half_rows)[None, None, :]
    tilt_y = ((pixel_index % DCOLS - half_cols).astype(jnp.float32) / half_cols)[None, None, :]
    ramp_rows = jnp.mod(jnp.arange(SR, dtype=jnp.int32)[:, None] * shifts[:, 0][None, :], SR)
    ramp_cols = jnp.mod(jnp.arange(SC, dtype=jnp.int32)[:, None] * shifts[:, 1][None, :], SC)
    shift_phase = (
        TWO_PI / SR * ramp_rows.astype(jnp.float32)[:, None, :]
        + TWO_PI / SC * ramp_cols.astype(jnp.float32)[None, :, :]
    )
    tilt_sq = tilt_x * tilt_x + tilt_y * tilt_y
    tilt_dot = tilt_x * freq_rows + tilt_y * freq_cols
    moved_x = freq_rows + tilt_x
    moved_y = freq_cols + tilt_y
    moved_sq = moved_x * moved_x + moved_y * moved_y
    lens_phase = math.pi * (
        aberration[0] * (freq_rows * freq_rows + freq_cols * freq_cols)
        + aberration[1] * (moved_sq * moved_sq - tilt_sq * tilt_sq - 4.0 * tilt_sq * tilt_dot)
    )
    return shift_phase - lens_phase


def window_weights(width):
    position = jnp.arange(width, dtype=jnp.int32)
    nearest = jnp.minimum(position, width - 1 - position)
    ramped = 0.3 + 0.35 * (
        1.0 - jnp.cos(math.pi * (nearest.astype(jnp.float32) + 0.5) / (2 * HALO))
    )
    return jnp.where(nearest < 2 * HALO, ramped, jnp.float32(1.0))


def inverse_transform(spec_real, spec_imag, columns, rows):
    col_angles = phase_angles(jnp.arange(SC, dtype=jnp.int32), columns, SC)
    cos_cols = jnp.cos(col_angles)
    sin_cols = jnp.sin(col_angles)
    real_piece = jnp.dot(spec_real, cos_cols, precision=EXACT_PRECISION) - jnp.dot(
        spec_imag, sin_cols, precision=EXACT_PRECISION
    )
    imaginary_piece = jnp.dot(spec_real, sin_cols, precision=EXACT_PRECISION) + jnp.dot(
        spec_imag, cos_cols, precision=EXACT_PRECISION
    )
    angles_by_row = phase_angles(jnp.arange(SR, dtype=jnp.int32), rows, SR)
    row_cosines = jnp.cos(angles_by_row)
    row_sines = jnp.sin(angles_by_row)
    return jnp.dot(row_cosines.T, real_piece, precision=EXACT_PRECISION) - jnp.dot(
        row_sines.T, imaginary_piece, precision=EXACT_PRECISION
    )


def butterfly_sum(values, axes, count, bit_groups):
    for low, bits in bit_groups:
        partners = [values] + [
            lax.ppermute(values, axes, [(i, i ^ (d << low)) for i in range(count)])
            for d in range(1, 1 << bits)
        ]
        while len(partners) > 1:
            partners = [partners[e] + partners[e + 1] for e in range(0, len(partners), 2)]
        values = partners[0]
    return values


def sincos(angle):
    turns = jnp.round(angle * (2.0 / math.pi))
    quadrant = turns.astype(jnp.int32) & 3
    rest = angle - turns * 1.5703125
    rest = rest - turns * 4.837512969970703125e-4
    rest = rest - turns * 7.54978995489188216e-8
    square = rest * rest
    sine = rest + rest * square * (
        -1.6666654611e-1 + square * (8.3321608736e-3 + square * -1.9515295891e-4)
    )
    cosine = 1.0 - 0.5 * square + square * square * (
        4.166664568298827e-2 + square * (-1.388731625493765e-3 + square * 2.443315711809948e-5)
    )
    swap = (quadrant & 1) == 1
    sin_out = jnp.where(swap, cosine, sine)
    cos_out = jnp.where(swap, sine, cosine)
    sin_out = jnp.where(quadrant >= 2, -sin_out, sin_out)
    cos_out = jnp.where((quadrant == 1) | (quadrant == 2), -cos_out, cos_out)
    return sin_out, cos_out


def phase_parts(pixel_index, shifts, aberration):
    freq_rows = signed_frequency(SR)[:, None]
    freq_cols = signed_frequency(SC)[:, None]
    half_rows = DROWS // 2
    half_cols = DCOLS // 2
    tilt_x = ((pixel_index // DCOLS - half_rows).astype(jnp.float32) / half_rows)[None, :]
    tilt_y = ((pixel_index % DCOLS - half_cols).astype(jnp.float32) / half_cols)[None, :]
    ramp_rows = jnp.mod(jnp.arange(SR, dtype=jnp.int32)[:, None] * shifts[:, 0][None, :], SR)
    ramp_cols = jnp.mod(jnp.arange(SC, dtype=jnp.int32)[:, None] * shifts[:, 1][None, :], SC)
    tilt_sq = tilt_x * tilt_x + tilt_y * tilt_y
    defocus = math.pi * aberration[0]
    spherical = math.pi * aberration[1]
    row_part = (
        TWO_PI / SR * ramp_rows.astype(jnp.float32)
        - defocus * freq_rows * freq_rows
        + spherical * (tilt_sq * tilt_sq + 4.0 * tilt_sq * tilt_x * freq_rows)
    )
    col_part = (
        TWO_PI / SC * ramp_cols.astype(jnp.float32)
        - defocus * freq_cols * freq_cols
        + spherical * (4.0 * tilt_sq * tilt_y * freq_cols)
    )
    moved_rows = (freq_rows + tilt_x) * (freq_rows + tilt_x)
    moved_cols = (freq_cols + tilt_y) * (freq_cols + tilt_y)
    return row_part, col_part, moved_rows, moved_cols, spherical


def local(frames, offsets, bright, aberration):
    scan_size = lax.axis_size("scan")
    det_size = lax.axis_size("det")
    rows_dev, tile, detector = frames.shape
    owned = offsets.shape[0]
    groups = detector // owned
    owner = lax.axis_index("scan") * det_size + lax.axis_index("det")
    blocks = jnp.transpose(frames.reshape(rows_dev * tile, groups, owned), (1, 0, 2))
    arrived = lax.all_to_all(blocks, ("scan", "det"), split_axis=0, concat_axis=0, tiled=True)
    images = arrived.reshape(scan_size, det_size, rows_dev, tile, owned)
    full_cols = jnp.arange(SC, dtype=jnp.int32)
    col_angles = phase_angles(full_cols, full_cols, SC)
    col_cos = jnp.cos(col_angles).astype(jnp.bfloat16)
    col_sin = jnp.sin(col_angles).astype(jnp.bfloat16)
    table = jnp.concatenate([col_cos, -col_sin], axis=1).reshape(scan_size, tile, 2 * SC)
    both_col = jnp.einsum(
        "abrcp,acq->brqp", images, table, preferred_element_type=jnp.float32
    ).reshape(SR, 2 * SC, owned)
    full_rows = jnp.arange(SR, dtype=jnp.int32)
    angles_by_row = phase_angles(full_rows, full_rows, SR)
    row_cos = jnp.cos(angles_by_row)
    row_sin = jnp.sin(angles_by_row)
    mix = jnp.stack(
        [jnp.stack([row_cos, -row_sin], axis=1), jnp.stack([row_sin, row_cos], axis=1)], axis=1
    )
    both_full = jnp.einsum(
        "rkqp,rkjs->jsqp",
        both_col.reshape(SR, 2, SC, owned),
        mix,
        precision=lax.Precision.HIGH,
        preferred_element_type=jnp.float32,
    )
    real_full = both_full[0]
    imag_full = both_full[1]
    pixel_index = owner * owned + jnp.arange(owned, dtype=jnp.int32)
    row_part, col_part, moved_rows, moved_cols, spherical = phase_parts(
        pixel_index, offsets, aberration
    )
    moved_sq = moved_rows[:, None, :] + moved_cols[None, :, :]
    phase = row_part[:, None, :] + col_part[None, :, :] - spherical * (moved_sq * moved_sq)
    weights = bright.astype(jnp.float32)
    turn_sin, turn_cos = sincos(phase)
    spec_real = jnp.sum((real_full * turn_cos - imag_full * turn_sin) * weights, axis=2)
    spec_imag = jnp.sum((real_full * turn_sin + imag_full * turn_cos) * weights, axis=2)
    packed = jnp.concatenate(
        [spec_real, spec_imag, jnp.broadcast_to(jnp.sum(weights), (1, SC))], axis=0
    )
    total = butterfly_sum(
        packed, ("scan", "det"), scan_size * det_size, ((0, 2), (2, 2), (4, 3))
    )
    spec_real = total[:SR]
    spec_imag = total[SR : 2 * SR]
    bright_sum = total[2 * SR, 0]
    width = tile + 2 * HALO
    columns = jnp.mod(
        lax.axis_index("scan") * tile - HALO + jnp.arange(width, dtype=jnp.int32), SC
    )
    rows = lax.axis_index("det") * rows_dev + jnp.arange(rows_dev, dtype=jnp.int32)
    picture = inverse_transform(spec_real, spec_imag, columns, rows)
    return (
        (picture * (1.0 / (SR * SC)) / jnp.sqrt(bright_sum) * window_weights(width)[None, :])
        .reshape(rows_dev, 1, width)
    )


def solution(mesh):
    placed = (P("det", "scan", None), P(("scan", "det"), None), P(("scan", "det")), P())
    return jax.shard_map(
        local, mesh=mesh, in_specs=placed, out_specs=P("det", "scan", None), check_vma=False
    )
```

```python
import math

import jax
import jax.numpy as jnp
from jax import lax
from jax.sharding import PartitionSpec as P

SR = 16
SC = 1024
DROWS = 128
DCOLS = 128
HALO = 16


TWO_PI = 2.0 * math.pi
EXACT_PRECISION = lax.Precision.HIGHEST


def phase_angles(first, second_operand, modulus):
    product = jnp.mod(first[:, None] * second_operand[None, :], modulus)
    return TWO_PI / modulus * product.astype(jnp.float32)


def signed_frequency(length):
    position = jnp.arange(length, dtype=jnp.int32)
    folded = jnp.where(position < length // 2, position, position - length)
    return 2.0 * folded.astype(jnp.float32) / length


def pixel_phase(pixel_index, shifts, aberration):
    freq_rows = signed_frequency(SR)[:, None, None]
    freq_cols = signed_frequency(SC)[None, :, None]
    half_rows = DROWS // 2
    half_cols = DCOLS // 2
    tilt_x = ((pixel_index // DCOLS - half_rows).astype(jnp.float32) / half_rows)[None, None, :]
    tilt_y = ((pixel_index % DCOLS - half_cols).astype(jnp.float32) / half_cols)[None, None, :]
    ramp_rows = jnp.mod(jnp.arange(SR, dtype=jnp.int32)[:, None] * shifts[:, 0][None, :], SR)
    ramp_cols = jnp.mod(jnp.arange(SC, dtype=jnp.int32)[:, None] * shifts[:, 1][None, :], SC)
    shift_phase = (
        TWO_PI / SR * ramp_rows.astype(jnp.float32)[:, None, :]
        + TWO_PI / SC * ramp_cols.astype(jnp.float32)[None, :, :]
    )
    tilt_sq = tilt_x * tilt_x + tilt_y * tilt_y
    tilt_dot = tilt_x * freq_rows + tilt_y * freq_cols
    moved_x = freq_rows + tilt_x
    moved_y = freq_cols + tilt_y
    moved_sq = moved_x * moved_x + moved_y * moved_y
    lens_phase = math.pi * (
        aberration[0] * (freq_rows * freq_rows + freq_cols * freq_cols)
        + aberration[1] * (moved_sq * moved_sq - tilt_sq * tilt_sq - 4.0 * tilt_sq * tilt_dot)
    )
    return shift_phase - lens_phase


def window_weights(width):
    position = jnp.arange(width, dtype=jnp.int32)
    nearest = jnp.minimum(position, width - 1 - position)
    ramped = 0.3 + 0.35 * (
        1.0 - jnp.cos(math.pi * (nearest.astype(jnp.float32) + 0.5) / (2 * HALO))
    )
    return jnp.where(nearest < 2 * HALO, ramped, jnp.float32(1.0))


def inverse_transform(spec_real, spec_imag, columns, rows):
    col_angles = phase_angles(jnp.arange(SC, dtype=jnp.int32), columns, SC)
    cos_cols = jnp.cos(col_angles)
    sin_cols = jnp.sin(col_angles)
    real_piece = jnp.dot(spec_real, cos_cols, precision=EXACT_PRECISION) - jnp.dot(
        spec_imag, sin_cols, precision=EXACT_PRECISION
    )
    imaginary_piece = jnp.dot(spec_real, sin_cols, precision=EXACT_PRECISION) + jnp.dot(
        spec_imag, cos_cols, precision=EXACT_PRECISION
    )
    angles_by_row = phase_angles(jnp.arange(SR, dtype=jnp.int32), rows, SR)
    row_cosines = jnp.cos(angles_by_row)
    row_sines = jnp.sin(angles_by_row)
    return jnp.dot(row_cosines.T, real_piece, precision=EXACT_PRECISION) - jnp.dot(
        row_sines.T, imaginary_piece, precision=EXACT_PRECISION
    )


def sincos_reduced(rest, quadrant):
    square = rest * rest
    sine = rest + rest * square * (
        -1.6666654611e-1 + square * (8.3321608736e-3 + square * -1.9515295891e-4)
    )
    cosine = 1.0 - 0.5 * square + square * square * (
        4.166664568298827e-2 + square * (-1.388731625493765e-3 + square * 2.443315711809948e-5)
    )
    swap = (quadrant & 1) == 1
    sin_out = jnp.where(swap, cosine, sine)
    cos_out = jnp.where(swap, sine, cosine)
    sin_out = jnp.where(quadrant >= 2, -sin_out, sin_out)
    cos_out = jnp.where((quadrant == 1) | (quadrant == 2), -cos_out, cos_out)
    return sin_out, cos_out


def sincos(angle):
    turns = jnp.round(angle * (2.0 / math.pi))
    quadrant = turns.astype(jnp.int32) & 3
    rest = angle - turns * 1.5703125
    rest = rest - turns * 4.837512969970703125e-4
    rest = rest - turns * 7.54978995489188216e-8
    return sincos_reduced(rest, quadrant)


def sincos_of_steps(steps, modulus):
    quarter = modulus // 4
    turns = (steps + quarter // 2) // quarter
    rest = (steps - turns * quarter).astype(jnp.float32) * (TWO_PI / modulus)
    return sincos_reduced(rest, turns & 3)


def exchange(values, axes, count, low, bits, rows):
    digit = (lax.axis_index(axes) >> low) & ((1 << bits) - 1)
    kept = lax.dynamic_index_in_dim(rows(values), digit, axis=1, keepdims=False)
    for d in range(1, 1 << bits):
        sent = lax.dynamic_index_in_dim(rows(values), digit ^ d, axis=1, keepdims=False)
        kept = kept + lax.ppermute(sent, axes, [(i, i ^ (d << low)) for i in range(count)])
    return kept


def phase_parts(pixel_index, shifts, aberration):
    freq_rows = signed_frequency(SR)[:, None]
    freq_cols = signed_frequency(SC)[:, None]
    half_rows = DROWS // 2
    half_cols = DCOLS // 2
    tilt_x = ((pixel_index // DCOLS - half_rows).astype(jnp.float32) / half_rows)[None, :]
    tilt_y = ((pixel_index % DCOLS - half_cols).astype(jnp.float32) / half_cols)[None, :]
    ramp_rows = jnp.mod(jnp.arange(SR, dtype=jnp.int32)[:, None] * shifts[:, 0][None, :], SR)
    ramp_cols = jnp.mod(jnp.arange(SC, dtype=jnp.int32)[:, None] * shifts[:, 1][None, :], SC)
    tilt_sq = tilt_x * tilt_x + tilt_y * tilt_y
    defocus = math.pi * aberration[0]
    spherical = math.pi * aberration[1]
    row_part = (
        TWO_PI / SR * ramp_rows.astype(jnp.float32)
        - defocus * freq_rows * freq_rows
        + spherical * (tilt_sq * tilt_sq + 4.0 * tilt_sq * tilt_x * freq_rows)
    )
    col_part = (
        TWO_PI / SC * ramp_cols.astype(jnp.float32)
        - defocus * freq_cols * freq_cols
        + spherical * (4.0 * tilt_sq * tilt_y * freq_cols)
    )
    moved_rows = (freq_rows + tilt_x) * (freq_rows + tilt_x)
    moved_cols = (freq_cols + tilt_y) * (freq_cols + tilt_y)
    return row_part, col_part, moved_rows, moved_cols, spherical


def local(frames, offsets, bright, aberration):
    scan_size = lax.axis_size("scan")
    det_size = lax.axis_size("det")
    rows_dev, tile, detector = frames.shape
    owned = offsets.shape[0]
    groups = detector // owned
    owner = lax.axis_index("scan") * det_size + lax.axis_index("det")
    blocks = jnp.transpose(frames.reshape(rows_dev * tile, groups, owned), (1, 0, 2))
    arrived = lax.all_to_all(blocks, ("scan", "det"), split_axis=0, concat_axis=0, tiled=True)
    images = arrived.reshape(scan_size, det_size, rows_dev, tile, owned)
    full_cols = jnp.arange(SC, dtype=jnp.int32)
    col_sin, col_cos = sincos_of_steps(jnp.mod(full_cols[:, None] * full_cols[None, :], SC), SC)
    col_cos = col_cos.astype(jnp.bfloat16)
    col_sin = col_sin.astype(jnp.bfloat16)
    table = jnp.concatenate([col_cos, -col_sin], axis=1).reshape(scan_size, tile, 2 * SC)
    both_col = jnp.einsum(
        "abrcp,acq->brqp", images, table, preferred_element_type=jnp.float32
    ).reshape(SR, 2 * SC, owned)
    full_rows = jnp.arange(SR, dtype=jnp.int32)
    angles_by_row = phase_angles(full_rows, full_rows, SR)
    row_cos = jnp.cos(angles_by_row)
    row_sin = jnp.sin(angles_by_row)
    mix = jnp.stack(
        [jnp.stack([row_cos, -row_sin], axis=1), jnp.stack([row_sin, row_cos], axis=1)], axis=1
    )
    both_full = jnp.einsum(
        "rkqp,rkjs->jsqp",
        both_col.reshape(SR, 2, SC, owned),
        mix,
        precision=lax.Precision.HIGH,
        preferred_element_type=jnp.float32,
    )
    real_full = both_full[0]
    imag_full = both_full[1]
    pixel_index = owner * owned + jnp.arange(owned, dtype=jnp.int32)
    row_part, col_part, moved_rows, moved_cols, spherical = phase_parts(
        pixel_index, offsets, aberration
    )
    moved_sq = moved_rows[:, None, :] + moved_cols[None, :, :]
    phase = row_part[:, None, :] + col_part[None, :, :] - spherical * (moved_sq * moved_sq)
    weights = bright.astype(jnp.float32)
    turn_sin, turn_cos = sincos(phase)
    turn_cos, turn_sin = lax.optimization_barrier((turn_cos * weights, turn_sin * weights))
    spec_real = jnp.sum(real_full * turn_cos - imag_full * turn_sin, axis=2)
    spec_imag = jnp.sum(real_full * turn_sin + imag_full * turn_cos, axis=2)
    row_cos_t = row_cos.T
    row_sin_t = row_sin.T
    rows_real = jnp.dot(row_cos_t, spec_real, precision=EXACT_PRECISION) - jnp.dot(
        row_sin_t, spec_imag, precision=EXACT_PRECISION
    )
    rows_imag = jnp.dot(row_sin_t, spec_real, precision=EXACT_PRECISION) + jnp.dot(
        row_cos_t, spec_imag, precision=EXACT_PRECISION
    )
    packed = jnp.concatenate(
        [rows_real, rows_imag, jnp.broadcast_to(jnp.sum(weights), (SR, 128))], axis=1
    )
    axes = ("scan", "det")
    count = scan_size * det_size
    quarters = packed.reshape(4, 4, packed.shape[1])
    partial = exchange(quarters, axes, count, 0, 2, lambda x: x)
    own = exchange(partial, axes, count, 2, 2, lambda x: x.reshape(1, 4, x.shape[1]))
    own = own.reshape(-1)
    partners = [own] + [
        lax.ppermute(own, axes, [(i, i ^ (d << 4)) for i in range(count)]) for d in range(1, 8)
    ]
    while len(partners) > 1:
        partners = [partners[e] + partners[e + 1] for e in range(0, len(partners), 2)]
    total = partners[0]
    line_real = total[:SC]
    line_imag = total[SC : 2 * SC]
    bright_sum = total[2 * SC]
    width = tile + 2 * HALO
    columns = jnp.mod(
        lax.axis_index("scan") * tile - HALO + jnp.arange(width, dtype=jnp.int32), SC
    )
    col_angles = phase_angles(jnp.arange(SC, dtype=jnp.int32), columns, SC)
    cos_cols = jnp.cos(col_angles)
    sin_cols = jnp.sin(col_angles)
    picture = jnp.dot(line_real, cos_cols, precision=EXACT_PRECISION) - jnp.dot(
        line_imag, sin_cols, precision=EXACT_PRECISION
    )
    return (
        (picture * (1.0 / (SR * SC)) / jnp.sqrt(bright_sum) * window_weights(width))
        .reshape(rows_dev, 1, width)
    )


def solution(mesh):
    placed = (P("det", "scan", None), P(("scan", "det"), None), P(("scan", "det")), P())
    return jax.shard_map(
        local, mesh=mesh, in_specs=placed, out_specs=P("det", "scan", None), check_vma=False
    )
```

```python
import math

import jax
import jax.numpy as jnp
from jax import lax
from jax.sharding import PartitionSpec as P
from jax.experimental import pallas as pl

SR = 16
SC = 1024
DROWS = 128
DCOLS = 128
HALO = 16


TWO_PI = 2.0 * math.pi
EXACT_PRECISION = lax.Precision.HIGHEST


def phase_angles(first, second_operand, modulus):
    product = jnp.mod(first[:, None] * second_operand[None, :], modulus)
    return TWO_PI / modulus * product.astype(jnp.float32)


def signed_frequency(length):
    position = jnp.arange(length, dtype=jnp.int32)
    folded = jnp.where(position < length // 2, position, position - length)
    return 2.0 * folded.astype(jnp.float32) / length


def pixel_phase(pixel_index, shifts, aberration):
    freq_rows = signed_frequency(SR)[:, None, None]
    freq_cols = signed_frequency(SC)[None, :, None]
    half_rows = DROWS // 2
    half_cols = DCOLS // 2
    tilt_x = ((pixel_index // DCOLS - half_rows).astype(jnp.float32) / half_rows)[None, None, :]
    tilt_y = ((pixel_index % DCOLS - half_cols).astype(jnp.float32) / half_cols)[None, None, :]
    ramp_rows = jnp.mod(jnp.arange(SR, dtype=jnp.int32)[:, None] * shifts[:, 0][None, :], SR)
    ramp_cols = jnp.mod(jnp.arange(SC, dtype=jnp.int32)[:, None] * shifts[:, 1][None, :], SC)
    shift_phase = (
        TWO_PI / SR * ramp_rows.astype(jnp.float32)[:, None, :]
        + TWO_PI / SC * ramp_cols.astype(jnp.float32)[None, :, :]
    )
    tilt_sq = tilt_x * tilt_x + tilt_y * tilt_y
    tilt_dot = tilt_x * freq_rows + tilt_y * freq_cols
    moved_x = freq_rows + tilt_x
    moved_y = freq_cols + tilt_y
    moved_sq = moved_x * moved_x + moved_y * moved_y
    lens_phase = math.pi * (
        aberration[0] * (freq_rows * freq_rows + freq_cols * freq_cols)
        + aberration[1] * (moved_sq * moved_sq - tilt_sq * tilt_sq - 4.0 * tilt_sq * tilt_dot)
    )
    return shift_phase - lens_phase


def window_weights(width):
    position = jnp.arange(width, dtype=jnp.int32)
    nearest = jnp.minimum(position, width - 1 - position)
    ramped = 0.3 + 0.35 * (
        1.0 - jnp.cos(math.pi * (nearest.astype(jnp.float32) + 0.5) / (2 * HALO))
    )
    return jnp.where(nearest < 2 * HALO, ramped, jnp.float32(1.0))


def inverse_transform(spec_real, spec_imag, columns, rows):
    real_piece = jnp.dot(spec_real, cos_cols, precision=EXACT_PRECISION) - jnp.dot(
        spec_imag, sin_cols, precision=EXACT_PRECISION
    )
    imaginary_piece = jnp.dot(spec_real, sin_cols, precision=EXACT_PRECISION) + jnp.dot(
        spec_imag, cos_cols, precision=EXACT_PRECISION
    )
    angles_by_row = phase_angles(jnp.arange(SR, dtype=jnp.int32), rows, SR)
    row_cosines = jnp.cos(angles_by_row)
    row_sines = jnp.sin(angles_by_row)
    return jnp.dot(row_cosines.T, real_piece, precision=EXACT_PRECISION) - jnp.dot(
        row_sines.T, imaginary_piece, precision=EXACT_PRECISION
    )


def sincos_reduced(rest, quadrant):
    square = rest * rest
    sine = rest + rest * square * (
        -1.6666654611e-1 + square * (8.3321608736e-3 + square * -1.9515295891e-4)
    )
    cosine = 1.0 - 0.5 * square + square * square * (
        4.166664568298827e-2 + square * (-1.388731625493765e-3 + square * 2.443315711809948e-5)
    )
    swap = (quadrant & 1) == 1
    sin_out = jnp.where(swap, cosine, sine)
    cos_out = jnp.where(swap, sine, cosine)
    sin_out = jnp.where(quadrant >= 2, -sin_out, sin_out)
    cos_out = jnp.where((quadrant == 1) | (quadrant == 2), -cos_out, cos_out)
    return sin_out, cos_out


def sincos(angle):
    turns = jnp.round(angle * (2.0 / math.pi))
    quadrant = turns.astype(jnp.int32) & 3
    rest = angle - turns * 1.5703125
    rest = rest - turns * 4.837512969970703125e-4
    rest = rest - turns * 7.54978995489188216e-8
    return sincos_reduced(rest, quadrant)


def sincos_of_steps(steps, modulus):
    quarter = modulus // 4
    turns = (steps + quarter // 2) // quarter
    rest = (steps - turns * quarter).astype(jnp.float32) * (TWO_PI / modulus)
    return sincos_reduced(rest, turns & 3)


def exchange(values, axes, count, low, bits, rows):
    digit = (lax.axis_index(axes) >> low) & ((1 << bits) - 1)
    kept = lax.dynamic_index_in_dim(rows(values), digit, axis=1, keepdims=False)
    for d in range(1, 1 << bits):
        sent = lax.dynamic_index_in_dim(rows(values), digit ^ d, axis=1, keepdims=False)
        kept = kept + lax.ppermute(sent, axes, [(i, i ^ (d << low)) for i in range(count)])
    return kept


def phase_parts(pixel_index, shifts, aberration):
    freq_rows = signed_frequency(SR)[:, None]
    freq_cols = signed_frequency(SC)[:, None]
    half_rows = DROWS // 2
    half_cols = DCOLS // 2
    tilt_x = ((pixel_index // DCOLS - half_rows).astype(jnp.float32) / half_rows)[None, :]
    tilt_y = ((pixel_index % DCOLS - half_cols).astype(jnp.float32) / half_cols)[None, :]
    ramp_rows = jnp.mod(jnp.arange(SR, dtype=jnp.int32)[:, None] * shifts[:, 0][None, :], SR)
    ramp_cols = jnp.mod(jnp.arange(SC, dtype=jnp.int32)[:, None] * shifts[:, 1][None, :], SC)
    tilt_sq = tilt_x * tilt_x + tilt_y * tilt_y
    defocus = math.pi * aberration[0]
    spherical = math.pi * aberration[1]
    row_part = (
        TWO_PI / SR * ramp_rows.astype(jnp.float32)
        - defocus * freq_rows * freq_rows
        + spherical * (tilt_sq * tilt_sq + 4.0 * tilt_sq * tilt_x * freq_rows)
    )
    col_part = (
        TWO_PI / SC * ramp_cols.astype(jnp.float32)
        - defocus * freq_cols * freq_cols
        + spherical * (4.0 * tilt_sq * tilt_y * freq_cols)
    )
    moved_rows = (freq_rows + tilt_x) * (freq_rows + tilt_x)
    moved_cols = (freq_cols + tilt_y) * (freq_cols + tilt_y)
    return row_part, col_part, moved_rows, moved_cols, spherical


def four_point(points):
    (ar, ai), (br, bi), (cr, ci), (dr, di) = points
    s02r = ar + cr
    s02i = ai + ci
    d02r = ar - cr
    d02i = ai - ci
    s13r = br + dr
    s13i = bi + di
    d13r = br - dr
    d13i = bi - di
    return [
        (s02r + s13r, s02i + s13i),
        (d02r + d13i, d02i - d13r),
        (s02r - s13r, s02i - s13i),
        (d02r - d13i, d02i + d13r),
    ]


def fft16(points):
    twisted = {}
    for b in range(4):
        column = four_point([points[4 * a + b] for a in range(4)])
        for s1, (gr, gi) in enumerate(column):
            k = b * s1
            if k == 0:
                twisted[b, s1] = (gr, gi)
            elif k == 4:
                twisted[b, s1] = (gi, -gr)
            else:
                c = math.cos(TWO_PI * k / 16)
                d = math.sin(TWO_PI * k / 16)
                twisted[b, s1] = (gr * c + gi * d, gi * c - gr * d)
    out = [None] * 16
    for s1 in range(4):
        row = four_point([twisted[b, s1] for b in range(4)])
        for s2 in range(4):
            out[s1 + 4 * s2] = row[s2]
    return out


def spectrum_kernel(re_ref, im_ref, tc_ref, ts_ref, out_ref):
    out_ref[...] = jnp.zeros(out_ref.shape, out_ref.dtype)

    def body(i, carry):
        rows = pl.ds(pl.multiple_of(i * 8, 8), 8)
        full = fft16([(re_ref[r, rows, :], im_ref[r, rows, :]) for r in range(SR)])
        for s in range(SR):
            fr, fi = full[s]
            tc = tc_ref[s, rows, :]
            ts = ts_ref[s, rows, :]
            out_ref[0, s] += fr * tc - fi * ts
            out_ref[1, s] += fr * ts + fi * tc
        return carry

    lax.fori_loop(0, re_ref.shape[1] // 8, body, 0)


def spectrum(both_col, turn_cos, turn_sin):
    pixels = both_col.shape[1]
    block = 128
    steps = SC // block
    spec = pl.pallas_call(
        spectrum_kernel,
        grid=(steps,),
        in_specs=[
            pl.BlockSpec((SR, pixels, block), lambda j: (0, 0, j)),
            pl.BlockSpec((SR, pixels, block), lambda j: (0, 0, j + steps)),
            pl.BlockSpec((SR, pixels, block), lambda j: (0, 0, j)),
            pl.BlockSpec((SR, pixels, block), lambda j: (0, 0, j)),
        ],
        out_specs=pl.BlockSpec((2, SR, 8, block), lambda j: (0, 0, 0, j)),
        out_shape=jax.ShapeDtypeStruct((2, SR, 8, SC), jnp.float32),
    )(both_col, both_col, turn_cos, turn_sin)
    return jnp.sum(spec, axis=2)


def local(frames, offsets, bright, aberration):
    scan_size = lax.axis_size("scan")
    det_size = lax.axis_size("det")
    rows_dev, tile, detector = frames.shape
    owned = offsets.shape[0]
    groups = detector // owned
    owner = lax.axis_index("scan") * det_size + lax.axis_index("det")
    blocks = jnp.transpose(frames.reshape(rows_dev * tile, groups, owned), (1, 0, 2))
    arrived = lax.all_to_all(blocks, ("scan", "det"), split_axis=0, concat_axis=0, tiled=True)
    images = arrived.reshape(scan_size, det_size, rows_dev, tile, owned)
    full_cols = jnp.arange(SC, dtype=jnp.int32)
    col_sin, col_cos = sincos_of_steps(jnp.mod(full_cols[:, None] * full_cols[None, :], SC), SC)
    col_cos = col_cos.astype(jnp.bfloat16)
    col_sin = col_sin.astype(jnp.bfloat16)
    table = jnp.concatenate([col_cos, -col_sin], axis=1).reshape(scan_size, tile, 2 * SC)
    both_col = jnp.einsum(
        "abrcp,acq->brpq", images, table, preferred_element_type=jnp.float32
    ).reshape(SR, owned, 2 * SC)
    full_rows = jnp.arange(SR, dtype=jnp.int32)
    angles_by_row = phase_angles(full_rows, full_rows, SR)
    row_cos = jnp.cos(angles_by_row)
    row_sin = jnp.sin(angles_by_row)
    pixel_index = owner * owned + jnp.arange(owned, dtype=jnp.int32)
    row_part, col_part, moved_rows, moved_cols, spherical = phase_parts(
        pixel_index, offsets, aberration
    )
    moved_sq = moved_rows[:, :, None] + moved_cols.T[None, :, :]
    phase = row_part[:, :, None] + col_part.T[None, :, :] - spherical * (moved_sq * moved_sq)
    weights = bright.astype(jnp.float32)
    turn_sin, turn_cos = sincos(phase)
    turn_cos, turn_sin = lax.optimization_barrier(
        (turn_cos * weights[None, :, None], turn_sin * weights[None, :, None])
    )
    spec_real, spec_imag = spectrum(both_col, turn_cos, turn_sin)
    row_cos_t = row_cos.T
    row_sin_t = row_sin.T
    rows_real = jnp.dot(row_cos_t, spec_real, precision=EXACT_PRECISION) - jnp.dot(
        row_sin_t, spec_imag, precision=EXACT_PRECISION
    )
    rows_imag = jnp.dot(row_sin_t, spec_real, precision=EXACT_PRECISION) + jnp.dot(
        row_cos_t, spec_imag, precision=EXACT_PRECISION
    )
    packed = jnp.concatenate(
        [rows_real, rows_imag, jnp.broadcast_to(jnp.sum(weights), (SR, 128))], axis=1
    )
    width = tile + 2 * HALO
    columns = jnp.mod(
        lax.axis_index("scan") * tile - HALO + jnp.arange(width, dtype=jnp.int32), SC
    )
    col_angles = phase_angles(jnp.arange(SC, dtype=jnp.int32), columns, SC)
    cos_cols, sin_cols = lax.optimization_barrier((jnp.cos(col_angles), jnp.sin(col_angles)))
    axes = ("scan", "det")
    count = scan_size * det_size
    quarters = packed.reshape(4, 4, packed.shape[1])
    partial = exchange(quarters, axes, count, 0, 2, lambda x: x)
    own = exchange(partial, axes, count, 2, 2, lambda x: x.reshape(1, 4, x.shape[1]))
    own = own.reshape(-1)
    partners = [own] + [
        lax.ppermute(own, axes, [(i, i ^ (d << 4)) for i in range(count)]) for d in range(1, 8)
    ]
    while len(partners) > 1:
        partners = [partners[e] + partners[e + 1] for e in range(0, len(partners), 2)]
    total = partners[0]
    line_real = total[:SC]
    line_imag = total[SC : 2 * SC]
    bright_sum = total[2 * SC]
    picture = jnp.dot(line_real, cos_cols, precision=EXACT_PRECISION) - jnp.dot(
        line_imag, sin_cols, precision=EXACT_PRECISION
    )
    return (
        (picture * (1.0 / (SR * SC)) / jnp.sqrt(bright_sum) * window_weights(width))
        .reshape(rows_dev, 1, width)
    )


def solution(mesh):
    placed = (P("det", "scan", None), P(("scan", "det"), None), P(("scan", "det")), P())
    return jax.shard_map(
        local, mesh=mesh, in_specs=placed, out_specs=P("det", "scan", None), check_vma=False
    )
```

```python
import math

import jax
import jax.numpy as jnp
from jax import lax
from jax.sharding import PartitionSpec as P
from jax.experimental import pallas as pl

SR = 16
SC = 1024
DROWS = 128
DCOLS = 128
HALO = 16


TWO_PI = 2.0 * math.pi
EXACT_PRECISION = lax.Precision.HIGHEST


def phase_angles(first, second_operand, modulus):
    product = jnp.mod(first[:, None] * second_operand[None, :], modulus)
    return TWO_PI / modulus * product.astype(jnp.float32)


def signed_frequency(length):
    position = jnp.arange(length, dtype=jnp.int32)
    folded = jnp.where(position < length // 2, position, position - length)
    return 2.0 * folded.astype(jnp.float32) / length


def pixel_phase(pixel_index, shifts, aberration):
    freq_rows = signed_frequency(SR)[:, None, None]
    freq_cols = signed_frequency(SC)[None, :, None]
    half_rows = DROWS // 2
    half_cols = DCOLS // 2
    tilt_x = ((pixel_index // DCOLS - half_rows).astype(jnp.float32) / half_rows)[None, None, :]
    tilt_y = ((pixel_index % DCOLS - half_cols).astype(jnp.float32) / half_cols)[None, None, :]
    ramp_rows = jnp.mod(jnp.arange(SR, dtype=jnp.int32)[:, None] * shifts[:, 0][None, :], SR)
    ramp_cols = jnp.mod(jnp.arange(SC, dtype=jnp.int32)[:, None] * shifts[:, 1][None, :], SC)
    shift_phase = (
        TWO_PI / SR * ramp_rows.astype(jnp.float32)[:, None, :]
        + TWO_PI / SC * ramp_cols.astype(jnp.float32)[None, :, :]
    )
    tilt_sq = tilt_x * tilt_x + tilt_y * tilt_y
    tilt_dot = tilt_x * freq_rows + tilt_y * freq_cols
    moved_x = freq_rows + tilt_x
    moved_y = freq_cols + tilt_y
    moved_sq = moved_x * moved_x + moved_y * moved_y
    lens_phase = math.pi * (
        aberration[0] * (freq_rows * freq_rows + freq_cols * freq_cols)
        + aberration[1] * (moved_sq * moved_sq - tilt_sq * tilt_sq - 4.0 * tilt_sq * tilt_dot)
    )
    return shift_phase - lens_phase


def window_weights(width):
    position = jnp.arange(width, dtype=jnp.int32)
    nearest = jnp.minimum(position, width - 1 - position)
    ramped = 0.3 + 0.35 * (
        1.0 - jnp.cos(math.pi * (nearest.astype(jnp.float32) + 0.5) / (2 * HALO))
    )
    return jnp.where(nearest < 2 * HALO, ramped, jnp.float32(1.0))


def inverse_transform(spec_real, spec_imag, columns, rows):
    real_piece = jnp.dot(spec_real, cos_cols, precision=EXACT_PRECISION) - jnp.dot(
        spec_imag, sin_cols, precision=EXACT_PRECISION
    )
    imaginary_piece = jnp.dot(spec_real, sin_cols, precision=EXACT_PRECISION) + jnp.dot(
        spec_imag, cos_cols, precision=EXACT_PRECISION
    )
    angles_by_row = phase_angles(jnp.arange(SR, dtype=jnp.int32), rows, SR)
    row_cosines = jnp.cos(angles_by_row)
    row_sines = jnp.sin(angles_by_row)
    return jnp.dot(row_cosines.T, real_piece, precision=EXACT_PRECISION) - jnp.dot(
        row_sines.T, imaginary_piece, precision=EXACT_PRECISION
    )


def sincos_reduced(rest, quadrant):
    square = rest * rest
    sine = rest + rest * square * (
        -1.6666654611e-1 + square * (8.3321608736e-3 + square * -1.9515295891e-4)
    )
    cosine = 1.0 - 0.5 * square + square * square * (
        4.166664568298827e-2 + square * (-1.388731625493765e-3 + square * 2.443315711809948e-5)
    )
    swap = (quadrant & 1) == 1
    sin_out = jnp.where(swap, cosine, sine)
    cos_out = jnp.where(swap, sine, cosine)
    sin_out = jnp.where(quadrant >= 2, -sin_out, sin_out)
    cos_out = jnp.where((quadrant == 1) | (quadrant == 2), -cos_out, cos_out)
    return sin_out, cos_out


def sincos(angle):
    turns = jnp.round(angle * (2.0 / math.pi))
    quadrant = turns.astype(jnp.int32) & 3
    rest = angle - turns * 1.5703125
    rest = rest - turns * 4.837512969970703125e-4
    rest = rest - turns * 7.54978995489188216e-8
    return sincos_reduced(rest, quadrant)


def sincos_of_steps(steps, modulus):
    quarter = modulus // 4
    turns = (steps + quarter // 2) // quarter
    rest = (steps - turns * quarter).astype(jnp.float32) * (TWO_PI / modulus)
    return sincos_reduced(rest, turns & 3)


def pairwise_sum(values):
    while len(values) > 1:
        values = [
            values[e] + values[e + 1] if e + 1 < len(values) else values[e]
            for e in range(0, len(values), 2)
        ]
    return values[0]


def phase_parts(pixel_index, shifts, aberration):
    freq_rows = signed_frequency(SR)[:, None]
    freq_cols = signed_frequency(SC)[:, None]
    half_rows = DROWS // 2
    half_cols = DCOLS // 2
    tilt_x = ((pixel_index // DCOLS - half_rows).astype(jnp.float32) / half_rows)[None, :]
    tilt_y = ((pixel_index % DCOLS - half_cols).astype(jnp.float32) / half_cols)[None, :]
    ramp_rows = jnp.mod(jnp.arange(SR, dtype=jnp.int32)[:, None] * shifts[:, 0][None, :], SR)
    ramp_cols = jnp.mod(jnp.arange(SC, dtype=jnp.int32)[:, None] * shifts[:, 1][None, :], SC)
    tilt_sq = tilt_x * tilt_x + tilt_y * tilt_y
    defocus = math.pi * aberration[0]
    spherical = math.pi * aberration[1]
    row_part = (
        TWO_PI / SR * ramp_rows.astype(jnp.float32)
        - defocus * freq_rows * freq_rows
        + spherical * (tilt_sq * tilt_sq + 4.0 * tilt_sq * tilt_x * freq_rows)
    )
    col_part = (
        TWO_PI / SC * ramp_cols.astype(jnp.float32)
        - defocus * freq_cols * freq_cols
        + spherical * (4.0 * tilt_sq * tilt_y * freq_cols)
    )
    moved_rows = (freq_rows + tilt_x) * (freq_rows + tilt_x)
    moved_cols = (freq_cols + tilt_y) * (freq_cols + tilt_y)
    return row_part, col_part, moved_rows, moved_cols, spherical


def four_point(points):
    (ar, ai), (br, bi), (cr, ci), (dr, di) = points
    s02r = ar + cr
    s02i = ai + ci
    d02r = ar - cr
    d02i = ai - ci
    s13r = br + dr
    s13i = bi + di
    d13r = br - dr
    d13i = bi - di
    return [
        (s02r + s13r, s02i + s13i),
        (d02r + d13i, d02i - d13r),
        (s02r - s13r, s02i - s13i),
        (d02r - d13i, d02i + d13r),
    ]


def fft16(points):
    twisted = {}
    for b in range(4):
        column = four_point([points[4 * a + b] for a in range(4)])
        for s1, (gr, gi) in enumerate(column):
            k = b * s1
            if k == 0:
                twisted[b, s1] = (gr, gi)
            elif k == 4:
                twisted[b, s1] = (gi, -gr)
            else:
                c = math.cos(TWO_PI * k / 16)
                d = math.sin(TWO_PI * k / 16)
                twisted[b, s1] = (gr * c + gi * d, gi * c - gr * d)
    out = [None] * 16
    for s1 in range(4):
        row = four_point([twisted[b, s1] for b in range(4)])
        for s2 in range(4):
            out[s1 + 4 * s2] = row[s2]
    return out


def spectrum_kernel(re_ref, im_ref, tc_ref, ts_ref, out_ref):
    out_ref[...] = jnp.zeros(out_ref.shape, out_ref.dtype)

    def body(i, carry):
        rows = pl.ds(pl.multiple_of(i * 8, 8), 8)
        full = fft16([(re_ref[r, rows, :], im_ref[r, rows, :]) for r in range(SR)])
        for s in range(SR):
            fr, fi = full[s]
            tc = tc_ref[s, rows, :]
            ts = ts_ref[s, rows, :]
            out_ref[0, s] += fr * tc - fi * ts
            out_ref[1, s] += fr * ts + fi * tc
        return carry

    lax.fori_loop(0, re_ref.shape[1] // 8, body, 0)


def spectrum(both_col, turn_cos, turn_sin):
    pixels = both_col.shape[1]
    block = 128
    steps = SC // block
    spec = pl.pallas_call(
        spectrum_kernel,
        grid=(steps,),
        in_specs=[
            pl.BlockSpec((SR, pixels, block), lambda j: (0, 0, j)),
            pl.BlockSpec((SR, pixels, block), lambda j: (0, 0, j + steps)),
            pl.BlockSpec((SR, pixels, block), lambda j: (0, 0, j)),
            pl.BlockSpec((SR, pixels, block), lambda j: (0, 0, j)),
        ],
        out_specs=pl.BlockSpec((2, SR, 8, block), lambda j: (0, 0, 0, j)),
        out_shape=jax.ShapeDtypeStruct((2, SR, 8, SC), jnp.float32),
    )(both_col, both_col, turn_cos, turn_sin)
    return jnp.sum(spec, axis=2)


def local(frames, offsets, bright, aberration):
    scan_size = lax.axis_size("scan")
    det_size = lax.axis_size("det")
    rows_dev, tile, detector = frames.shape
    owned = offsets.shape[0]
    groups = detector // owned
    owner = lax.axis_index("scan") * det_size + lax.axis_index("det")
    blocks = jnp.transpose(frames.reshape(rows_dev * tile, groups, owned), (1, 0, 2))
    arrived = lax.all_to_all(blocks, ("scan", "det"), split_axis=0, concat_axis=0, tiled=True)
    images = arrived.reshape(scan_size, det_size, rows_dev, tile, owned)
    full_cols = jnp.arange(SC, dtype=jnp.int32)
    col_sin, col_cos = sincos_of_steps(jnp.mod(full_cols[:, None] * full_cols[None, :], SC), SC)
    col_cos = col_cos.astype(jnp.bfloat16)
    col_sin = col_sin.astype(jnp.bfloat16)
    table = jnp.concatenate([col_cos, -col_sin], axis=1).reshape(scan_size, tile, 2 * SC)
    both_col = jnp.einsum(
        "abrcp,acq->brpq", images, table, preferred_element_type=jnp.float32
    ).reshape(SR, owned, 2 * SC)
    full_rows = jnp.arange(SR, dtype=jnp.int32)
    angles_by_row = phase_angles(full_rows, full_rows, SR)
    row_cos = jnp.cos(angles_by_row)
    row_sin = jnp.sin(angles_by_row)
    pixel_index = owner * owned + jnp.arange(owned, dtype=jnp.int32)
    row_part, col_part, moved_rows, moved_cols, spherical = phase_parts(
        pixel_index, offsets, aberration
    )
    moved_sq = moved_rows[:, :, None] + moved_cols.T[None, :, :]
    phase = row_part[:, :, None] + col_part.T[None, :, :] - spherical * (moved_sq * moved_sq)
    weights = bright.astype(jnp.float32)
    turn_sin, turn_cos = sincos(phase)
    turn_cos, turn_sin = lax.optimization_barrier(
        (turn_cos * weights[None, :, None], turn_sin * weights[None, :, None])
    )
    spec_real, spec_imag = spectrum(both_col, turn_cos, turn_sin)
    row_cos_t = row_cos.T
    row_sin_t = row_sin.T
    rows_real = jnp.dot(row_cos_t, spec_real, precision=EXACT_PRECISION) - jnp.dot(
        row_sin_t, spec_imag, precision=EXACT_PRECISION
    )
    rows_imag = jnp.dot(row_sin_t, spec_real, precision=EXACT_PRECISION) + jnp.dot(
        row_cos_t, spec_imag, precision=EXACT_PRECISION
    )
    packed = jnp.concatenate(
        [rows_real, rows_imag, jnp.broadcast_to(jnp.sum(weights), (SR, 128))], axis=1
    )
    width = tile + 2 * HALO
    columns = jnp.mod(
        lax.axis_index("scan") * tile - HALO + jnp.arange(width, dtype=jnp.int32), SC
    )
    col_angles = phase_angles(jnp.arange(SC, dtype=jnp.int32), columns, SC)
    cos_cols, sin_cols = lax.optimization_barrier((jnp.cos(col_angles), jnp.sin(col_angles)))
    gathered = lax.all_to_all(packed, "det", 0, 0, tiled=True)
    own = pairwise_sum([gathered[i] for i in range(det_size)])
    spread = jnp.broadcast_to(own, (scan_size,) + own.shape)
    gathered = lax.all_to_all(spread, "scan", 0, 0, tiled=True)
    total = pairwise_sum([gathered[i] for i in range(scan_size)])
    line_real = total[:SC]
    line_imag = total[SC : 2 * SC]
    bright_sum = total[2 * SC]
    picture = jnp.dot(line_real, cos_cols, precision=EXACT_PRECISION) - jnp.dot(
        line_imag, sin_cols, precision=EXACT_PRECISION
    )
    return (
        (picture * (1.0 / (SR * SC)) / jnp.sqrt(bright_sum) * window_weights(width))
        .reshape(rows_dev, 1, width)
    )


def solution(mesh):
    placed = (P("det", "scan", None), P(("scan", "det"), None), P(("scan", "det")), P())
    return jax.shard_map(
        local, mesh=mesh, in_specs=placed, out_specs=P("det", "scan", None), check_vma=False
    )
```

```python
import math

import jax
import jax.numpy as jnp
from jax import lax
from jax.sharding import PartitionSpec as P
from jax.experimental import pallas as pl
from jax.experimental.pallas import tpu as pltpu

SR = 16
SC = 1024
DROWS = 128
DCOLS = 128
HALO = 16


TWO_PI = 2.0 * math.pi
EXACT_PRECISION = lax.Precision.HIGHEST


def phase_angles(first, second_operand, modulus):
    product = jnp.mod(first[:, None] * second_operand[None, :], modulus)
    return TWO_PI / modulus * product.astype(jnp.float32)


def signed_frequency(length):
    position = jnp.arange(length, dtype=jnp.int32)
    folded = jnp.where(position < length // 2, position, position - length)
    return 2.0 * folded.astype(jnp.float32) / length


def pixel_phase(pixel_index, shifts, aberration):
    freq_rows = signed_frequency(SR)[:, None, None]
    freq_cols = signed_frequency(SC)[None, :, None]
    half_rows = DROWS // 2
    half_cols = DCOLS // 2
    tilt_x = ((pixel_index // DCOLS - half_rows).astype(jnp.float32) / half_rows)[None, None, :]
    tilt_y = ((pixel_index % DCOLS - half_cols).astype(jnp.float32) / half_cols)[None, None, :]
    ramp_rows = jnp.mod(jnp.arange(SR, dtype=jnp.int32)[:, None] * shifts[:, 0][None, :], SR)
    ramp_cols = jnp.mod(jnp.arange(SC, dtype=jnp.int32)[:, None] * shifts[:, 1][None, :], SC)
    shift_phase = (
        TWO_PI / SR * ramp_rows.astype(jnp.float32)[:, None, :]
        + TWO_PI / SC * ramp_cols.astype(jnp.float32)[None, :, :]
    )
    tilt_sq = tilt_x * tilt_x + tilt_y * tilt_y
    tilt_dot = tilt_x * freq_rows + tilt_y * freq_cols
    moved_x = freq_rows + tilt_x
    moved_y = freq_cols + tilt_y
    moved_sq = moved_x * moved_x + moved_y * moved_y
    lens_phase = math.pi * (
        aberration[0] * (freq_rows * freq_rows + freq_cols * freq_cols)
        + aberration[1] * (moved_sq * moved_sq - tilt_sq * tilt_sq - 4.0 * tilt_sq * tilt_dot)
    )
    return shift_phase - lens_phase


def window_weights(width):
    position = jnp.arange(width, dtype=jnp.int32)
    nearest = jnp.minimum(position, width - 1 - position)
    ramped = 0.3 + 0.35 * (
        1.0 - jnp.cos(math.pi * (nearest.astype(jnp.float32) + 0.5) / (2 * HALO))
    )
    return jnp.where(nearest < 2 * HALO, ramped, jnp.float32(1.0))


def inverse_transform(spec_real, spec_imag, columns, rows):
    real_piece = jnp.dot(spec_real, cos_cols, precision=EXACT_PRECISION) - jnp.dot(
        spec_imag, sin_cols, precision=EXACT_PRECISION
    )
    imaginary_piece = jnp.dot(spec_real, sin_cols, precision=EXACT_PRECISION) + jnp.dot(
        spec_imag, cos_cols, precision=EXACT_PRECISION
    )
    angles_by_row = phase_angles(jnp.arange(SR, dtype=jnp.int32), rows, SR)
    row_cosines = jnp.cos(angles_by_row)
    row_sines = jnp.sin(angles_by_row)
    return jnp.dot(row_cosines.T, real_piece, precision=EXACT_PRECISION) - jnp.dot(
        row_sines.T, imaginary_piece, precision=EXACT_PRECISION
    )


def sincos_reduced(rest, quadrant):
    square = rest * rest
    sine = rest + rest * square * (
        -1.6666654611e-1 + square * (8.3321608736e-3 + square * -1.9515295891e-4)
    )
    cosine = 1.0 - 0.5 * square + square * square * (
        4.166664568298827e-2 + square * (-1.388731625493765e-3 + square * 2.443315711809948e-5)
    )
    swap = (quadrant & 1) == 1
    sin_out = jnp.where(swap, cosine, sine)
    cos_out = jnp.where(swap, sine, cosine)
    sin_out = jnp.where(quadrant >= 2, -sin_out, sin_out)
    cos_out = jnp.where((quadrant == 1) | (quadrant == 2), -cos_out, cos_out)
    return sin_out, cos_out


def sincos(angle):
    turns = jnp.round(angle * (2.0 / math.pi))
    quadrant = turns.astype(jnp.int32) & 3
    rest = angle - turns * 1.5703125
    rest = rest - turns * 4.837512969970703125e-4
    rest = rest - turns * 7.54978995489188216e-8
    return sincos_reduced(rest, quadrant)


def sincos_of_steps(steps, modulus):
    quarter = modulus // 4
    turns = (steps + quarter // 2) // quarter
    rest = (steps - turns * quarter).astype(jnp.float32) * (TWO_PI / modulus)
    return sincos_reduced(rest, turns & 3)


def pairwise_sum(values):
    while len(values) > 1:
        values = [
            values[e] + values[e + 1] if e + 1 < len(values) else values[e]
            for e in range(0, len(values), 2)
        ]
    return values[0]


def phase_parts(pixel_index, shifts, aberration):
    freq_rows = signed_frequency(SR)[:, None]
    freq_cols = signed_frequency(SC)[:, None]
    half_rows = DROWS // 2
    half_cols = DCOLS // 2
    tilt_x = ((pixel_index // DCOLS - half_rows).astype(jnp.float32) / half_rows)[None, :]
    tilt_y = ((pixel_index % DCOLS - half_cols).astype(jnp.float32) / half_cols)[None, :]
    ramp_rows = jnp.mod(jnp.arange(SR, dtype=jnp.int32)[:, None] * shifts[:, 0][None, :], SR)
    ramp_cols = jnp.mod(jnp.arange(SC, dtype=jnp.int32)[:, None] * shifts[:, 1][None, :], SC)
    tilt_sq = tilt_x * tilt_x + tilt_y * tilt_y
    defocus = math.pi * aberration[0]
    spherical = math.pi * aberration[1]
    row_part = (
        TWO_PI / SR * ramp_rows.astype(jnp.float32)
        - defocus * freq_rows * freq_rows
        + spherical * (tilt_sq * tilt_sq + 4.0 * tilt_sq * tilt_x * freq_rows)
    )
    col_part = (
        TWO_PI / SC * ramp_cols.astype(jnp.float32)
        - defocus * freq_cols * freq_cols
        + spherical * (4.0 * tilt_sq * tilt_y * freq_cols)
    )
    moved_rows = (freq_rows + tilt_x) * (freq_rows + tilt_x)
    moved_cols = (freq_cols + tilt_y) * (freq_cols + tilt_y)
    return row_part, col_part, moved_rows, moved_cols, spherical


def four_point(points):
    (ar, ai), (br, bi), (cr, ci), (dr, di) = points
    s02r = ar + cr
    s02i = ai + ci
    d02r = ar - cr
    d02i = ai - ci
    s13r = br + dr
    s13i = bi + di
    d13r = br - dr
    d13i = bi - di
    return [
        (s02r + s13r, s02i + s13i),
        (d02r + d13i, d02i - d13r),
        (s02r - s13r, s02i - s13i),
        (d02r - d13i, d02i + d13r),
    ]


def fft16(points):
    twisted = {}
    for b in range(4):
        column = four_point([points[4 * a + b] for a in range(4)])
        for s1, (gr, gi) in enumerate(column):
            k = b * s1
            if k == 0:
                twisted[b, s1] = (gr, gi)
            elif k == 4:
                twisted[b, s1] = (gi, -gr)
            else:
                c = math.cos(TWO_PI * k / 16)
                d = math.sin(TWO_PI * k / 16)
                twisted[b, s1] = (gr * c + gi * d, gi * c - gr * d)
    out = [None] * 16
    for s1 in range(4):
        row = four_point([twisted[b, s1] for b in range(4)])
        for s2 in range(4):
            out[s1 + 4 * s2] = row[s2]
    return out


def fused_kernel(x_ref, t_ref, tc_ref, ts_ref, out_ref, y_ref):
    step = pl.program_id(0)
    blocks = pl.num_programs(0) - 1
    sources = x_ref.shape[0] // SR
    width = tc_ref.shape[2]
    slot = step % 2

    def columns(i):
        acc = jnp.zeros((x_ref.shape[1], 2 * width), jnp.float32)
        for t in range(sources):
            acc = acc + jnp.dot(
                x_ref[t * SR + i],
                t_ref[pl.ds(t * x_ref.shape[2], x_ref.shape[2]), :],
                preferred_element_type=jnp.float32,
            )
        y_ref[slot, i] = acc

    def rows(i):
        lines = pl.ds(pl.multiple_of(i * 8, 8), 8)
        full = fft16(
            [
                (y_ref[1 - slot, r, lines, pl.ds(0, width)], y_ref[1 - slot, r, lines, pl.ds(width, width)])
                for r in range(SR)
            ]
        )
        for s in range(SR):
            fr, fi = full[s]
            tc = tc_ref[s, lines, :]
            ts = ts_ref[s, lines, :]
            out_ref[0, s] += fr * tc - fi * ts
            out_ref[1, s] += fr * ts + fi * tc

    def both(i, carry):
        columns(i)
        rows(i)
        return carry

    def first(i, carry):
        columns(i)
        return carry

    def last(i, carry):
        rows(i)
        return carry

    @pl.when(step == 0)
    def _():
        lax.fori_loop(0, SR, first, 0)

    @pl.when((step > 0) & (step < blocks))
    def _():
        out_ref[...] = jnp.zeros(out_ref.shape, out_ref.dtype)
        lax.fori_loop(0, SR, both, 0)

    @pl.when(step == blocks)
    def _():
        out_ref[...] = jnp.zeros(out_ref.shape, out_ref.dtype)
        lax.fori_loop(0, x_ref.shape[1] // 8, last, 0)


def spectrum(sources, table, turn_cos, turn_sin):
    pixels = sources.shape[1]
    chunk = sources.shape[2]
    block = 128
    steps = SC // block
    spec = pl.pallas_call(
        fused_kernel,
        grid=(steps + 1,),
        in_specs=[
            pl.BlockSpec(sources.shape, lambda j: (0, 0, 0)),
            pl.BlockSpec((table.shape[0], 2 * block), lambda j: (0, jnp.minimum(j, steps - 1))),
            pl.BlockSpec((SR, pixels, block), lambda j: (0, 0, jnp.maximum(j - 1, 0))),
            pl.BlockSpec((SR, pixels, block), lambda j: (0, 0, jnp.maximum(j - 1, 0))),
        ],
        out_specs=pl.BlockSpec((2, SR, 8, block), lambda j: (0, 0, 0, jnp.maximum(j - 1, 0))),
        out_shape=jax.ShapeDtypeStruct((2, SR, 8, SC), jnp.float32),
        scratch_shapes=[pltpu.VMEM((2, SR, pixels, 2 * block), jnp.float32)],
        compiler_params=pltpu.CompilerParams(vmem_limit_bytes=48 * 1024 * 1024),
    )(sources, table, turn_cos, turn_sin)
    return jnp.sum(spec, axis=2)


def local(frames, offsets, bright, aberration):
    scan_size = lax.axis_size("scan")
    det_size = lax.axis_size("det")
    rows_dev, tile, detector = frames.shape
    owned = offsets.shape[0]
    groups = detector // owned
    owner = lax.axis_index("scan") * det_size + lax.axis_index("det")
    blocks = jnp.transpose(frames.reshape(rows_dev * tile, groups, owned), (1, 0, 2))
    arrived = lax.all_to_all(blocks, ("scan", "det"), split_axis=0, concat_axis=0, tiled=True)
    full_cols = jnp.arange(SC, dtype=jnp.int32)
    col_sin, col_cos = sincos_of_steps(jnp.mod(full_cols[:, None] * full_cols[None, :], SC), SC)
    col_cos = col_cos.astype(jnp.bfloat16)
    col_sin = col_sin.astype(jnp.bfloat16)
    table = jnp.stack(
        [col_cos.reshape(SC, SC // 128, 128), -col_sin.reshape(SC, SC // 128, 128)], axis=2
    ).reshape(SC, 2 * SC)
    sources = jnp.swapaxes(arrived, 1, 2)
    full_rows = jnp.arange(SR, dtype=jnp.int32)
    angles_by_row = phase_angles(full_rows, full_rows, SR)
    row_cos = jnp.cos(angles_by_row)
    row_sin = jnp.sin(angles_by_row)
    pixel_index = owner * owned + jnp.arange(owned, dtype=jnp.int32)
    row_part, col_part, moved_rows, moved_cols, spherical = phase_parts(
        pixel_index, offsets, aberration
    )
    moved_sq = moved_rows[:, :, None] + moved_cols.T[None, :, :]
    phase = row_part[:, :, None] + col_part.T[None, :, :] - spherical * (moved_sq * moved_sq)
    weights = bright.astype(jnp.float32)
    turn_sin, turn_cos = sincos(phase)
    turn_cos, turn_sin = lax.optimization_barrier(
        (turn_cos * weights[None, :, None], turn_sin * weights[None, :, None])
    )
    spec_real, spec_imag = spectrum(sources, table, turn_cos, turn_sin)
    row_cos_t = row_cos.T
    row_sin_t = row_sin.T
    rows_real = jnp.dot(row_cos_t, spec_real, precision=EXACT_PRECISION) - jnp.dot(
        row_sin_t, spec_imag, precision=EXACT_PRECISION
    )
    rows_imag = jnp.dot(row_sin_t, spec_real, precision=EXACT_PRECISION) + jnp.dot(
        row_cos_t, spec_imag, precision=EXACT_PRECISION
    )
    packed = jnp.concatenate(
        [rows_real, rows_imag, jnp.broadcast_to(jnp.sum(weights), (SR, 128))], axis=1
    )
    width = tile + 2 * HALO
    columns = jnp.mod(
        lax.axis_index("scan") * tile - HALO + jnp.arange(width, dtype=jnp.int32), SC
    )
    col_angles = phase_angles(jnp.arange(SC, dtype=jnp.int32), columns, SC)
    cos_cols, sin_cols = lax.optimization_barrier((jnp.cos(col_angles), jnp.sin(col_angles)))
    gathered = lax.all_to_all(packed, "det", 0, 0, tiled=True)
    own = pairwise_sum([gathered[i] for i in range(det_size)])
    spread = jnp.broadcast_to(own, (scan_size,) + own.shape)
    gathered = lax.all_to_all(spread, "scan", 0, 0, tiled=True)
    total = pairwise_sum([gathered[i] for i in range(scan_size)])
    line_real = total[:SC]
    line_imag = total[SC : 2 * SC]
    bright_sum = total[2 * SC]
    picture = jnp.dot(line_real, cos_cols, precision=EXACT_PRECISION) - jnp.dot(
        line_imag, sin_cols, precision=EXACT_PRECISION
    )
    return (
        (picture * (1.0 / (SR * SC)) / jnp.sqrt(bright_sum) * window_weights(width))
        .reshape(rows_dev, 1, width)
    )


def solution(mesh):
    placed = (P("det", "scan", None), P(("scan", "det"), None), P(("scan", "det")), P())
    return jax.shard_map(
        local, mesh=mesh, in_specs=placed, out_specs=P("det", "scan", None), check_vma=False
    )
```

```python
import math

import jax
import jax.numpy as jnp
from jax import lax
from jax.sharding import PartitionSpec as P
from jax.experimental import pallas as pl

SR = 16
SC = 1024
DROWS = 128
DCOLS = 128
HALO = 16


TWO_PI = 2.0 * math.pi
EXACT_PRECISION = lax.Precision.HIGHEST


def phase_angles(first, second_operand, modulus):
    product = jnp.mod(first[:, None] * second_operand[None, :], modulus)
    return TWO_PI / modulus * product.astype(jnp.float32)


def signed_frequency(length):
    position = jnp.arange(length, dtype=jnp.int32)
    folded = jnp.where(position < length // 2, position, position - length)
    return 2.0 * folded.astype(jnp.float32) / length


def pixel_phase(pixel_index, shifts, aberration):
    freq_rows = signed_frequency(SR)[:, None, None]
    freq_cols = signed_frequency(SC)[None, :, None]
    half_rows = DROWS // 2
    half_cols = DCOLS // 2
    tilt_x = ((pixel_index // DCOLS - half_rows).astype(jnp.float32) / half_rows)[None, None, :]
    tilt_y = ((pixel_index % DCOLS - half_cols).astype(jnp.float32) / half_cols)[None, None, :]
    ramp_rows = jnp.mod(jnp.arange(SR, dtype=jnp.int32)[:, None] * shifts[:, 0][None, :], SR)
    ramp_cols = jnp.mod(jnp.arange(SC, dtype=jnp.int32)[:, None] * shifts[:, 1][None, :], SC)
    shift_phase = (
        TWO_PI / SR * ramp_rows.astype(jnp.float32)[:, None, :]
        + TWO_PI / SC * ramp_cols.astype(jnp.float32)[None, :, :]
    )
    tilt_sq = tilt_x * tilt_x + tilt_y * tilt_y
    tilt_dot = tilt_x * freq_rows + tilt_y * freq_cols
    moved_x = freq_rows + tilt_x
    moved_y = freq_cols + tilt_y
    moved_sq = moved_x * moved_x + moved_y * moved_y
    lens_phase = math.pi * (
        aberration[0] * (freq_rows * freq_rows + freq_cols * freq_cols)
        + aberration[1] * (moved_sq * moved_sq - tilt_sq * tilt_sq - 4.0 * tilt_sq * tilt_dot)
    )
    return shift_phase - lens_phase


def window_weights(width):
    position = jnp.arange(width, dtype=jnp.int32)
    nearest = jnp.minimum(position, width - 1 - position)
    ramped = 0.3 + 0.35 * (
        1.0 - jnp.cos(math.pi * (nearest.astype(jnp.float32) + 0.5) / (2 * HALO))
    )
    return jnp.where(nearest < 2 * HALO, ramped, jnp.float32(1.0))


def inverse_transform(spec_real, spec_imag, columns, rows):
    real_piece = jnp.dot(spec_real, cos_cols, precision=EXACT_PRECISION) - jnp.dot(
        spec_imag, sin_cols, precision=EXACT_PRECISION
    )
    imaginary_piece = jnp.dot(spec_real, sin_cols, precision=EXACT_PRECISION) + jnp.dot(
        spec_imag, cos_cols, precision=EXACT_PRECISION
    )
    angles_by_row = phase_angles(jnp.arange(SR, dtype=jnp.int32), rows, SR)
    row_cosines = jnp.cos(angles_by_row)
    row_sines = jnp.sin(angles_by_row)
    return jnp.dot(row_cosines.T, real_piece, precision=EXACT_PRECISION) - jnp.dot(
        row_sines.T, imaginary_piece, precision=EXACT_PRECISION
    )


def sincos_reduced(rest, quadrant):
    square = rest * rest
    sine = rest + rest * square * (
        -1.6666654611e-1 + square * (8.3321608736e-3 + square * -1.9515295891e-4)
    )
    cosine = 1.0 - 0.5 * square + square * square * (
        4.166664568298827e-2 + square * (-1.388731625493765e-3 + square * 2.443315711809948e-5)
    )
    swap = (quadrant & 1) == 1
    sin_out = jnp.where(swap, cosine, sine)
    cos_out = jnp.where(swap, sine, cosine)
    sin_out = jnp.where(quadrant >= 2, -sin_out, sin_out)
    cos_out = jnp.where((quadrant == 1) | (quadrant == 2), -cos_out, cos_out)
    return sin_out, cos_out


def sincos(angle):
    turns = jnp.round(angle * (2.0 / math.pi))
    quadrant = turns.astype(jnp.int32) & 3
    rest = angle - turns * 1.5703125
    rest = rest - turns * 4.837512969970703125e-4
    rest = rest - turns * 7.54978995489188216e-8
    return sincos_reduced(rest, quadrant)


def sincos_of_steps(steps, modulus):
    quarter = modulus // 4
    turns = (steps + quarter // 2) // quarter
    rest = (steps - turns * quarter).astype(jnp.float32) * (TWO_PI / modulus)
    return sincos_reduced(rest, turns & 3)


def pairwise_sum(values):
    while len(values) > 1:
        values = [
            values[e] + values[e + 1] if e + 1 < len(values) else values[e]
            for e in range(0, len(values), 2)
        ]
    return values[0]


def phase_parts(pixel_index, shifts, aberration, col_index):
    freq_rows = signed_frequency(SR)[:, None]
    freq_cols = jnp.take(signed_frequency(SC), col_index)[:, None]
    half_rows = DROWS // 2
    half_cols = DCOLS // 2
    tilt_x = ((pixel_index // DCOLS - half_rows).astype(jnp.float32) / half_rows)[None, :]
    tilt_y = ((pixel_index % DCOLS - half_cols).astype(jnp.float32) / half_cols)[None, :]
    ramp_rows = jnp.mod(jnp.arange(SR, dtype=jnp.int32)[:, None] * shifts[:, 0][None, :], SR)
    ramp_cols = jnp.mod(col_index[:, None] * shifts[:, 1][None, :], SC)
    tilt_sq = tilt_x * tilt_x + tilt_y * tilt_y
    defocus = math.pi * aberration[0]
    spherical = math.pi * aberration[1]
    row_part = (
        TWO_PI / SR * ramp_rows.astype(jnp.float32)
        - defocus * freq_rows * freq_rows
        + spherical * (tilt_sq * tilt_sq + 4.0 * tilt_sq * tilt_x * freq_rows)
    )
    col_part = (
        TWO_PI / SC * ramp_cols.astype(jnp.float32)
        - defocus * freq_cols * freq_cols
        + spherical * (4.0 * tilt_sq * tilt_y * freq_cols)
    )
    moved_rows = (freq_rows + tilt_x) * (freq_rows + tilt_x)
    moved_cols = (freq_cols + tilt_y) * (freq_cols + tilt_y)
    return row_part, col_part, moved_rows, moved_cols, spherical


def four_point(points):
    (ar, ai), (br, bi), (cr, ci), (dr, di) = points
    s02r = ar + cr
    s02i = ai + ci
    d02r = ar - cr
    d02i = ai - ci
    s13r = br + dr
    s13i = bi + di
    d13r = br - dr
    d13i = bi - di
    return [
        (s02r + s13r, s02i + s13i),
        (d02r + d13i, d02i - d13r),
        (s02r - s13r, s02i - s13i),
        (d02r - d13i, d02i + d13r),
    ]


def fft16(points):
    twisted = {}
    for b in range(4):
        column = four_point([points[4 * a + b] for a in range(4)])
        for s1, (gr, gi) in enumerate(column):
            k = b * s1
            if k == 0:
                twisted[b, s1] = (gr, gi)
            elif k == 4:
                twisted[b, s1] = (gi, -gr)
            else:
                c = math.cos(TWO_PI * k / 16)
                d = math.sin(TWO_PI * k / 16)
                twisted[b, s1] = (gr * c + gi * d, gi * c - gr * d)
    out = [None] * 16
    for s1 in range(4):
        row = four_point([twisted[b, s1] for b in range(4)])
        for s2 in range(4):
            out[s1 + 4 * s2] = row[s2]
    return out


def spectrum_kernel(re_ref, im_ref, lc_ref, ls_ref, uc_ref, us_ref, out_ref):
    out_ref[...] = jnp.zeros(out_ref.shape, out_ref.dtype)

    def body(i, carry):
        rows = pl.ds(pl.multiple_of(i * 8, 8), 8)
        full = fft16([(re_ref[r, rows, :], im_ref[r, rows, :]) for r in range(SR)])
        for s in range(SR):
            fr, fi = full[s]
            tc = lc_ref[s, rows, :]
            ts = ls_ref[s, rows, :]
            out_ref[0, 0, s] += fr * tc - fi * ts
            out_ref[0, 1, s] += fr * ts + fi * tc
            gr, gi = full[(SR - s) % SR]
            tc = uc_ref[s, rows, :]
            ts = us_ref[s, rows, :]
            out_ref[1, 0, s] += gr * tc + gi * ts
            out_ref[1, 1, s] += gr * ts - gi * tc
        return carry

    lax.fori_loop(0, re_ref.shape[1] // 8, body, 0)


def spectrum(both_col, turn_cos, turn_sin):
    pixels = both_col.shape[1]
    half = SC // 2
    block = 128
    steps = half // block
    lower = lambda j: (0, 0, j)
    upper = lambda j: (0, 0, j + steps)
    spec = pl.pallas_call(
        spectrum_kernel,
        grid=(steps,),
        in_specs=[
            pl.BlockSpec((SR, pixels, block), lower),
            pl.BlockSpec((SR, pixels, block), upper),
            pl.BlockSpec((SR, pixels, block), lower),
            pl.BlockSpec((SR, pixels, block), lower),
            pl.BlockSpec((SR, pixels, block), upper),
            pl.BlockSpec((SR, pixels, block), upper),
        ],
        out_specs=pl.BlockSpec((2, 2, SR, 8, block), lambda j: (0, 0, 0, 0, j)),
        out_shape=jax.ShapeDtypeStruct((2, 2, SR, 8, half), jnp.float32),
    )(both_col, both_col, turn_cos, turn_sin, turn_cos, turn_sin)
    return jnp.sum(spec, axis=3)


def local(frames, offsets, bright, aberration):
    scan_size = lax.axis_size("scan")
    det_size = lax.axis_size("det")
    rows_dev, tile, detector = frames.shape
    owned = offsets.shape[0]
    groups = detector // owned
    owner = lax.axis_index("scan") * det_size + lax.axis_index("det")
    blocks = jnp.transpose(frames.reshape(rows_dev * tile, groups, owned), (1, 0, 2))
    arrived = lax.all_to_all(blocks, ("scan", "det"), split_axis=0, concat_axis=0, tiled=True)
    images = arrived.reshape(scan_size, det_size, rows_dev, tile, owned)
    full_cols = jnp.arange(SC, dtype=jnp.int32)
    col_sin, col_cos = sincos_of_steps(jnp.mod(full_cols[:, None] * full_cols[None, :], SC), SC)
    col_cos = col_cos.astype(jnp.bfloat16)
    col_sin = col_sin.astype(jnp.bfloat16)
    half = SC // 2
    nyquist = jnp.zeros((SC, 128), jnp.bfloat16).at[:, 0].set(col_cos[:, half])
    table = jnp.concatenate([col_cos[:, :half], -col_sin[:, :half], nyquist], axis=1)
    both_col = jnp.einsum(
        "abrcp,acq->brpq",
        images,
        table.reshape(scan_size, tile, table.shape[1]),
        preferred_element_type=jnp.float32,
    ).reshape(SR, owned, table.shape[1])
    full_rows = jnp.arange(SR, dtype=jnp.int32)
    angles_by_row = phase_angles(full_rows, full_rows, SR)
    row_cos = jnp.cos(angles_by_row)
    row_sin = jnp.sin(angles_by_row)
    pixel_index = owner * owned + jnp.arange(owned, dtype=jnp.int32)
    steps = jnp.arange(half, dtype=jnp.int32)
    col_index = jnp.concatenate([steps, jnp.mod(SC - steps, SC), jnp.full((1,), half, jnp.int32)])
    row_part, col_part, moved_rows, moved_cols, spherical = phase_parts(
        pixel_index, offsets, aberration, col_index
    )
    moved_sq = moved_rows[:, :, None] + moved_cols.T[None, :, :]
    phase = row_part[:, :, None] + col_part.T[None, :, :] - spherical * (moved_sq * moved_sq)
    weights = bright.astype(jnp.float32)
    keep = (jnp.arange(SC + 1) != half).astype(jnp.float32)
    turn_sin, turn_cos = sincos(phase)
    turn_cos, turn_sin = lax.optimization_barrier(
        (
            turn_cos * weights[None, :, None] * keep[None, None, :],
            turn_sin * weights[None, :, None] * keep[None, None, :],
        )
    )
    parts = spectrum(both_col, turn_cos, turn_sin)
    nyquist_col = both_col[:, :, SC]
    nyquist_real = jnp.dot(row_cos.T, nyquist_col, precision=EXACT_PRECISION)
    nyquist_imag = -jnp.dot(row_sin.T, nyquist_col, precision=EXACT_PRECISION)
    last_cos = turn_cos[:, :, SC]
    last_sin = turn_sin[:, :, SC]
    nyquist_spec_real = jnp.sum(nyquist_real * last_cos - nyquist_imag * last_sin, axis=1)
    nyquist_spec_imag = jnp.sum(nyquist_real * last_sin + nyquist_imag * last_cos, axis=1)
    spec_real = jnp.concatenate(
        [parts[0, 0], nyquist_spec_real[:, None], parts[1, 0, :, :0:-1]], axis=1
    )
    spec_imag = jnp.concatenate(
        [parts[0, 1], nyquist_spec_imag[:, None], parts[1, 1, :, :0:-1]], axis=1
    )
    row_cos_t = row_cos.T
    row_sin_t = row_sin.T
    rows_real = jnp.dot(row_cos_t, spec_real, precision=EXACT_PRECISION) - jnp.dot(
        row_sin_t, spec_imag, precision=EXACT_PRECISION
    )
    rows_imag = jnp.dot(row_sin_t, spec_real, precision=EXACT_PRECISION) + jnp.dot(
        row_cos_t, spec_imag, precision=EXACT_PRECISION
    )
    packed = jnp.concatenate(
        [rows_real, rows_imag, jnp.broadcast_to(jnp.sum(weights), (SR, 128))], axis=1
    )
    width = tile + 2 * HALO
    columns = jnp.mod(
        lax.axis_index("scan") * tile - HALO + jnp.arange(width, dtype=jnp.int32), SC
    )
    col_angles = phase_angles(jnp.arange(SC, dtype=jnp.int32), columns, SC)
    cos_cols, sin_cols = lax.optimization_barrier((jnp.cos(col_angles), jnp.sin(col_angles)))
    gathered = lax.all_to_all(packed, "det", 0, 0, tiled=True)
    own = pairwise_sum([gathered[i] for i in range(det_size)])
    spread = jnp.broadcast_to(own, (scan_size,) + own.shape)
    gathered = lax.all_to_all(spread, "scan", 0, 0, tiled=True)
    total = pairwise_sum([gathered[i] for i in range(scan_size)])
    line_real = total[:SC]
    line_imag = total[SC : 2 * SC]
    bright_sum = total[2 * SC]
    picture = jnp.dot(line_real, cos_cols, precision=EXACT_PRECISION) - jnp.dot(
        line_imag, sin_cols, precision=EXACT_PRECISION
    )
    return (
        (picture * (1.0 / (SR * SC)) / jnp.sqrt(bright_sum) * window_weights(width))
        .reshape(rows_dev, 1, width)
    )


def solution(mesh):
    placed = (P("det", "scan", None), P(("scan", "det"), None), P(("scan", "det")), P())
    return jax.shard_map(
        local, mesh=mesh, in_specs=placed, out_specs=P("det", "scan", None), check_vma=False
    )
```

```python
import math

import jax
import jax.numpy as jnp
from jax import lax
from jax.sharding import PartitionSpec as P
from jax.experimental import pallas as pl
from jax.experimental.pallas import tpu as pltpu

SR = 16
SC = 1024
DROWS = 128
DCOLS = 128
HALO = 16


TWO_PI = 2.0 * math.pi
EXACT_PRECISION = lax.Precision.HIGHEST


def phase_angles(first, second_operand, modulus):
    product = jnp.mod(first[:, None] * second_operand[None, :], modulus)
    return TWO_PI / modulus * product.astype(jnp.float32)


def signed_frequency(length):
    position = jnp.arange(length, dtype=jnp.int32)
    folded = jnp.where(position < length // 2, position, position - length)
    return 2.0 * folded.astype(jnp.float32) / length


def pixel_phase(pixel_index, shifts, aberration):
    freq_rows = signed_frequency(SR)[:, None, None]
    freq_cols = signed_frequency(SC)[None, :, None]
    half_rows = DROWS // 2
    half_cols = DCOLS // 2
    tilt_x = ((pixel_index // DCOLS - half_rows).astype(jnp.float32) / half_rows)[None, None, :]
    tilt_y = ((pixel_index % DCOLS - half_cols).astype(jnp.float32) / half_cols)[None, None, :]
    ramp_rows = jnp.mod(jnp.arange(SR, dtype=jnp.int32)[:, None] * shifts[:, 0][None, :], SR)
    ramp_cols = jnp.mod(jnp.arange(SC, dtype=jnp.int32)[:, None] * shifts[:, 1][None, :], SC)
    shift_phase = (
        TWO_PI / SR * ramp_rows.astype(jnp.float32)[:, None, :]
        + TWO_PI / SC * ramp_cols.astype(jnp.float32)[None, :, :]
    )
    tilt_sq = tilt_x * tilt_x + tilt_y * tilt_y
    tilt_dot = tilt_x * freq_rows + tilt_y * freq_cols
    moved_x = freq_rows + tilt_x
    moved_y = freq_cols + tilt_y
    moved_sq = moved_x * moved_x + moved_y * moved_y
    lens_phase = math.pi * (
        aberration[0] * (freq_rows * freq_rows + freq_cols * freq_cols)
        + aberration[1] * (moved_sq * moved_sq - tilt_sq * tilt_sq - 4.0 * tilt_sq * tilt_dot)
    )
    return shift_phase - lens_phase


def window_weights(width):
    position = jnp.arange(width, dtype=jnp.int32)
    nearest = jnp.minimum(position, width - 1 - position)
    ramped = 0.3 + 0.35 * (
        1.0 - jnp.cos(math.pi * (nearest.astype(jnp.float32) + 0.5) / (2 * HALO))
    )
    return jnp.where(nearest < 2 * HALO, ramped, jnp.float32(1.0))


def inverse_transform(spec_real, spec_imag, columns, rows):
    real_piece = jnp.dot(spec_real, cos_cols, precision=EXACT_PRECISION) - jnp.dot(
        spec_imag, sin_cols, precision=EXACT_PRECISION
    )
    imaginary_piece = jnp.dot(spec_real, sin_cols, precision=EXACT_PRECISION) + jnp.dot(
        spec_imag, cos_cols, precision=EXACT_PRECISION
    )
    angles_by_row = phase_angles(jnp.arange(SR, dtype=jnp.int32), rows, SR)
    row_cosines = jnp.cos(angles_by_row)
    row_sines = jnp.sin(angles_by_row)
    return jnp.dot(row_cosines.T, real_piece, precision=EXACT_PRECISION) - jnp.dot(
        row_sines.T, imaginary_piece, precision=EXACT_PRECISION
    )


def sincos_reduced(rest, quadrant):
    square = rest * rest
    sine = rest + rest * square * (
        -1.6666654611e-1 + square * (8.3321608736e-3 + square * -1.9515295891e-4)
    )
    cosine = 1.0 - 0.5 * square + square * square * (
        4.166664568298827e-2 + square * (-1.388731625493765e-3 + square * 2.443315711809948e-5)
    )
    swap = (quadrant & 1) == 1
    sin_out = jnp.where(swap, cosine, sine)
    cos_out = jnp.where(swap, sine, cosine)
    sin_out = jnp.where(quadrant >= 2, -sin_out, sin_out)
    cos_out = jnp.where((quadrant == 1) | (quadrant == 2), -cos_out, cos_out)
    return sin_out, cos_out


def sincos(angle):
    turns = jnp.round(angle * (2.0 / math.pi))
    quadrant = turns.astype(jnp.int32) & 3
    rest = angle - turns * 1.5703125
    rest = rest - turns * 4.837512969970703125e-4
    rest = rest - turns * 7.54978995489188216e-8
    return sincos_reduced(rest, quadrant)


def sincos_of_steps(steps, modulus):
    quarter = modulus // 4
    turns = (steps + quarter // 2) // quarter
    rest = (steps - turns * quarter).astype(jnp.float32) * (TWO_PI / modulus)
    return sincos_reduced(rest, turns & 3)


def pairwise_sum(values):
    while len(values) > 1:
        values = [
            values[e] + values[e + 1] if e + 1 < len(values) else values[e]
            for e in range(0, len(values), 2)
        ]
    return values[0]


def phase_parts(pixel_index, shifts, aberration, col_index):
    freq_rows = signed_frequency(SR)[:, None]
    freq_cols = (2.0 * jnp.where(col_index < SC // 2, col_index, col_index - SC).astype(jnp.float32) / SC)[:, None]
    half_rows = DROWS // 2
    half_cols = DCOLS // 2
    tilt_x = ((pixel_index // DCOLS - half_rows).astype(jnp.float32) / half_rows)[None, :]
    tilt_y = ((pixel_index % DCOLS - half_cols).astype(jnp.float32) / half_cols)[None, :]
    ramp_rows = jnp.mod(jnp.arange(SR, dtype=jnp.int32)[:, None] * shifts[:, 0][None, :], SR)
    ramp_cols = jnp.mod(col_index[:, None] * shifts[:, 1][None, :], SC)
    tilt_sq = tilt_x * tilt_x + tilt_y * tilt_y
    defocus = math.pi * aberration[0]
    spherical = math.pi * aberration[1]
    row_part = (
        TWO_PI / SR * ramp_rows.astype(jnp.float32)
        - defocus * freq_rows * freq_rows
        + spherical * (tilt_sq * tilt_sq + 4.0 * tilt_sq * tilt_x * freq_rows)
    )
    col_part = (
        TWO_PI / SC * ramp_cols.astype(jnp.float32)
        - defocus * freq_cols * freq_cols
        + spherical * (4.0 * tilt_sq * tilt_y * freq_cols)
    )
    moved_rows = (freq_rows + tilt_x) * (freq_rows + tilt_x)
    moved_cols = (freq_cols + tilt_y) * (freq_cols + tilt_y)
    return row_part, col_part, moved_rows, moved_cols, spherical


def four_point(points):
    (ar, ai), (br, bi), (cr, ci), (dr, di) = points
    s02r = ar + cr
    s02i = ai + ci
    d02r = ar - cr
    d02i = ai - ci
    s13r = br + dr
    s13i = bi + di
    d13r = br - dr
    d13i = bi - di
    return [
        (s02r + s13r, s02i + s13i),
        (d02r + d13i, d02i - d13r),
        (s02r - s13r, s02i - s13i),
        (d02r - d13i, d02i + d13r),
    ]


def fft16(points):
    twisted = {}
    for b in range(4):
        column = four_point([points[4 * a + b] for a in range(4)])
        for s1, (gr, gi) in enumerate(column):
            k = b * s1
            if k == 0:
                twisted[b, s1] = (gr, gi)
            elif k == 4:
                twisted[b, s1] = (gi, -gr)
            else:
                c = math.cos(TWO_PI * k / 16)
                d = math.sin(TWO_PI * k / 16)
                twisted[b, s1] = (gr * c + gi * d, gi * c - gr * d)
    out = [None] * 16
    for s1 in range(4):
        row = four_point([twisted[b, s1] for b in range(4)])
        for s2 in range(4):
            out[s1 + 4 * s2] = row[s2]
    return out


def spectrum_kernel(re_ref, im_ref, lc_ref, ls_ref, uc_ref, us_ref, out_ref, acc_ref):
    acc_ref[...] = jnp.zeros(acc_ref.shape, acc_ref.dtype)

    def body(i, carry):
        rows = pl.ds(pl.multiple_of(i * 8, 8), 8)
        full = fft16([(re_ref[r, rows, :], im_ref[r, rows, :]) for r in range(SR)])
        for s in range(SR):
            fr, fi = full[s]
            tc = lc_ref[s, rows, :]
            ts = ls_ref[s, rows, :]
            acc_ref[0, 0, s] += fr * tc - fi * ts
            acc_ref[0, 1, s] += fr * ts + fi * tc
            gr, gi = full[(SR - s) % SR]
            tc = uc_ref[s, rows, :]
            ts = us_ref[s, rows, :]
            acc_ref[1, 0, s] += gr * tc + gi * ts
            acc_ref[1, 1, s] += gr * ts - gi * tc
        return carry

    lax.fori_loop(0, re_ref.shape[1] // 8, body, 0)
    for a in range(2):
        for b in range(2):
            out_ref[a, b] = jnp.sum(acc_ref[a, b], axis=1)


def spectrum(both_col, turn_cos, turn_sin):
    pixels = both_col.shape[1]
    half = SC // 2
    block = 128
    steps = half // block
    lower = lambda j: (0, 0, j)
    upper = lambda j: (0, 0, j + steps)
    spec = pl.pallas_call(
        spectrum_kernel,
        grid=(steps,),
        in_specs=[
            pl.BlockSpec((SR, pixels, block), lower),
            pl.BlockSpec((SR, pixels, block), upper),
            pl.BlockSpec((SR, pixels, block), lower),
            pl.BlockSpec((SR, pixels, block), lower),
            pl.BlockSpec((SR, pixels, block), upper),
            pl.BlockSpec((SR, pixels, block), upper),
        ],
        out_specs=pl.BlockSpec((2, 2, SR, block), lambda j: (0, 0, 0, j)),
        out_shape=jax.ShapeDtypeStruct((2, 2, SR, half), jnp.float32),
        scratch_shapes=[pltpu.VMEM((2, 2, SR, 8, block), jnp.float32)],
    )(both_col, both_col, turn_cos, turn_sin, turn_cos, turn_sin)
    return spec


def local(frames, offsets, bright, aberration):
    scan_size = lax.axis_size("scan")
    det_size = lax.axis_size("det")
    rows_dev, tile, detector = frames.shape
    owned = offsets.shape[0]
    groups = detector // owned
    owner = lax.axis_index("scan") * det_size + lax.axis_index("det")
    blocks = jnp.transpose(frames.reshape(rows_dev * tile, groups, owned), (1, 0, 2))
    arrived = lax.all_to_all(blocks, ("scan", "det"), split_axis=0, concat_axis=0, tiled=True)
    images = arrived.reshape(scan_size, det_size, rows_dev, tile, owned)
    half = SC // 2
    full_cols = jnp.arange(SC, dtype=jnp.int32)
    col_sin, col_cos = sincos_of_steps(
        jnp.mod(full_cols[:, None] * full_cols[None, :half], SC), SC
    )
    alternating = jnp.where(full_cols % 2 == 0, 1.0, -1.0)
    nyquist = jnp.where(jnp.arange(128)[None, :] == 0, alternating[:, None], 0.0)
    table = jnp.concatenate([col_cos, -col_sin, nyquist], axis=1).astype(jnp.bfloat16)
    both_col = jnp.einsum(
        "abrcp,acq->brpq",
        images,
        table.reshape(scan_size, tile, table.shape[1]),
        preferred_element_type=jnp.float32,
    ).reshape(SR, owned, table.shape[1])
    full_rows = jnp.arange(SR, dtype=jnp.int32)
    angles_by_row = phase_angles(full_rows, full_rows, SR)
    row_cos = jnp.cos(angles_by_row)
    row_sin = jnp.sin(angles_by_row)
    pixel_index = owner * owned + jnp.arange(owned, dtype=jnp.int32)
    steps = jnp.arange(half, dtype=jnp.int32)
    col_index = jnp.concatenate([steps, jnp.mod(SC - steps, SC), jnp.full((1,), half, jnp.int32)])
    row_part, col_part, moved_rows, moved_cols, spherical = phase_parts(
        pixel_index, offsets, aberration, col_index
    )
    moved_sq = moved_rows[:, :, None] + moved_cols.T[None, :, :]
    phase = row_part[:, :, None] + col_part.T[None, :, :] - spherical * (moved_sq * moved_sq)
    weights = bright.astype(jnp.float32)
    keep = (jnp.arange(SC + 1) != half).astype(jnp.float32)
    turn_sin, turn_cos = sincos(phase)
    turn_cos, turn_sin = lax.optimization_barrier(
        (
            turn_cos * weights[None, :, None] * keep[None, None, :],
            turn_sin * weights[None, :, None] * keep[None, None, :],
        )
    )
    parts = spectrum(both_col, turn_cos, turn_sin)
    nyquist_col = both_col[:, :, SC]
    nyquist_real = jnp.dot(row_cos.T, nyquist_col, precision=EXACT_PRECISION)
    nyquist_imag = -jnp.dot(row_sin.T, nyquist_col, precision=EXACT_PRECISION)
    last_cos = turn_cos[:, :, SC]
    last_sin = turn_sin[:, :, SC]
    nyquist_spec_real = jnp.sum(nyquist_real * last_cos - nyquist_imag * last_sin, axis=1)
    nyquist_spec_imag = jnp.sum(nyquist_real * last_sin + nyquist_imag * last_cos, axis=1)
    spec_real = jnp.concatenate(
        [parts[0, 0], nyquist_spec_real[:, None], parts[1, 0, :, :0:-1]], axis=1
    )
    spec_imag = jnp.concatenate(
        [parts[0, 1], nyquist_spec_imag[:, None], parts[1, 1, :, :0:-1]], axis=1
    )
    row_cos_t = row_cos.T
    row_sin_t = row_sin.T
    rows_real = jnp.dot(row_cos_t, spec_real, precision=EXACT_PRECISION) - jnp.dot(
        row_sin_t, spec_imag, precision=EXACT_PRECISION
    )
    rows_imag = jnp.dot(row_sin_t, spec_real, precision=EXACT_PRECISION) + jnp.dot(
        row_cos_t, spec_imag, precision=EXACT_PRECISION
    )
    packed = jnp.concatenate(
        [rows_real, rows_imag, jnp.broadcast_to(jnp.sum(weights), (SR, 128))], axis=1
    )
    width = tile + 2 * HALO
    columns = jnp.mod(
        lax.axis_index("scan") * tile - HALO + jnp.arange(width, dtype=jnp.int32), SC
    )
    col_angles = phase_angles(jnp.arange(SC, dtype=jnp.int32), columns, SC)
    cos_cols, sin_cols = lax.optimization_barrier((jnp.cos(col_angles), jnp.sin(col_angles)))
    gathered = lax.all_to_all(packed, "det", 0, 0, tiled=True)
    own = pairwise_sum([gathered[i] for i in range(det_size)])
    spread = jnp.broadcast_to(own, (scan_size,) + own.shape)
    gathered = lax.all_to_all(spread, "scan", 0, 0, tiled=True)
    total = pairwise_sum([gathered[i] for i in range(scan_size)])
    line_real = total[:SC]
    line_imag = total[SC : 2 * SC]
    bright_sum = total[2 * SC]
    picture = jnp.dot(line_real, cos_cols, precision=EXACT_PRECISION) - jnp.dot(
        line_imag, sin_cols, precision=EXACT_PRECISION
    )
    return (
        (picture * (1.0 / (SR * SC)) / jnp.sqrt(bright_sum) * window_weights(width))
        .reshape(rows_dev, 1, width)
    )


def solution(mesh):
    placed = (P("det", "scan", None), P(("scan", "det"), None), P(("scan", "det")), P())
    return jax.shard_map(
        local, mesh=mesh, in_specs=placed, out_specs=P("det", "scan", None), check_vma=False
    )
```

```python
import math

import jax
import jax.numpy as jnp
from jax import lax
from jax.sharding import PartitionSpec as P
from jax.experimental import pallas as pl
from jax.experimental.pallas import tpu as pltpu

SR = 16
SC = 1024
DROWS = 128
DCOLS = 128
HALO = 16


TWO_PI = 2.0 * math.pi
EXACT_PRECISION = lax.Precision.HIGHEST


def phase_angles(first, second_operand, modulus):
    product = jnp.mod(first[:, None] * second_operand[None, :], modulus)
    return TWO_PI / modulus * product.astype(jnp.float32)


def signed_frequency(length):
    position = jnp.arange(length, dtype=jnp.int32)
    folded = jnp.where(position < length // 2, position, position - length)
    return 2.0 * folded.astype(jnp.float32) / length


def pixel_phase(pixel_index, shifts, aberration):
    freq_rows = signed_frequency(SR)[:, None, None]
    freq_cols = signed_frequency(SC)[None, :, None]
    half_rows = DROWS // 2
    half_cols = DCOLS // 2
    tilt_x = ((pixel_index // DCOLS - half_rows).astype(jnp.float32) / half_rows)[None, None, :]
    tilt_y = ((pixel_index % DCOLS - half_cols).astype(jnp.float32) / half_cols)[None, None, :]
    ramp_rows = jnp.mod(jnp.arange(SR, dtype=jnp.int32)[:, None] * shifts[:, 0][None, :], SR)
    ramp_cols = jnp.mod(jnp.arange(SC, dtype=jnp.int32)[:, None] * shifts[:, 1][None, :], SC)
    shift_phase = (
        TWO_PI / SR * ramp_rows.astype(jnp.float32)[:, None, :]
        + TWO_PI / SC * ramp_cols.astype(jnp.float32)[None, :, :]
    )
    tilt_sq = tilt_x * tilt_x + tilt_y * tilt_y
    tilt_dot = tilt_x * freq_rows + tilt_y * freq_cols
    moved_x = freq_rows + tilt_x
    moved_y = freq_cols + tilt_y
    moved_sq = moved_x * moved_x + moved_y * moved_y
    lens_phase = math.pi * (
        aberration[0] * (freq_rows * freq_rows + freq_cols * freq_cols)
        + aberration[1] * (moved_sq * moved_sq - tilt_sq * tilt_sq - 4.0 * tilt_sq * tilt_dot)
    )
    return shift_phase - lens_phase


def window_weights(width):
    position = jnp.arange(width, dtype=jnp.int32)
    nearest = jnp.minimum(position, width - 1 - position)
    ramped = 0.3 + 0.35 * (
        1.0 - jnp.cos(math.pi * (nearest.astype(jnp.float32) + 0.5) / (2 * HALO))
    )
    return jnp.where(nearest < 2 * HALO, ramped, jnp.float32(1.0))


def inverse_transform(spec_real, spec_imag, columns, rows):
    real_piece = jnp.dot(spec_real, cos_cols, precision=EXACT_PRECISION) - jnp.dot(
        spec_imag, sin_cols, precision=EXACT_PRECISION
    )
    imaginary_piece = jnp.dot(spec_real, sin_cols, precision=EXACT_PRECISION) + jnp.dot(
        spec_imag, cos_cols, precision=EXACT_PRECISION
    )
    angles_by_row = phase_angles(jnp.arange(SR, dtype=jnp.int32), rows, SR)
    row_cosines = jnp.cos(angles_by_row)
    row_sines = jnp.sin(angles_by_row)
    return jnp.dot(row_cosines.T, real_piece, precision=EXACT_PRECISION) - jnp.dot(
        row_sines.T, imaginary_piece, precision=EXACT_PRECISION
    )


def sincos_reduced(rest, quadrant):
    square = rest * rest
    sine = rest + rest * square * (
        -1.6666654611e-1 + square * (8.3321608736e-3 + square * -1.9515295891e-4)
    )
    cosine = 1.0 - 0.5 * square + square * square * (
        4.166664568298827e-2 + square * (-1.388731625493765e-3 + square * 2.443315711809948e-5)
    )
    swap = (quadrant & 1) == 1
    sin_out = jnp.where(swap, cosine, sine)
    cos_out = jnp.where(swap, sine, cosine)
    sin_out = jnp.where(quadrant >= 2, -sin_out, sin_out)
    cos_out = jnp.where((quadrant == 1) | (quadrant == 2), -cos_out, cos_out)
    return sin_out, cos_out


def sincos(angle):
    turns = jnp.round(angle * (2.0 / math.pi))
    quadrant = turns.astype(jnp.int32) & 3
    rest = angle - turns * 1.5703125
    rest = rest - turns * 4.837512969970703125e-4
    rest = rest - turns * 7.54978995489188216e-8
    return sincos_reduced(rest, quadrant)


def sincos_of_steps(steps, modulus):
    quarter = modulus // 4
    turns = (steps + quarter // 2) // quarter
    rest = (steps - turns * quarter).astype(jnp.float32) * (TWO_PI / modulus)
    return sincos_reduced(rest, turns & 3)


def pairwise_sum(values):
    while len(values) > 1:
        values = [
            values[e] + values[e + 1] if e + 1 < len(values) else values[e]
            for e in range(0, len(values), 2)
        ]
    return values[0]


def phase_parts(pixel_index, shifts, aberration, col_index):
    freq_rows = signed_frequency(SR)[:, None]
    freq_cols = (2.0 * jnp.where(col_index < SC // 2, col_index, col_index - SC).astype(jnp.float32) / SC)[:, None]
    half_rows = DROWS // 2
    half_cols = DCOLS // 2
    tilt_x = ((pixel_index // DCOLS - half_rows).astype(jnp.float32) / half_rows)[None, :]
    tilt_y = ((pixel_index % DCOLS - half_cols).astype(jnp.float32) / half_cols)[None, :]
    ramp_rows = jnp.mod(jnp.arange(SR, dtype=jnp.int32)[:, None] * shifts[:, 0][None, :], SR)
    ramp_cols = jnp.mod(col_index[:, None] * shifts[:, 1][None, :], SC)
    tilt_sq = tilt_x * tilt_x + tilt_y * tilt_y
    defocus = math.pi * aberration[0]
    spherical = math.pi * aberration[1]
    row_part = (
        TWO_PI / SR * ramp_rows.astype(jnp.float32)
        - defocus * freq_rows * freq_rows
        + spherical * (tilt_sq * tilt_sq + 4.0 * tilt_sq * tilt_x * freq_rows)
    )
    col_part = (
        TWO_PI / SC * ramp_cols.astype(jnp.float32)
        - defocus * freq_cols * freq_cols
        + spherical * (4.0 * tilt_sq * tilt_y * freq_cols)
    )
    moved_rows = (freq_rows + tilt_x) * (freq_rows + tilt_x)
    moved_cols = (freq_cols + tilt_y) * (freq_cols + tilt_y)
    return row_part, col_part, moved_rows, moved_cols, spherical


def four_point(points):
    (ar, ai), (br, bi), (cr, ci), (dr, di) = points
    s02r = ar + cr
    s02i = ai + ci
    d02r = ar - cr
    d02i = ai - ci
    s13r = br + dr
    s13i = bi + di
    d13r = br - dr
    d13i = bi - di
    return [
        (s02r + s13r, s02i + s13i),
        (d02r + d13i, d02i - d13r),
        (s02r - s13r, s02i - s13i),
        (d02r - d13i, d02i + d13r),
    ]


def fft16(points):
    twisted = {}
    for b in range(4):
        column = four_point([points[4 * a + b] for a in range(4)])
        for s1, (gr, gi) in enumerate(column):
            k = b * s1
            if k == 0:
                twisted[b, s1] = (gr, gi)
            elif k == 4:
                twisted[b, s1] = (gi, -gr)
            else:
                c = math.cos(TWO_PI * k / 16)
                d = math.sin(TWO_PI * k / 16)
                twisted[b, s1] = (gr * c + gi * d, gi * c - gr * d)
    out = [None] * 16
    for s1 in range(4):
        row = four_point([twisted[b, s1] for b in range(4)])
        for s2 in range(4):
            out[s1 + 4 * s2] = row[s2]
    return out


def spectrum_kernel(re_ref, im_ref, lc_ref, ls_ref, uc_ref, us_ref, out_ref, acc_ref):
    acc_ref[...] = jnp.zeros(acc_ref.shape, acc_ref.dtype)

    def body(i, carry):
        rows = pl.ds(pl.multiple_of(i * 8, 8), 8)
        full = fft16([(re_ref[r, rows, :], im_ref[r, rows, :]) for r in range(SR)])
        for s in range(SR):
            fr, fi = full[s]
            tc = lc_ref[s, rows, :]
            ts = ls_ref[s, rows, :]
            acc_ref[0, 0, s] += fr * tc - fi * ts
            acc_ref[0, 1, s] += fr * ts + fi * tc
            gr, gi = full[(SR - s) % SR]
            tc = uc_ref[s, rows, :]
            ts = us_ref[s, rows, :]
            acc_ref[1, 0, s] += gr * tc + gi * ts
            acc_ref[1, 1, s] += gr * ts - gi * tc
        return carry

    lax.fori_loop(0, re_ref.shape[1] // 8, body, 0)
    for a in range(2):
        for b in range(2):
            out_ref[a, b] = jnp.sum(acc_ref[a, b], axis=1)


def spectrum(both_col, turn_cos, turn_sin):
    pixels = both_col.shape[1]
    half = SC // 2
    block = 128
    steps = half // block
    lower = lambda j: (0, 0, j)
    upper = lambda j: (0, 0, j + steps)
    spec = pl.pallas_call(
        spectrum_kernel,
        grid=(steps,),
        in_specs=[
            pl.BlockSpec((SR, pixels, block), lower),
            pl.BlockSpec((SR, pixels, block), upper),
            pl.BlockSpec((SR, pixels, block), lower),
            pl.BlockSpec((SR, pixels, block), lower),
            pl.BlockSpec((SR, pixels, block), upper),
            pl.BlockSpec((SR, pixels, block), upper),
        ],
        out_specs=pl.BlockSpec((2, 2, SR, block), lambda j: (0, 0, 0, j)),
        out_shape=jax.ShapeDtypeStruct((2, 2, SR, half), jnp.float32),
        scratch_shapes=[pltpu.VMEM((2, 2, SR, 8, block), jnp.float32)],
    )(both_col, both_col, turn_cos, turn_sin, turn_cos, turn_sin)
    return spec


def local(frames, offsets, bright, aberration):
    scan_size = lax.axis_size("scan")
    det_size = lax.axis_size("det")
    rows_dev, tile, detector = frames.shape
    owned = offsets.shape[0]
    groups = detector // owned
    owner = lax.axis_index("scan") * det_size + lax.axis_index("det")
    blocks = jnp.transpose(frames.reshape(rows_dev * tile, groups, owned), (1, 0, 2))
    arrived = lax.all_to_all(blocks, ("scan", "det"), split_axis=0, concat_axis=0, tiled=True)
    images = arrived.reshape(scan_size, det_size, rows_dev, tile, owned)
    half = SC // 2
    full_cols = jnp.arange(SC, dtype=jnp.int32)
    col_sin, col_cos = sincos_of_steps(
        jnp.mod(full_cols[:, None] * full_cols[None, :half], SC), SC
    )
    alternating = jnp.where(full_cols % 2 == 0, 1.0, -1.0)
    nyquist = jnp.where(jnp.arange(128)[None, :] == 0, alternating[:, None], 0.0)
    table = jnp.concatenate([col_cos, -col_sin, nyquist], axis=1).astype(jnp.bfloat16)
    both_col = jnp.einsum(
        "abrcp,acq->brpq",
        images,
        table.reshape(scan_size, tile, table.shape[1]),
        preferred_element_type=jnp.float32,
    ).reshape(SR, owned, table.shape[1])
    full_rows = jnp.arange(SR, dtype=jnp.int32)
    angles_by_row = phase_angles(full_rows, full_rows, SR)
    row_cos = jnp.cos(angles_by_row)
    row_sin = jnp.sin(angles_by_row)
    pixel_index = owner * owned + jnp.arange(owned, dtype=jnp.int32)
    steps = jnp.arange(half, dtype=jnp.int32)
    col_index = jnp.concatenate([steps, jnp.mod(SC - steps, SC), jnp.full((1,), half, jnp.int32)])
    row_part, col_part, moved_rows, moved_cols, spherical = phase_parts(
        pixel_index, offsets, aberration, col_index
    )
    moved_sq = moved_rows[:, :, None] + moved_cols.T[None, :, :]
    phase = row_part[:, :, None] + col_part.T[None, :, :] - spherical * (moved_sq * moved_sq)
    weights = bright.astype(jnp.float32)
    keep = (jnp.arange(SC + 1) != half).astype(jnp.float32)
    turn_sin, turn_cos = sincos(phase)
    turn_cos, turn_sin = lax.optimization_barrier(
        (
            turn_cos * weights[None, :, None] * keep[None, None, :],
            turn_sin * weights[None, :, None] * keep[None, None, :],
        )
    )
    parts = spectrum(both_col, turn_cos, turn_sin)
    nyquist_col = both_col[:, :, SC]
    nyquist_real = jnp.dot(row_cos.T, nyquist_col, precision=EXACT_PRECISION)
    nyquist_imag = -jnp.dot(row_sin.T, nyquist_col, precision=EXACT_PRECISION)
    last_cos = turn_cos[:, :, SC]
    last_sin = turn_sin[:, :, SC]
    nyquist_spec_real = jnp.sum(nyquist_real * last_cos - nyquist_imag * last_sin, axis=1)
    nyquist_spec_imag = jnp.sum(nyquist_real * last_sin + nyquist_imag * last_cos, axis=1)
    spec_real = jnp.concatenate([parts[0, 0], parts[1, 0], nyquist_spec_real[:, None]], axis=1)
    spec_imag = jnp.concatenate([parts[0, 1], parts[1, 1], nyquist_spec_imag[:, None]], axis=1)
    row_cos_t = row_cos.T
    row_sin_t = row_sin.T
    rows_real = jnp.dot(row_cos_t, spec_real, precision=EXACT_PRECISION) - jnp.dot(
        row_sin_t, spec_imag, precision=EXACT_PRECISION
    )
    rows_imag = jnp.dot(row_sin_t, spec_real, precision=EXACT_PRECISION) + jnp.dot(
        row_cos_t, spec_imag, precision=EXACT_PRECISION
    )
    lanes = 2 * (SC + 1)
    packed = jnp.concatenate(
        [rows_real, rows_imag, jnp.broadcast_to(jnp.sum(weights), (SR, (-lanes) % 128 or 128))],
        axis=1,
    )
    width = tile + 2 * HALO
    columns = jnp.mod(
        lax.axis_index("scan") * tile - HALO + jnp.arange(width, dtype=jnp.int32), SC
    )
    col_angles = phase_angles(col_index, columns, SC)
    cos_cols, sin_cols = lax.optimization_barrier((jnp.cos(col_angles), jnp.sin(col_angles)))
    gathered = lax.all_to_all(packed, "det", 0, 0, tiled=True)
    own = pairwise_sum([gathered[i] for i in range(det_size)])
    spread = jnp.broadcast_to(own, (scan_size,) + own.shape)
    gathered = lax.all_to_all(spread, "scan", 0, 0, tiled=True)
    total = pairwise_sum([gathered[i] for i in range(scan_size)])
    line_real = total[: SC + 1]
    line_imag = total[SC + 1 : lanes]
    bright_sum = total[lanes]
    picture = jnp.dot(line_real, cos_cols, precision=EXACT_PRECISION) - jnp.dot(
        line_imag, sin_cols, precision=EXACT_PRECISION
    )
    return (
        (picture * (1.0 / (SR * SC)) / jnp.sqrt(bright_sum) * window_weights(width))
        .reshape(rows_dev, 1, width)
    )


def solution(mesh):
    placed = (P("det", "scan", None), P(("scan", "det"), None), P(("scan", "det")), P())
    return jax.shard_map(
        local, mesh=mesh, in_specs=placed, out_specs=P("det", "scan", None), check_vma=False
    )
```

```python
import math

import jax
import jax.numpy as jnp
from jax import lax
from jax.sharding import PartitionSpec as P
from jax.experimental import pallas as pl
from jax.experimental.pallas import tpu as pltpu

SR = 16
SC = 1024
DROWS = 128
DCOLS = 128
HALO = 16


TWO_PI = 2.0 * math.pi
EXACT_PRECISION = lax.Precision.HIGHEST


def phase_angles(first, second_operand, modulus):
    product = jnp.mod(first[:, None] * second_operand[None, :], modulus)
    return TWO_PI / modulus * product.astype(jnp.float32)


def signed_frequency(length):
    position = jnp.arange(length, dtype=jnp.int32)
    folded = jnp.where(position < length // 2, position, position - length)
    return 2.0 * folded.astype(jnp.float32) / length


def pixel_phase(pixel_index, shifts, aberration):
    freq_rows = signed_frequency(SR)[:, None, None]
    freq_cols = signed_frequency(SC)[None, :, None]
    half_rows = DROWS // 2
    half_cols = DCOLS // 2
    tilt_x = ((pixel_index // DCOLS - half_rows).astype(jnp.float32) / half_rows)[None, None, :]
    tilt_y = ((pixel_index % DCOLS - half_cols).astype(jnp.float32) / half_cols)[None, None, :]
    ramp_rows = jnp.mod(jnp.arange(SR, dtype=jnp.int32)[:, None] * shifts[:, 0][None, :], SR)
    ramp_cols = jnp.mod(jnp.arange(SC, dtype=jnp.int32)[:, None] * shifts[:, 1][None, :], SC)
    shift_phase = (
        TWO_PI / SR * ramp_rows.astype(jnp.float32)[:, None, :]
        + TWO_PI / SC * ramp_cols.astype(jnp.float32)[None, :, :]
    )
    tilt_sq = tilt_x * tilt_x + tilt_y * tilt_y
    tilt_dot = tilt_x * freq_rows + tilt_y * freq_cols
    moved_x = freq_rows + tilt_x
    moved_y = freq_cols + tilt_y
    moved_sq = moved_x * moved_x + moved_y * moved_y
    lens_phase = math.pi * (
        aberration[0] * (freq_rows * freq_rows + freq_cols * freq_cols)
        + aberration[1] * (moved_sq * moved_sq - tilt_sq * tilt_sq - 4.0 * tilt_sq * tilt_dot)
    )
    return shift_phase - lens_phase


def window_weights(width):
    position = jnp.arange(width, dtype=jnp.int32)
    nearest = jnp.minimum(position, width - 1 - position)
    ramped = 0.3 + 0.35 * (
        1.0 - jnp.cos(math.pi * (nearest.astype(jnp.float32) + 0.5) / (2 * HALO))
    )
    return jnp.where(nearest < 2 * HALO, ramped, jnp.float32(1.0))


def inverse_transform(spec_real, spec_imag, columns, rows):
    real_piece = jnp.dot(spec_real, cos_cols, precision=EXACT_PRECISION) - jnp.dot(
        spec_imag, sin_cols, precision=EXACT_PRECISION
    )
    imaginary_piece = jnp.dot(spec_real, sin_cols, precision=EXACT_PRECISION) + jnp.dot(
        spec_imag, cos_cols, precision=EXACT_PRECISION
    )
    angles_by_row = phase_angles(jnp.arange(SR, dtype=jnp.int32), rows, SR)
    row_cosines = jnp.cos(angles_by_row)
    row_sines = jnp.sin(angles_by_row)
    return jnp.dot(row_cosines.T, real_piece, precision=EXACT_PRECISION) - jnp.dot(
        row_sines.T, imaginary_piece, precision=EXACT_PRECISION
    )


def sincos_reduced(rest, quadrant):
    square = rest * rest
    sine = rest + rest * square * (
        -1.6666654611e-1 + square * (8.3321608736e-3 + square * -1.9515295891e-4)
    )
    cosine = 1.0 - 0.5 * square + square * square * (
        4.166664568298827e-2 + square * (-1.388731625493765e-3 + square * 2.443315711809948e-5)
    )
    swap = (quadrant & 1) == 1
    sin_out = jnp.where(swap, cosine, sine)
    cos_out = jnp.where(swap, sine, cosine)
    sin_out = jnp.where(quadrant >= 2, -sin_out, sin_out)
    cos_out = jnp.where((quadrant == 1) | (quadrant == 2), -cos_out, cos_out)
    return sin_out, cos_out


def sincos(angle):
    turns = jnp.round(angle * (2.0 / math.pi))
    quadrant = turns.astype(jnp.int32) & 3
    rest = angle - turns * 1.5703125
    rest = rest - turns * 4.837512969970703125e-4
    rest = rest - turns * 7.54978995489188216e-8
    return sincos_reduced(rest, quadrant)


def sincos_of_steps(steps, modulus):
    quarter = modulus // 4
    turns = (steps + quarter // 2) // quarter
    rest = (steps - turns * quarter).astype(jnp.float32) * (TWO_PI / modulus)
    return sincos_reduced(rest, turns & 3)


def pairwise_sum(values):
    while len(values) > 1:
        values = [
            values[e] + values[e + 1] if e + 1 < len(values) else values[e]
            for e in range(0, len(values), 2)
        ]
    return values[0]


def phase_parts(pixel_index, shifts, aberration, col_index):
    freq_rows = signed_frequency(SR)[:, None]
    freq_cols = (2.0 * jnp.where(col_index < SC // 2, col_index, col_index - SC).astype(jnp.float32) / SC)[:, None]
    half_rows = DROWS // 2
    half_cols = DCOLS // 2
    tilt_x = ((pixel_index // DCOLS - half_rows).astype(jnp.float32) / half_rows)[None, :]
    tilt_y = ((pixel_index % DCOLS - half_cols).astype(jnp.float32) / half_cols)[None, :]
    ramp_rows = jnp.mod(jnp.arange(SR, dtype=jnp.int32)[:, None] * shifts[:, 0][None, :], SR)
    ramp_cols = jnp.mod(col_index[:, None] * shifts[:, 1][None, :], SC)
    tilt_sq = tilt_x * tilt_x + tilt_y * tilt_y
    defocus = math.pi * aberration[0]
    spherical = math.pi * aberration[1]
    row_part = (
        TWO_PI / SR * ramp_rows.astype(jnp.float32)
        - defocus * freq_rows * freq_rows
        + spherical * (tilt_sq * tilt_sq + 4.0 * tilt_sq * tilt_x * freq_rows)
    )
    col_part = (
        TWO_PI / SC * ramp_cols.astype(jnp.float32)
        - defocus * freq_cols * freq_cols
        + spherical * (4.0 * tilt_sq * tilt_y * freq_cols)
    )
    moved_rows = (freq_rows + tilt_x) * (freq_rows + tilt_x)
    moved_cols = (freq_cols + tilt_y) * (freq_cols + tilt_y)
    return row_part, col_part, moved_rows, moved_cols, spherical


def four_point(points):
    (ar, ai), (br, bi), (cr, ci), (dr, di) = points
    s02r = ar + cr
    s02i = ai + ci
    d02r = ar - cr
    d02i = ai - ci
    s13r = br + dr
    s13i = bi + di
    d13r = br - dr
    d13i = bi - di
    return [
        (s02r + s13r, s02i + s13i),
        (d02r + d13i, d02i - d13r),
        (s02r - s13r, s02i - s13i),
        (d02r - d13i, d02i + d13r),
    ]


def fft16(points):
    twisted = {}
    for b in range(4):
        column = four_point([points[4 * a + b] for a in range(4)])
        for s1, (gr, gi) in enumerate(column):
            k = b * s1
            if k == 0:
                twisted[b, s1] = (gr, gi)
            elif k == 4:
                twisted[b, s1] = (gi, -gr)
            else:
                c = math.cos(TWO_PI * k / 16)
                d = math.sin(TWO_PI * k / 16)
                twisted[b, s1] = (gr * c + gi * d, gi * c - gr * d)
    out = [None] * 16
    for s1 in range(4):
        row = four_point([twisted[b, s1] for b in range(4)])
        for s2 in range(4):
            out[s1 + 4 * s2] = row[s2]
    return out


def spectrum_kernel(y_ref, lc_ref, ls_ref, uc_ref, us_ref, out_ref, acc_ref):
    acc_ref[...] = jnp.zeros(acc_ref.shape, acc_ref.dtype)
    width = lc_ref.shape[2]
    low = pl.multiple_of(pl.program_id(0) * width, width)
    high = pl.multiple_of(pl.program_id(0) * width + SC // 2, width)

    def body(i, carry):
        rows = pl.ds(pl.multiple_of(i * 8, 8), 8)
        full = fft16(
            [(y_ref[r, rows, pl.ds(low, width)], y_ref[r, rows, pl.ds(high, width)]) for r in range(SR)]
        )
        for s in range(SR):
            fr, fi = full[s]
            tc = lc_ref[s, rows, :]
            ts = ls_ref[s, rows, :]
            acc_ref[0, 0, s] += fr * tc - fi * ts
            acc_ref[0, 1, s] += fr * ts + fi * tc
            gr, gi = full[(SR - s) % SR]
            tc = uc_ref[s, rows, :]
            ts = us_ref[s, rows, :]
            acc_ref[1, 0, s] += gr * tc + gi * ts
            acc_ref[1, 1, s] += gr * ts - gi * tc
        return carry

    lax.fori_loop(0, lc_ref.shape[1] // 8, body, 0)
    for a in range(2):
        for b in range(2):
            out_ref[a, b] = jnp.sum(acc_ref[a, b], axis=1)


def spectrum(both_col, turn_cos, turn_sin):
    pixels = both_col.shape[1]
    half = SC // 2
    block = 128
    steps = half // block
    lower = lambda j: (0, 0, j)
    upper = lambda j: (0, 0, j + steps)
    spec = pl.pallas_call(
        spectrum_kernel,
        grid=(steps,),
        in_specs=[
            pl.BlockSpec(memory_space=pltpu.VMEM),
            pl.BlockSpec((SR, pixels, block), lower),
            pl.BlockSpec((SR, pixels, block), lower),
            pl.BlockSpec((SR, pixels, block), upper),
            pl.BlockSpec((SR, pixels, block), upper),
        ],
        out_specs=pl.BlockSpec((2, 2, SR, block), lambda j: (0, 0, 0, j)),
        out_shape=jax.ShapeDtypeStruct((2, 2, SR, half), jnp.float32),
        scratch_shapes=[pltpu.VMEM((2, 2, SR, 8, block), jnp.float32)],
        compiler_params=pltpu.CompilerParams(vmem_limit_bytes=40 * 1024 * 1024),
    )(both_col, turn_cos, turn_sin, turn_cos, turn_sin)
    return spec


def local(frames, offsets, bright, aberration):
    scan_size = lax.axis_size("scan")
    det_size = lax.axis_size("det")
    rows_dev, tile, detector = frames.shape
    owned = offsets.shape[0]
    groups = detector // owned
    owner = lax.axis_index("scan") * det_size + lax.axis_index("det")
    blocks = jnp.transpose(frames.reshape(rows_dev * tile, groups, owned), (1, 0, 2))
    arrived = lax.all_to_all(blocks, ("scan", "det"), split_axis=0, concat_axis=0, tiled=True)
    images = arrived.reshape(scan_size, det_size, rows_dev, tile, owned)
    half = SC // 2
    full_cols = jnp.arange(SC, dtype=jnp.int32)
    col_sin, col_cos = sincos_of_steps(
        jnp.mod(full_cols[:, None] * full_cols[None, :half], SC), SC
    )
    alternating = jnp.where(full_cols % 2 == 0, 1.0, -1.0)
    nyquist = jnp.where(jnp.arange(128)[None, :] == 0, alternating[:, None], 0.0)
    table = jnp.concatenate([col_cos, -col_sin, nyquist], axis=1).astype(jnp.bfloat16)
    both_col = jnp.einsum(
        "abrcp,acq->brpq",
        images,
        table.reshape(scan_size, tile, table.shape[1]),
        preferred_element_type=jnp.float32,
    ).reshape(SR, owned, table.shape[1])
    full_rows = jnp.arange(SR, dtype=jnp.int32)
    angles_by_row = phase_angles(full_rows, full_rows, SR)
    row_cos = jnp.cos(angles_by_row)
    row_sin = jnp.sin(angles_by_row)
    pixel_index = owner * owned + jnp.arange(owned, dtype=jnp.int32)
    steps = jnp.arange(half, dtype=jnp.int32)
    col_index = jnp.concatenate([steps, jnp.mod(SC - steps, SC), jnp.full((1,), half, jnp.int32)])
    row_part, col_part, moved_rows, moved_cols, spherical = phase_parts(
        pixel_index, offsets, aberration, col_index
    )
    moved_sq = moved_rows[:, :, None] + moved_cols.T[None, :, :]
    phase = row_part[:, :, None] + col_part.T[None, :, :] - spherical * (moved_sq * moved_sq)
    weights = bright.astype(jnp.float32)
    keep = (jnp.arange(SC + 1) != half).astype(jnp.float32)
    turn_sin, turn_cos = sincos(phase)
    turn_cos, turn_sin = lax.optimization_barrier(
        (
            turn_cos * weights[None, :, None] * keep[None, None, :],
            turn_sin * weights[None, :, None] * keep[None, None, :],
        )
    )
    parts = spectrum(both_col, turn_cos, turn_sin)
    nyquist_col = both_col[:, :, SC]
    nyquist_real = jnp.dot(row_cos.T, nyquist_col, precision=EXACT_PRECISION)
    nyquist_imag = -jnp.dot(row_sin.T, nyquist_col, precision=EXACT_PRECISION)
    last_cos = turn_cos[:, :, SC]
    last_sin = turn_sin[:, :, SC]
    nyquist_spec_real = jnp.sum(nyquist_real * last_cos - nyquist_imag * last_sin, axis=1)
    nyquist_spec_imag = jnp.sum(nyquist_real * last_sin + nyquist_imag * last_cos, axis=1)
    spec_real = jnp.concatenate([parts[0, 0], parts[1, 0], nyquist_spec_real[:, None]], axis=1)
    spec_imag = jnp.concatenate([parts[0, 1], parts[1, 1], nyquist_spec_imag[:, None]], axis=1)
    row_cos_t = row_cos.T
    row_sin_t = row_sin.T
    rows_real = jnp.dot(row_cos_t, spec_real, precision=EXACT_PRECISION) - jnp.dot(
        row_sin_t, spec_imag, precision=EXACT_PRECISION
    )
    rows_imag = jnp.dot(row_sin_t, spec_real, precision=EXACT_PRECISION) + jnp.dot(
        row_cos_t, spec_imag, precision=EXACT_PRECISION
    )
    lanes = 2 * (SC + 1)
    packed = jnp.concatenate(
        [rows_real, rows_imag, jnp.broadcast_to(jnp.sum(weights), (SR, (-lanes) % 128 or 128))],
        axis=1,
    )
    width = tile + 2 * HALO
    columns = jnp.mod(
        lax.axis_index("scan") * tile - HALO + jnp.arange(width, dtype=jnp.int32), SC
    )
    col_angles = phase_angles(col_index, columns, SC)
    cos_cols, sin_cols = lax.optimization_barrier((jnp.cos(col_angles), jnp.sin(col_angles)))
    gathered = lax.all_to_all(packed, "det", 0, 0, tiled=True)
    own = pairwise_sum([gathered[i] for i in range(det_size)])
    spread = jnp.broadcast_to(own, (scan_size,) + own.shape)
    gathered = lax.all_to_all(spread, "scan", 0, 0, tiled=True)
    total = pairwise_sum([gathered[i] for i in range(scan_size)])
    line_real = total[: SC + 1]
    line_imag = total[SC + 1 : lanes]
    bright_sum = total[lanes]
    picture = jnp.dot(line_real, cos_cols, precision=EXACT_PRECISION) - jnp.dot(
        line_imag, sin_cols, precision=EXACT_PRECISION
    )
    return (
        (picture * (1.0 / (SR * SC)) / jnp.sqrt(bright_sum) * window_weights(width))
        .reshape(rows_dev, 1, width)
    )


def solution(mesh):
    placed = (P("det", "scan", None), P(("scan", "det"), None), P(("scan", "det")), P())
    return jax.shard_map(
        local, mesh=mesh, in_specs=placed, out_specs=P("det", "scan", None), check_vma=False
    )
```

```python
import math

import jax
import jax.numpy as jnp
from jax import lax
from jax.sharding import PartitionSpec as P
from jax.experimental import pallas as pl
from jax.experimental.pallas import tpu as pltpu

SR = 16
SC = 1024
DROWS = 128
DCOLS = 128
HALO = 16


TWO_PI = 2.0 * math.pi
EXACT_PRECISION = lax.Precision.HIGHEST


def phase_angles(first, second_operand, modulus):
    product = jnp.mod(first[:, None] * second_operand[None, :], modulus)
    return TWO_PI / modulus * product.astype(jnp.float32)


def signed_frequency(length):
    position = jnp.arange(length, dtype=jnp.int32)
    folded = jnp.where(position < length // 2, position, position - length)
    return 2.0 * folded.astype(jnp.float32) / length


def pixel_phase(pixel_index, shifts, aberration):
    freq_rows = signed_frequency(SR)[:, None, None]
    freq_cols = signed_frequency(SC)[None, :, None]
    half_rows = DROWS // 2
    half_cols = DCOLS // 2
    tilt_x = ((pixel_index // DCOLS - half_rows).astype(jnp.float32) / half_rows)[None, None, :]
    tilt_y = ((pixel_index % DCOLS - half_cols).astype(jnp.float32) / half_cols)[None, None, :]
    ramp_rows = jnp.mod(jnp.arange(SR, dtype=jnp.int32)[:, None] * shifts[:, 0][None, :], SR)
    ramp_cols = jnp.mod(jnp.arange(SC, dtype=jnp.int32)[:, None] * shifts[:, 1][None, :], SC)
    shift_phase = (
        TWO_PI / SR * ramp_rows.astype(jnp.float32)[:, None, :]
        + TWO_PI / SC * ramp_cols.astype(jnp.float32)[None, :, :]
    )
    tilt_sq = tilt_x * tilt_x + tilt_y * tilt_y
    tilt_dot = tilt_x * freq_rows + tilt_y * freq_cols
    moved_x = freq_rows + tilt_x
    moved_y = freq_cols + tilt_y
    moved_sq = moved_x * moved_x + moved_y * moved_y
    lens_phase = math.pi * (
        aberration[0] * (freq_rows * freq_rows + freq_cols * freq_cols)
        + aberration[1] * (moved_sq * moved_sq - tilt_sq * tilt_sq - 4.0 * tilt_sq * tilt_dot)
    )
    return shift_phase - lens_phase


def window_weights(width):
    position = jnp.arange(width, dtype=jnp.int32)
    nearest = jnp.minimum(position, width - 1 - position)
    ramped = 0.3 + 0.35 * (
        1.0 - jnp.cos(math.pi * (nearest.astype(jnp.float32) + 0.5) / (2 * HALO))
    )
    return jnp.where(nearest < 2 * HALO, ramped, jnp.float32(1.0))


def inverse_transform(spec_real, spec_imag, columns, rows):
    real_piece = jnp.dot(spec_real, cos_cols, precision=EXACT_PRECISION) - jnp.dot(
        spec_imag, sin_cols, precision=EXACT_PRECISION
    )
    imaginary_piece = jnp.dot(spec_real, sin_cols, precision=EXACT_PRECISION) + jnp.dot(
        spec_imag, cos_cols, precision=EXACT_PRECISION
    )
    angles_by_row = phase_angles(jnp.arange(SR, dtype=jnp.int32), rows, SR)
    row_cosines = jnp.cos(angles_by_row)
    row_sines = jnp.sin(angles_by_row)
    return jnp.dot(row_cosines.T, real_piece, precision=EXACT_PRECISION) - jnp.dot(
        row_sines.T, imaginary_piece, precision=EXACT_PRECISION
    )


def sincos_reduced(rest, quadrant):
    square = rest * rest
    sine = rest + rest * square * (
        -1.6666654611e-1 + square * (8.3321608736e-3 + square * -1.9515295891e-4)
    )
    cosine = 1.0 - 0.5 * square + square * square * (
        4.166664568298827e-2 + square * (-1.388731625493765e-3 + square * 2.443315711809948e-5)
    )
    swap = (quadrant & 1) == 1
    sin_out = jnp.where(swap, cosine, sine)
    cos_out = jnp.where(swap, sine, cosine)
    sin_out = jnp.where(quadrant >= 2, -sin_out, sin_out)
    cos_out = jnp.where((quadrant == 1) | (quadrant == 2), -cos_out, cos_out)
    return sin_out, cos_out


def sincos(angle):
    turns = jnp.round(angle * (2.0 / math.pi))
    quadrant = turns.astype(jnp.int32) & 3
    rest = angle - turns * 1.5703125
    rest = rest - turns * 4.837512969970703125e-4
    rest = rest - turns * 7.54978995489188216e-8
    return sincos_reduced(rest, quadrant)


def sincos_of_steps(steps, modulus):
    quarter = modulus // 4
    turns = (steps + quarter // 2) // quarter
    rest = (steps - turns * quarter).astype(jnp.float32) * (TWO_PI / modulus)
    return sincos_reduced(rest, turns & 3)


def pairwise_sum(values):
    while len(values) > 1:
        values = [
            values[e] + values[e + 1] if e + 1 < len(values) else values[e]
            for e in range(0, len(values), 2)
        ]
    return values[0]


def phase_parts(pixel_index, shifts, aberration, col_index):
    freq_rows = signed_frequency(SR)[:, None]
    freq_cols = (2.0 * jnp.where(col_index < SC // 2, col_index, col_index - SC).astype(jnp.float32) / SC)[:, None]
    half_rows = DROWS // 2
    half_cols = DCOLS // 2
    tilt_x = ((pixel_index // DCOLS - half_rows).astype(jnp.float32) / half_rows)[None, :]
    tilt_y = ((pixel_index % DCOLS - half_cols).astype(jnp.float32) / half_cols)[None, :]
    ramp_rows = jnp.mod(jnp.arange(SR, dtype=jnp.int32)[:, None] * shifts[:, 0][None, :], SR)
    ramp_cols = jnp.mod(col_index[:, None] * shifts[:, 1][None, :], SC)
    tilt_sq = tilt_x * tilt_x + tilt_y * tilt_y
    defocus = math.pi * aberration[0]
    spherical = math.pi * aberration[1]
    row_part = (
        TWO_PI / SR * ramp_rows.astype(jnp.float32)
        - defocus * freq_rows * freq_rows
        + spherical * (tilt_sq * tilt_sq + 4.0 * tilt_sq * tilt_x * freq_rows)
    )
    col_part = (
        TWO_PI / SC * ramp_cols.astype(jnp.float32)
        - defocus * freq_cols * freq_cols
        + spherical * (4.0 * tilt_sq * tilt_y * freq_cols)
    )
    moved_rows = (freq_rows + tilt_x) * (freq_rows + tilt_x)
    moved_cols = (freq_cols + tilt_y) * (freq_cols + tilt_y)
    return row_part, col_part, moved_rows, moved_cols, spherical


def four_point(points):
    (ar, ai), (br, bi), (cr, ci), (dr, di) = points
    s02r = ar + cr
    s02i = ai + ci
    d02r = ar - cr
    d02i = ai - ci
    s13r = br + dr
    s13i = bi + di
    d13r = br - dr
    d13i = bi - di
    return [
        (s02r + s13r, s02i + s13i),
        (d02r + d13i, d02i - d13r),
        (s02r - s13r, s02i - s13i),
        (d02r - d13i, d02i + d13r),
    ]


def fft16(points):
    twisted = {}
    for b in range(4):
        column = four_point([points[4 * a + b] for a in range(4)])
        for s1, (gr, gi) in enumerate(column):
            k = b * s1
            if k == 0:
                twisted[b, s1] = (gr, gi)
            elif k == 4:
                twisted[b, s1] = (gi, -gr)
            else:
                c = math.cos(TWO_PI * k / 16)
                d = math.sin(TWO_PI * k / 16)
                twisted[b, s1] = (gr * c + gi * d, gi * c - gr * d)
    out = [None] * 16
    for s1 in range(4):
        row = four_point([twisted[b, s1] for b in range(4)])
        for s2 in range(4):
            out[s1 + 4 * s2] = row[s2]
    return out


def spectrum_kernel(y_ref, lc_ref, ls_ref, uc_ref, us_ref, out_ref, acc_ref):
    acc_ref[...] = jnp.zeros(acc_ref.shape, acc_ref.dtype)
    width = lc_ref.shape[2]
    low = pl.multiple_of(pl.program_id(0) * width, width)
    high = pl.multiple_of(pl.program_id(0) * width + SC // 2, width)

    def body(i, carry):
        rows = pl.ds(pl.multiple_of(i * 8, 8), 8)
        full = fft16(
            [(y_ref[r, rows, pl.ds(low, width)], y_ref[r, rows, pl.ds(high, width)]) for r in range(SR)]
        )
        for s in range(SR):
            fr, fi = full[s]
            tc = lc_ref[s, rows, :]
            ts = ls_ref[s, rows, :]
            acc_ref[0, 0, s] += fr * tc - fi * ts
            acc_ref[0, 1, s] += fr * ts + fi * tc
            gr, gi = full[(SR - s) % SR]
            tc = uc_ref[s, rows, :]
            ts = us_ref[s, rows, :]
            acc_ref[1, 0, s] += gr * tc + gi * ts
            acc_ref[1, 1, s] += gr * ts - gi * tc
        return carry

    lax.fori_loop(0, lc_ref.shape[1] // 8, body, 0)
    for a in range(2):
        for b in range(2):
            out_ref[a, b] = jnp.sum(acc_ref[a, b], axis=1)


def spectrum(both_col, turn_cos, turn_sin):
    pixels = both_col.shape[1]
    half = SC // 2
    block = 128
    steps = half // block
    lower = lambda j: (0, 0, j)
    upper = lambda j: (0, 0, j + steps)
    spec = pl.pallas_call(
        spectrum_kernel,
        grid=(steps,),
        in_specs=[
            pl.BlockSpec(memory_space=pltpu.VMEM),
            pl.BlockSpec((SR, pixels, block), lower),
            pl.BlockSpec((SR, pixels, block), lower),
            pl.BlockSpec((SR, pixels, block), upper),
            pl.BlockSpec((SR, pixels, block), upper),
        ],
        out_specs=pl.BlockSpec((2, 2, SR, block), lambda j: (0, 0, 0, j)),
        out_shape=jax.ShapeDtypeStruct((2, 2, SR, half), jnp.float32),
        scratch_shapes=[pltpu.VMEM((2, 2, SR, 8, block), jnp.float32)],
        compiler_params=pltpu.CompilerParams(vmem_limit_bytes=40 * 1024 * 1024),
    )(both_col, turn_cos, turn_sin, turn_cos, turn_sin)
    return spec


def local(frames, offsets, bright, aberration):
    scan_size = lax.axis_size("scan")
    det_size = lax.axis_size("det")
    rows_dev, tile, detector = frames.shape
    owned = offsets.shape[0]
    groups = detector // owned
    owner = lax.axis_index("scan") * det_size + lax.axis_index("det")
    blocks = jnp.transpose(frames.reshape(rows_dev * tile, groups, owned), (1, 0, 2))
    arrived = lax.all_to_all(blocks, ("scan", "det"), split_axis=0, concat_axis=0, tiled=True)
    images = arrived.reshape(scan_size, det_size, rows_dev, tile, owned)
    half = SC // 2
    full_cols = jnp.arange(SC, dtype=jnp.int32)
    col_sin, col_cos = sincos_of_steps(
        jnp.mod(full_cols[:, None] * full_cols[None, :half], SC), SC
    )
    alternating = jnp.where(full_cols % 2 == 0, 1.0, -1.0)
    nyquist = jnp.where(jnp.arange(128)[None, :] == 0, alternating[:, None], 0.0)
    table = jnp.concatenate([col_cos, -col_sin, nyquist], axis=1).astype(jnp.bfloat16)
    both_col = jnp.einsum(
        "abrcp,acq->brpq",
        images,
        table.reshape(scan_size, tile, table.shape[1]),
        preferred_element_type=jnp.float32,
    ).reshape(SR, owned, table.shape[1])
    full_rows = jnp.arange(SR, dtype=jnp.int32)
    angles_by_row = phase_angles(full_rows, full_rows, SR)
    row_cos = jnp.cos(angles_by_row)
    row_sin = jnp.sin(angles_by_row)
    pixel_index = owner * owned + jnp.arange(owned, dtype=jnp.int32)
    steps = jnp.arange(half, dtype=jnp.int32)
    col_index = jnp.concatenate([steps, jnp.mod(SC - steps, SC), jnp.full((1,), half, jnp.int32)])
    row_part, col_part, moved_rows, moved_cols, spherical = phase_parts(
        pixel_index, offsets, aberration, col_index
    )
    moved_sq = moved_rows[:, :, None] + moved_cols.T[None, :, :]
    phase = row_part[:, :, None] + col_part.T[None, :, :] - spherical * (moved_sq * moved_sq)
    weights = bright.astype(jnp.float32)
    keep = (jnp.arange(SC + 1) != half).astype(jnp.float32)
    turn_sin, turn_cos = sincos(phase)
    turn_cos, turn_sin = lax.optimization_barrier(
        (
            turn_cos * weights[None, :, None] * keep[None, None, :],
            turn_sin * weights[None, :, None] * keep[None, None, :],
        )
    )
    parts = spectrum(both_col, turn_cos, turn_sin)
    nyquist_col = both_col[:, :, SC]
    nyquist_real = jnp.dot(row_cos.T, nyquist_col, precision=EXACT_PRECISION)
    nyquist_imag = -jnp.dot(row_sin.T, nyquist_col, precision=EXACT_PRECISION)
    last_cos = turn_cos[:, :, SC]
    last_sin = turn_sin[:, :, SC]
    nyquist_spec_real = jnp.sum(nyquist_real * last_cos - nyquist_imag * last_sin, axis=1)
    nyquist_spec_imag = jnp.sum(nyquist_real * last_sin + nyquist_imag * last_cos, axis=1)
    spectra = jnp.stack(
        [
            jnp.concatenate([parts[0, 0], parts[1, 0], nyquist_spec_real[:, None]], axis=1),
            jnp.concatenate([parts[0, 1], parts[1, 1], nyquist_spec_imag[:, None]], axis=1),
        ]
    )
    inverse_rows = jnp.stack(
        [
            jnp.stack([row_cos.T, -row_sin.T], axis=1),
            jnp.stack([row_sin.T, row_cos.T], axis=1),
        ]
    )
    rows_both = jnp.einsum("jrks,ksq->jrq", inverse_rows, spectra, precision=EXACT_PRECISION)
    rows_real = rows_both[0]
    rows_imag = rows_both[1]
    lanes = 2 * (SC + 1)
    packed = jnp.concatenate(
        [rows_real, rows_imag, jnp.broadcast_to(jnp.sum(weights), (SR, (-lanes) % 128 or 128))],
        axis=1,
    )
    width = tile + 2 * HALO
    columns = jnp.mod(
        lax.axis_index("scan") * tile - HALO + jnp.arange(width, dtype=jnp.int32), SC
    )
    col_angles = phase_angles(col_index, columns, SC)
    final_table = lax.optimization_barrier(
        jnp.concatenate([jnp.cos(col_angles), -jnp.sin(col_angles)], axis=0)
    )
    gathered = lax.all_to_all(packed, "det", 0, 0, tiled=True)
    own = pairwise_sum([gathered[i] for i in range(det_size)])
    spread = jnp.broadcast_to(own, (scan_size,) + own.shape)
    gathered = lax.all_to_all(spread, "scan", 0, 0, tiled=True)
    total = pairwise_sum([gathered[i] for i in range(scan_size)])
    bright_sum = total[lanes]
    picture = jnp.dot(total[:lanes], final_table, precision=EXACT_PRECISION)
    return (
        (picture * (1.0 / (SR * SC)) / jnp.sqrt(bright_sum) * window_weights(width))
        .reshape(rows_dev, 1, width)
    )


def solution(mesh):
    placed = (P("det", "scan", None), P(("scan", "det"), None), P(("scan", "det")), P())
    return jax.shard_map(
        local, mesh=mesh, in_specs=placed, out_specs=P("det", "scan", None), check_vma=False
    )
```

```python
import math

import jax
import jax.numpy as jnp
from jax import lax
from jax.sharding import PartitionSpec as P
from jax.experimental import pallas as pl
from jax.experimental.pallas import tpu as pltpu

SR = 16
SC = 1024
DROWS = 128
DCOLS = 128
HALO = 16


TWO_PI = 2.0 * math.pi
EXACT_PRECISION = lax.Precision.HIGHEST


def phase_angles(first, second_operand, modulus):
    product = jnp.mod(first[:, None] * second_operand[None, :], modulus)
    return TWO_PI / modulus * product.astype(jnp.float32)


def signed_frequency(length):
    position = jnp.arange(length, dtype=jnp.int32)
    folded = jnp.where(position < length // 2, position, position - length)
    return 2.0 * folded.astype(jnp.float32) / length


def pixel_phase(pixel_index, shifts, aberration):
    freq_rows = signed_frequency(SR)[:, None, None]
    freq_cols = signed_frequency(SC)[None, :, None]
    half_rows = DROWS // 2
    half_cols = DCOLS // 2
    tilt_x = ((pixel_index // DCOLS - half_rows).astype(jnp.float32) / half_rows)[None, None, :]
    tilt_y = ((pixel_index % DCOLS - half_cols).astype(jnp.float32) / half_cols)[None, None, :]
    ramp_rows = jnp.mod(jnp.arange(SR, dtype=jnp.int32)[:, None] * shifts[:, 0][None, :], SR)
    ramp_cols = jnp.mod(jnp.arange(SC, dtype=jnp.int32)[:, None] * shifts[:, 1][None, :], SC)
    shift_phase = (
        TWO_PI / SR * ramp_rows.astype(jnp.float32)[:, None, :]
        + TWO_PI / SC * ramp_cols.astype(jnp.float32)[None, :, :]
    )
    tilt_sq = tilt_x * tilt_x + tilt_y * tilt_y
    tilt_dot = tilt_x * freq_rows + tilt_y * freq_cols
    moved_x = freq_rows + tilt_x
    moved_y = freq_cols + tilt_y
    moved_sq = moved_x * moved_x + moved_y * moved_y
    lens_phase = math.pi * (
        aberration[0] * (freq_rows * freq_rows + freq_cols * freq_cols)
        + aberration[1] * (moved_sq * moved_sq - tilt_sq * tilt_sq - 4.0 * tilt_sq * tilt_dot)
    )
    return shift_phase - lens_phase


def window_weights(width):
    position = jnp.arange(width, dtype=jnp.int32)
    nearest = jnp.minimum(position, width - 1 - position)
    ramped = 0.3 + 0.35 * (
        1.0 - jnp.cos(math.pi * (nearest.astype(jnp.float32) + 0.5) / (2 * HALO))
    )
    return jnp.where(nearest < 2 * HALO, ramped, jnp.float32(1.0))


def inverse_transform(spec_real, spec_imag, columns, rows):
    real_piece = jnp.dot(spec_real, cos_cols, precision=EXACT_PRECISION) - jnp.dot(
        spec_imag, sin_cols, precision=EXACT_PRECISION
    )
    imaginary_piece = jnp.dot(spec_real, sin_cols, precision=EXACT_PRECISION) + jnp.dot(
        spec_imag, cos_cols, precision=EXACT_PRECISION
    )
    angles_by_row = phase_angles(jnp.arange(SR, dtype=jnp.int32), rows, SR)
    row_cosines = jnp.cos(angles_by_row)
    row_sines = jnp.sin(angles_by_row)
    return jnp.dot(row_cosines.T, real_piece, precision=EXACT_PRECISION) - jnp.dot(
        row_sines.T, imaginary_piece, precision=EXACT_PRECISION
    )


def sincos_reduced(rest, quadrant):
    square = rest * rest
    sine = rest + rest * square * (
        -1.6666654611e-1 + square * (8.3321608736e-3 + square * -1.9515295891e-4)
    )
    cosine = 1.0 - 0.5 * square + square * square * (
        4.166664568298827e-2 + square * (-1.388731625493765e-3 + square * 2.443315711809948e-5)
    )
    swap = (quadrant & 1) == 1
    sin_out = jnp.where(swap, cosine, sine)
    cos_out = jnp.where(swap, sine, cosine)
    sin_out = jnp.where(quadrant >= 2, -sin_out, sin_out)
    cos_out = jnp.where((quadrant == 1) | (quadrant == 2), -cos_out, cos_out)
    return sin_out, cos_out


def sincos(angle):
    turns = jnp.round(angle * (2.0 / math.pi))
    quadrant = turns.astype(jnp.int32) & 3
    rest = angle - turns * 1.5703125
    rest = rest - turns * 4.837512969970703125e-4
    rest = rest - turns * 7.54978995489188216e-8
    return sincos_reduced(rest, quadrant)


def sincos_of_steps(steps, modulus):
    quarter = modulus // 4
    turns = (steps + quarter // 2) // quarter
    rest = (steps - turns * quarter).astype(jnp.float32) * (TWO_PI / modulus)
    return sincos_reduced(rest, turns & 3)


def pairwise_sum(values):
    while len(values) > 1:
        values = [
            values[e] + values[e + 1] if e + 1 < len(values) else values[e]
            for e in range(0, len(values), 2)
        ]
    return values[0]


def phase_parts(pixel_index, shifts, aberration, col_index):
    freq_rows = signed_frequency(SR)[:, None]
    freq_cols = (2.0 * jnp.where(col_index < SC // 2, col_index, col_index - SC).astype(jnp.float32) / SC)[:, None]
    half_rows = DROWS // 2
    half_cols = DCOLS // 2
    tilt_x = ((pixel_index // DCOLS - half_rows).astype(jnp.float32) / half_rows)[None, :]
    tilt_y = ((pixel_index % DCOLS - half_cols).astype(jnp.float32) / half_cols)[None, :]
    ramp_rows = jnp.mod(jnp.arange(SR, dtype=jnp.int32)[:, None] * shifts[:, 0][None, :], SR)
    ramp_cols = jnp.mod(col_index[:, None] * shifts[:, 1][None, :], SC)
    tilt_sq = tilt_x * tilt_x + tilt_y * tilt_y
    defocus = math.pi * aberration[0]
    spherical = math.pi * aberration[1]
    row_part = (
        TWO_PI / SR * ramp_rows.astype(jnp.float32)
        - defocus * freq_rows * freq_rows
        + spherical * (tilt_sq * tilt_sq + 4.0 * tilt_sq * tilt_x * freq_rows)
    )
    col_part = (
        TWO_PI / SC * ramp_cols.astype(jnp.float32)
        - defocus * freq_cols * freq_cols
        + spherical * (4.0 * tilt_sq * tilt_y * freq_cols)
    )
    moved_rows = (freq_rows + tilt_x) * (freq_rows + tilt_x)
    moved_cols = (freq_cols + tilt_y) * (freq_cols + tilt_y)
    return row_part, col_part, moved_rows, moved_cols, spherical


def four_point(points):
    (ar, ai), (br, bi), (cr, ci), (dr, di) = points
    s02r = ar + cr
    s02i = ai + ci
    d02r = ar - cr
    d02i = ai - ci
    s13r = br + dr
    s13i = bi + di
    d13r = br - dr
    d13i = bi - di
    return [
        (s02r + s13r, s02i + s13i),
        (d02r + d13i, d02i - d13r),
        (s02r - s13r, s02i - s13i),
        (d02r - d13i, d02i + d13r),
    ]


def fft16(points):
    twisted = {}
    for b in range(4):
        column = four_point([points[4 * a + b] for a in range(4)])
        for s1, (gr, gi) in enumerate(column):
            k = b * s1
            if k == 0:
                twisted[b, s1] = (gr, gi)
            elif k == 4:
                twisted[b, s1] = (gi, -gr)
            else:
                c = math.cos(TWO_PI * k / 16)
                d = math.sin(TWO_PI * k / 16)
                twisted[b, s1] = (gr * c + gi * d, gi * c - gr * d)
    out = [None] * 16
    for s1 in range(4):
        row = four_point([twisted[b, s1] for b in range(4)])
        for s2 in range(4):
            out[s1 + 4 * s2] = row[s2]
    return out


def spectrum_kernel(y_ref, lc_ref, ls_ref, uc_ref, us_ref, out_ref, acc_ref):
    part = pl.program_id(1)

    @pl.when(part == 0)
    def _():
        acc_ref[...] = jnp.zeros(acc_ref.shape, acc_ref.dtype)

    width = lc_ref.shape[2]
    span = lc_ref.shape[1]
    low = pl.multiple_of(pl.program_id(0) * width, width)
    high = pl.multiple_of(pl.program_id(0) * width + SC // 2, width)

    def body(i, carry):
        rows = pl.ds(pl.multiple_of(i * 8, 8), 8)
        lines = pl.ds(pl.multiple_of(part * span + i * 8, 8), 8)
        full = fft16(
            [(y_ref[r, lines, pl.ds(low, width)], y_ref[r, lines, pl.ds(high, width)]) for r in range(SR)]
        )
        for s in range(SR):
            fr, fi = full[s]
            tc = lc_ref[s, rows, :]
            ts = ls_ref[s, rows, :]
            acc_ref[0, 0, s] += fr * tc - fi * ts
            acc_ref[0, 1, s] += fr * ts + fi * tc
            gr, gi = full[(SR - s) % SR]
            tc = uc_ref[s, rows, :]
            ts = us_ref[s, rows, :]
            acc_ref[1, 0, s] += gr * tc + gi * ts
            acc_ref[1, 1, s] += gr * ts - gi * tc
        return carry

    lax.fori_loop(0, span // 8, body, 0)

    @pl.when(part == pl.num_programs(1) - 1)
    def _():
        for a in range(2):
            for b in range(2):
                out_ref[a, b] = jnp.sum(acc_ref[a, b], axis=1)


def spectrum(both_col, turn_cos, turn_sin):
    pixels = both_col.shape[1]
    half = SC // 2
    block = 128
    steps = half // block
    splits = 2
    lower = lambda j, k: (0, k, j)
    upper = lambda j, k: (0, k, j + steps)
    spec = pl.pallas_call(
        spectrum_kernel,
        grid=(steps, splits),
        in_specs=[
            pl.BlockSpec(memory_space=pltpu.VMEM),
            pl.BlockSpec((SR, pixels // splits, block), lower),
            pl.BlockSpec((SR, pixels // splits, block), lower),
            pl.BlockSpec((SR, pixels // splits, block), upper),
            pl.BlockSpec((SR, pixels // splits, block), upper),
        ],
        out_specs=pl.BlockSpec((2, 2, SR, block), lambda j, k: (0, 0, 0, j)),
        out_shape=jax.ShapeDtypeStruct((2, 2, SR, half), jnp.float32),
        scratch_shapes=[pltpu.VMEM((2, 2, SR, 8, block), jnp.float32)],
        compiler_params=pltpu.CompilerParams(vmem_limit_bytes=40 * 1024 * 1024),
    )(both_col, turn_cos, turn_sin, turn_cos, turn_sin)
    return spec


def local(frames, offsets, bright, aberration):
    scan_size = lax.axis_size("scan")
    det_size = lax.axis_size("det")
    rows_dev, tile, detector = frames.shape
    owned = offsets.shape[0]
    groups = detector // owned
    owner = lax.axis_index("scan") * det_size + lax.axis_index("det")
    blocks = jnp.transpose(frames.reshape(rows_dev * tile, groups, owned), (1, 0, 2))
    arrived = lax.all_to_all(blocks, ("scan", "det"), split_axis=0, concat_axis=0, tiled=True)
    images = arrived.reshape(scan_size, det_size, rows_dev, tile, owned)
    half = SC // 2
    full_cols = jnp.arange(SC, dtype=jnp.int32)
    col_sin, col_cos = sincos_of_steps(
        jnp.mod(full_cols[:, None] * full_cols[None, :half], SC), SC
    )
    alternating = jnp.where(full_cols % 2 == 0, 1.0, -1.0)
    nyquist = jnp.where(jnp.arange(128)[None, :] == 0, alternating[:, None], 0.0)
    table = jnp.concatenate([col_cos, -col_sin, nyquist], axis=1).astype(jnp.bfloat16)
    both_col = jnp.einsum(
        "abrcp,acq->brpq",
        images,
        table.reshape(scan_size, tile, table.shape[1]),
        preferred_element_type=jnp.float32,
    ).reshape(SR, owned, table.shape[1])
    full_rows = jnp.arange(SR, dtype=jnp.int32)
    angles_by_row = phase_angles(full_rows, full_rows, SR)
    row_cos = jnp.cos(angles_by_row)
    row_sin = jnp.sin(angles_by_row)
    pixel_index = owner * owned + jnp.arange(owned, dtype=jnp.int32)
    steps = jnp.arange(half, dtype=jnp.int32)
    col_index = jnp.concatenate([steps, jnp.mod(SC - steps, SC), jnp.full((1,), half, jnp.int32)])
    row_part, col_part, moved_rows, moved_cols, spherical = phase_parts(
        pixel_index, offsets, aberration, col_index
    )
    moved_sq = moved_rows[:, :, None] + moved_cols.T[None, :, :]
    phase = row_part[:, :, None] + col_part.T[None, :, :] - spherical * (moved_sq * moved_sq)
    weights = bright.astype(jnp.float32)
    keep = (jnp.arange(SC + 1) != half).astype(jnp.float32)
    turn_sin, turn_cos = sincos(phase)
    turn_cos, turn_sin = lax.optimization_barrier(
        (
            turn_cos * weights[None, :, None] * keep[None, None, :],
            turn_sin * weights[None, :, None] * keep[None, None, :],
        )
    )
    parts = spectrum(both_col, turn_cos, turn_sin)
    nyquist_col = both_col[:, :, SC]
    nyquist_real = jnp.dot(row_cos.T, nyquist_col, precision=EXACT_PRECISION)
    nyquist_imag = -jnp.dot(row_sin.T, nyquist_col, precision=EXACT_PRECISION)
    last_cos = turn_cos[:, :, SC]
    last_sin = turn_sin[:, :, SC]
    nyquist_spec_real = jnp.sum(nyquist_real * last_cos - nyquist_imag * last_sin, axis=1)
    nyquist_spec_imag = jnp.sum(nyquist_real * last_sin + nyquist_imag * last_cos, axis=1)
    spectra = jnp.stack(
        [
            jnp.concatenate([parts[0, 0], parts[1, 0], nyquist_spec_real[:, None]], axis=1),
            jnp.concatenate([parts[0, 1], parts[1, 1], nyquist_spec_imag[:, None]], axis=1),
        ]
    )
    inverse_rows = jnp.stack(
        [
            jnp.stack([row_cos.T, -row_sin.T], axis=1),
            jnp.stack([row_sin.T, row_cos.T], axis=1),
        ]
    )
    rows_both = jnp.einsum("jrks,ksq->jrq", inverse_rows, spectra, precision=EXACT_PRECISION)
    rows_real = rows_both[0]
    rows_imag = rows_both[1]
    lanes = 2 * (SC + 1)
    packed = jnp.concatenate(
        [rows_real, rows_imag, jnp.broadcast_to(jnp.sum(weights), (SR, (-lanes) % 128 or 128))],
        axis=1,
    )
    width = tile + 2 * HALO
    columns = jnp.mod(
        lax.axis_index("scan") * tile - HALO + jnp.arange(width, dtype=jnp.int32), SC
    )
    col_angles = phase_angles(col_index, columns, SC)
    final_table = lax.optimization_barrier(
        jnp.concatenate([jnp.cos(col_angles), -jnp.sin(col_angles)], axis=0)
    )
    gathered = lax.all_to_all(packed, "det", 0, 0, tiled=True)
    own = pairwise_sum([gathered[i] for i in range(det_size)])
    spread = jnp.broadcast_to(own, (scan_size,) + own.shape)
    gathered = lax.all_to_all(spread, "scan", 0, 0, tiled=True)
    total = pairwise_sum([gathered[i] for i in range(scan_size)])
    bright_sum = total[lanes]
    picture = jnp.dot(total[:lanes], final_table, precision=EXACT_PRECISION)
    return (
        (picture * (1.0 / (SR * SC)) / jnp.sqrt(bright_sum) * window_weights(width))
        .reshape(rows_dev, 1, width)
    )


def solution(mesh):
    placed = (P("det", "scan", None), P(("scan", "det"), None), P(("scan", "det")), P())
    return jax.shard_map(
        local, mesh=mesh, in_specs=placed, out_specs=P("det", "scan", None), check_vma=False
    )
```

```python
import math

import jax
import jax.numpy as jnp
from jax import lax
from jax.sharding import PartitionSpec as P
from jax.experimental import pallas as pl
from jax.experimental.pallas import tpu as pltpu

SR = 16
SC = 1024
DROWS = 128
DCOLS = 128
HALO = 16


TWO_PI = 2.0 * math.pi
EXACT_PRECISION = lax.Precision.HIGHEST


def phase_angles(first, second_operand, modulus):
    product = jnp.mod(first[:, None] * second_operand[None, :], modulus)
    return TWO_PI / modulus * product.astype(jnp.float32)


def signed_frequency(length):
    position = jnp.arange(length, dtype=jnp.int32)
    folded = jnp.where(position < length // 2, position, position - length)
    return 2.0 * folded.astype(jnp.float32) / length


def pixel_phase(pixel_index, shifts, aberration):
    freq_rows = signed_frequency(SR)[:, None, None]
    freq_cols = signed_frequency(SC)[None, :, None]
    half_rows = DROWS // 2
    half_cols = DCOLS // 2
    tilt_x = ((pixel_index // DCOLS - half_rows).astype(jnp.float32) / half_rows)[None, None, :]
    tilt_y = ((pixel_index % DCOLS - half_cols).astype(jnp.float32) / half_cols)[None, None, :]
    ramp_rows = jnp.mod(jnp.arange(SR, dtype=jnp.int32)[:, None] * shifts[:, 0][None, :], SR)
    ramp_cols = jnp.mod(jnp.arange(SC, dtype=jnp.int32)[:, None] * shifts[:, 1][None, :], SC)
    shift_phase = (
        TWO_PI / SR * ramp_rows.astype(jnp.float32)[:, None, :]
        + TWO_PI / SC * ramp_cols.astype(jnp.float32)[None, :, :]
    )
    tilt_sq = tilt_x * tilt_x + tilt_y * tilt_y
    tilt_dot = tilt_x * freq_rows + tilt_y * freq_cols
    moved_x = freq_rows + tilt_x
    moved_y = freq_cols + tilt_y
    moved_sq = moved_x * moved_x + moved_y * moved_y
    lens_phase = math.pi * (
        aberration[0] * (freq_rows * freq_rows + freq_cols * freq_cols)
        + aberration[1] * (moved_sq * moved_sq - tilt_sq * tilt_sq - 4.0 * tilt_sq * tilt_dot)
    )
    return shift_phase - lens_phase


def window_weights(width):
    position = jnp.arange(width, dtype=jnp.int32)
    nearest = jnp.minimum(position, width - 1 - position)
    ramped = 0.3 + 0.35 * (
        1.0 - jnp.cos(math.pi * (nearest.astype(jnp.float32) + 0.5) / (2 * HALO))
    )
    return jnp.where(nearest < 2 * HALO, ramped, jnp.float32(1.0))


def inverse_transform(spec_real, spec_imag, columns, rows):
    real_piece = jnp.dot(spec_real, cos_cols, precision=EXACT_PRECISION) - jnp.dot(
        spec_imag, sin_cols, precision=EXACT_PRECISION
    )
    imaginary_piece = jnp.dot(spec_real, sin_cols, precision=EXACT_PRECISION) + jnp.dot(
        spec_imag, cos_cols, precision=EXACT_PRECISION
    )
    angles_by_row = phase_angles(jnp.arange(SR, dtype=jnp.int32), rows, SR)
    row_cosines = jnp.cos(angles_by_row)
    row_sines = jnp.sin(angles_by_row)
    return jnp.dot(row_cosines.T, real_piece, precision=EXACT_PRECISION) - jnp.dot(
        row_sines.T, imaginary_piece, precision=EXACT_PRECISION
    )


def sincos_reduced(rest, quadrant):
    square = rest * rest
    sine = rest + rest * square * (
        -1.6666654611e-1 + square * (8.3321608736e-3 + square * -1.9515295891e-4)
    )
    cosine = 1.0 - 0.5 * square + square * square * (
        4.166664568298827e-2 + square * (-1.388731625493765e-3 + square * 2.443315711809948e-5)
    )
    swap = (quadrant & 1) == 1
    sin_out = jnp.where(swap, cosine, sine)
    cos_out = jnp.where(swap, sine, cosine)
    sin_out = jnp.where(quadrant >= 2, -sin_out, sin_out)
    cos_out = jnp.where((quadrant == 1) | (quadrant == 2), -cos_out, cos_out)
    return sin_out, cos_out


def sincos(angle):
    turns = jnp.round(angle * (2.0 / math.pi))
    quadrant = turns.astype(jnp.int32) & 3
    rest = angle - turns * 1.5703125
    rest = rest - turns * 4.837512969970703125e-4
    rest = rest - turns * 7.54978995489188216e-8
    return sincos_reduced(rest, quadrant)


def sincos_of_steps(steps, modulus):
    quarter = modulus // 4
    turns = (steps + quarter // 2) // quarter
    rest = (steps - turns * quarter).astype(jnp.float32) * (TWO_PI / modulus)
    return sincos_reduced(rest, turns & 3)


def pairwise_sum(values):
    while len(values) > 1:
        values = [
            values[e] + values[e + 1] if e + 1 < len(values) else values[e]
            for e in range(0, len(values), 2)
        ]
    return values[0]


def phase_parts(pixel_index, shifts, aberration, col_index):
    freq_rows = signed_frequency(SR)[:, None]
    freq_cols = (2.0 * jnp.where(col_index < SC // 2, col_index, col_index - SC).astype(jnp.float32) / SC)[:, None]
    half_rows = DROWS // 2
    half_cols = DCOLS // 2
    tilt_x = ((pixel_index // DCOLS - half_rows).astype(jnp.float32) / half_rows)[None, :]
    tilt_y = ((pixel_index % DCOLS - half_cols).astype(jnp.float32) / half_cols)[None, :]
    ramp_rows = jnp.mod(jnp.arange(SR, dtype=jnp.int32)[:, None] * shifts[:, 0][None, :], SR)
    ramp_cols = jnp.mod(col_index[:, None] * shifts[:, 1][None, :], SC)
    tilt_sq = tilt_x * tilt_x + tilt_y * tilt_y
    defocus = math.pi * aberration[0]
    spherical = math.pi * aberration[1]
    row_part = (
        TWO_PI / SR * ramp_rows.astype(jnp.float32)
        - defocus * freq_rows * freq_rows
        + spherical * (tilt_sq * tilt_sq + 4.0 * tilt_sq * tilt_x * freq_rows)
    )
    col_part = (
        TWO_PI / SC * ramp_cols.astype(jnp.float32)
        - defocus * freq_cols * freq_cols
        + spherical * (4.0 * tilt_sq * tilt_y * freq_cols)
    )
    moved_rows = (freq_rows + tilt_x) * (freq_rows + tilt_x)
    moved_cols = (freq_cols + tilt_y) * (freq_cols + tilt_y)
    return row_part, col_part, moved_rows, moved_cols, spherical


def four_point(points):
    (ar, ai), (br, bi), (cr, ci), (dr, di) = points
    s02r = ar + cr
    s02i = ai + ci
    d02r = ar - cr
    d02i = ai - ci
    s13r = br + dr
    s13i = bi + di
    d13r = br - dr
    d13i = bi - di
    return [
        (s02r + s13r, s02i + s13i),
        (d02r + d13i, d02i - d13r),
        (s02r - s13r, s02i - s13i),
        (d02r - d13i, d02i + d13r),
    ]


def fft16(points):
    twisted = {}
    for b in range(4):
        column = four_point([points[4 * a + b] for a in range(4)])
        for s1, (gr, gi) in enumerate(column):
            k = b * s1
            if k == 0:
                twisted[b, s1] = (gr, gi)
            elif k == 4:
                twisted[b, s1] = (gi, -gr)
            else:
                c = math.cos(TWO_PI * k / 16)
                d = math.sin(TWO_PI * k / 16)
                twisted[b, s1] = (gr * c + gi * d, gi * c - gr * d)
    out = [None] * 16
    for s1 in range(4):
        row = four_point([twisted[b, s1] for b in range(4)])
        for s2 in range(4):
            out[s1 + 4 * s2] = row[s2]
    return out


def spectrum_kernel(y_ref, lc_ref, ls_ref, uc_ref, us_ref, out_ref, acc_ref):
    acc_ref[...] = jnp.zeros(acc_ref.shape, acc_ref.dtype)
    width = lc_ref.shape[2]
    low = pl.multiple_of(pl.program_id(0) * width, width)
    high = pl.multiple_of(pl.program_id(0) * width + SC // 2, width)

    def body(i, carry):
        rows = pl.ds(pl.multiple_of(i * 8, 8), 8)
        full = fft16(
            [(y_ref[r, rows, pl.ds(low, width)], y_ref[r, rows, pl.ds(high, width)]) for r in range(SR)]
        )
        for s in range(SR):
            fr, fi = full[s]
            tc = lc_ref[s, rows, :]
            ts = ls_ref[s, rows, :]
            acc_ref[0, 0, s] += fr * tc - fi * ts
            acc_ref[0, 1, s] += fr * ts + fi * tc
            gr, gi = full[(SR - s) % SR]
            tc = uc_ref[s, rows, :]
            ts = us_ref[s, rows, :]
            acc_ref[1, 0, s] += gr * tc + gi * ts
            acc_ref[1, 1, s] += gr * ts - gi * tc
        return carry

    lax.fori_loop(0, lc_ref.shape[1] // 8, body, 0)
    for a in range(2):
        for b in range(2):
            out_ref[a, b] = jnp.sum(acc_ref[a, b], axis=1)


def spectrum(both_col, turn_cos, turn_sin):
    pixels = both_col.shape[1]
    half = SC // 2
    block = 128
    steps = half // block
    lower = lambda j: (0, 0, j)
    upper = lambda j: (0, 0, j + steps)
    spec = pl.pallas_call(
        spectrum_kernel,
        grid=(steps,),
        in_specs=[
            pl.BlockSpec(memory_space=pltpu.VMEM),
            pl.BlockSpec((SR, pixels, block), lower),
            pl.BlockSpec((SR, pixels, block), lower),
            pl.BlockSpec((SR, pixels, block), upper),
            pl.BlockSpec((SR, pixels, block), upper),
        ],
        out_specs=pl.BlockSpec((2, 2, SR, block), lambda j: (0, 0, 0, j)),
        out_shape=jax.ShapeDtypeStruct((2, 2, SR, half), jnp.float32),
        scratch_shapes=[pltpu.VMEM((2, 2, SR, 8, block), jnp.float32)],
        compiler_params=pltpu.CompilerParams(vmem_limit_bytes=40 * 1024 * 1024),
    )(both_col, turn_cos, turn_sin, turn_cos, turn_sin)
    return spec


def local(frames, offsets, bright, aberration):
    scan_size = lax.axis_size("scan")
    det_size = lax.axis_size("det")
    rows_dev, tile, detector = frames.shape
    owned = offsets.shape[0]
    groups = detector // owned
    owner = lax.axis_index("scan") * det_size + lax.axis_index("det")
    blocks = jnp.transpose(frames.reshape(rows_dev * tile, groups, owned), (1, 0, 2))
    arrived = lax.all_to_all(blocks, ("scan", "det"), split_axis=0, concat_axis=0, tiled=True)
    images = arrived.reshape(scan_size, det_size, rows_dev, tile, owned)
    half = SC // 2
    full_cols = jnp.arange(SC, dtype=jnp.int32)
    col_sin, col_cos = sincos_of_steps(
        jnp.mod(full_cols[:, None] * full_cols[None, :half], SC), SC
    )
    alternating = jnp.where(full_cols % 2 == 0, 1.0, -1.0)
    nyquist = jnp.where(jnp.arange(128)[None, :] == 0, alternating[:, None], 0.0)
    table = jnp.concatenate([col_cos, -col_sin, nyquist], axis=1).astype(jnp.bfloat16)
    both_col = jnp.einsum(
        "abrcp,acq->brpq",
        images,
        table.reshape(scan_size, tile, table.shape[1]),
        preferred_element_type=jnp.float32,
    ).reshape(SR, owned, table.shape[1])
    full_rows = jnp.arange(SR, dtype=jnp.int32)
    angles_by_row = phase_angles(full_rows, full_rows, SR)
    row_cos = jnp.cos(angles_by_row)
    row_sin = jnp.sin(angles_by_row)
    pixel_index = owner * owned + jnp.arange(owned, dtype=jnp.int32)
    steps = jnp.arange(half, dtype=jnp.int32)
    col_index = jnp.concatenate([steps, jnp.mod(SC - steps, SC), jnp.full((1,), half, jnp.int32)])
    row_part, col_part, moved_rows, moved_cols, spherical = phase_parts(
        pixel_index, offsets, aberration, col_index
    )
    moved_sq = moved_rows[:, :, None] + moved_cols.T[None, :, :]
    phase = row_part[:, :, None] + col_part.T[None, :, :] - spherical * (moved_sq * moved_sq)
    weights = bright.astype(jnp.float32)
    keep = (jnp.arange(SC + 1) != half).astype(jnp.float32)
    turn_sin, turn_cos = sincos(phase)
    turn_cos, turn_sin = lax.optimization_barrier(
        (
            turn_cos * weights[None, :, None] * keep[None, None, :],
            turn_sin * weights[None, :, None] * keep[None, None, :],
        )
    )
    parts = spectrum(both_col, turn_cos, turn_sin)
    nyquist_col = both_col[:, :, SC]
    nyquist_real = jnp.dot(row_cos.T, nyquist_col, precision=EXACT_PRECISION)
    nyquist_imag = -jnp.dot(row_sin.T, nyquist_col, precision=EXACT_PRECISION)
    last_cos = turn_cos[:, :, SC]
    last_sin = turn_sin[:, :, SC]
    nyquist_spec_real = jnp.sum(nyquist_real * last_cos - nyquist_imag * last_sin, axis=1)
    nyquist_spec_imag = jnp.sum(nyquist_real * last_sin + nyquist_imag * last_cos, axis=1)
    spectra = jnp.stack(
        [
            jnp.concatenate([parts[0, 0], parts[1, 0], nyquist_spec_real[:, None]], axis=1),
            jnp.concatenate([parts[0, 1], parts[1, 1], nyquist_spec_imag[:, None]], axis=1),
        ]
    )
    inverse_rows = jnp.stack(
        [
            jnp.stack([row_cos.T, -row_sin.T], axis=1),
            jnp.stack([row_sin.T, row_cos.T], axis=1),
        ]
    )
    rows_both = jnp.einsum("jrks,ksq->jrq", inverse_rows, spectra, precision=EXACT_PRECISION)
    rows_real = rows_both[0]
    rows_imag = rows_both[1]
    lanes = 2 * (SC + 1)
    packed = jnp.concatenate(
        [rows_real, rows_imag, jnp.broadcast_to(jnp.sum(weights), (SR, (-lanes) % 128 or 128))],
        axis=1,
    )
    width = tile + 2 * HALO
    columns = jnp.mod(
        lax.axis_index("scan") * tile - HALO + jnp.arange(width, dtype=jnp.int32), SC
    )
    col_angles = phase_angles(col_index, columns, SC)
    final_table = lax.optimization_barrier(
        jnp.concatenate([jnp.cos(col_angles), -jnp.sin(col_angles)], axis=0)
    )
    gathered = lax.all_to_all(packed.reshape(SR, -1, 128), "det", 0, 0, tiled=True)
    own = pairwise_sum([gathered[i] for i in range(det_size)])
    spread = jnp.broadcast_to(own, (scan_size,) + own.shape)
    gathered = lax.all_to_all(spread, "scan", 0, 0, tiled=True)
    total = pairwise_sum([gathered[i] for i in range(scan_size)]).reshape(-1)
    bright_sum = total[lanes]
    picture = jnp.dot(total[:lanes], final_table, precision=EXACT_PRECISION)
    return (
        (picture * (1.0 / (SR * SC)) / jnp.sqrt(bright_sum) * window_weights(width))
        .reshape(rows_dev, 1, width)
    )


def solution(mesh):
    placed = (P("det", "scan", None), P(("scan", "det"), None), P(("scan", "det")), P())
    return jax.shard_map(
        local, mesh=mesh, in_specs=placed, out_specs=P("det", "scan", None), check_vma=False
    )
```

```python
import math

import jax
import jax.numpy as jnp
from jax import lax
from jax.sharding import PartitionSpec as P
from jax.experimental import pallas as pl
from jax.experimental.pallas import tpu as pltpu

SR = 16
SC = 1024
DROWS = 128
DCOLS = 128
HALO = 16


TWO_PI = 2.0 * math.pi
EXACT_PRECISION = lax.Precision.HIGHEST


def phase_angles(first, second_operand, modulus):
    product = jnp.mod(first[:, None] * second_operand[None, :], modulus)
    return TWO_PI / modulus * product.astype(jnp.float32)


def signed_frequency(length):
    position = jnp.arange(length, dtype=jnp.int32)
    folded = jnp.where(position < length // 2, position, position - length)
    return 2.0 * folded.astype(jnp.float32) / length


def pixel_phase(pixel_index, shifts, aberration):
    freq_rows = signed_frequency(SR)[:, None, None]
    freq_cols = signed_frequency(SC)[None, :, None]
    half_rows = DROWS // 2
    half_cols = DCOLS // 2
    tilt_x = ((pixel_index // DCOLS - half_rows).astype(jnp.float32) / half_rows)[None, None, :]
    tilt_y = ((pixel_index % DCOLS - half_cols).astype(jnp.float32) / half_cols)[None, None, :]
    ramp_rows = jnp.mod(jnp.arange(SR, dtype=jnp.int32)[:, None] * shifts[:, 0][None, :], SR)
    ramp_cols = jnp.mod(jnp.arange(SC, dtype=jnp.int32)[:, None] * shifts[:, 1][None, :], SC)
    shift_phase = (
        TWO_PI / SR * ramp_rows.astype(jnp.float32)[:, None, :]
        + TWO_PI / SC * ramp_cols.astype(jnp.float32)[None, :, :]
    )
    tilt_sq = tilt_x * tilt_x + tilt_y * tilt_y
    tilt_dot = tilt_x * freq_rows + tilt_y * freq_cols
    moved_x = freq_rows + tilt_x
    moved_y = freq_cols + tilt_y
    moved_sq = moved_x * moved_x + moved_y * moved_y
    lens_phase = math.pi * (
        aberration[0] * (freq_rows * freq_rows + freq_cols * freq_cols)
        + aberration[1] * (moved_sq * moved_sq - tilt_sq * tilt_sq - 4.0 * tilt_sq * tilt_dot)
    )
    return shift_phase - lens_phase


def window_weights(width):
    position = jnp.arange(width, dtype=jnp.int32)
    nearest = jnp.minimum(position, width - 1 - position)
    ramped = 0.3 + 0.35 * (
        1.0 - jnp.cos(math.pi * (nearest.astype(jnp.float32) + 0.5) / (2 * HALO))
    )
    return jnp.where(nearest < 2 * HALO, ramped, jnp.float32(1.0))


def inverse_transform(spec_real, spec_imag, columns, rows):
    real_piece = jnp.dot(spec_real, cos_cols, precision=EXACT_PRECISION) - jnp.dot(
        spec_imag, sin_cols, precision=EXACT_PRECISION
    )
    imaginary_piece = jnp.dot(spec_real, sin_cols, precision=EXACT_PRECISION) + jnp.dot(
        spec_imag, cos_cols, precision=EXACT_PRECISION
    )
    angles_by_row = phase_angles(jnp.arange(SR, dtype=jnp.int32), rows, SR)
    row_cosines = jnp.cos(angles_by_row)
    row_sines = jnp.sin(angles_by_row)
    return jnp.dot(row_cosines.T, real_piece, precision=EXACT_PRECISION) - jnp.dot(
        row_sines.T, imaginary_piece, precision=EXACT_PRECISION
    )


def sincos_reduced(rest, quadrant):
    square = rest * rest
    sine = rest + rest * square * (
        -1.6666654611e-1 + square * (8.3321608736e-3 + square * -1.9515295891e-4)
    )
    cosine = 1.0 - 0.5 * square + square * square * (
        4.166664568298827e-2 + square * (-1.388731625493765e-3 + square * 2.443315711809948e-5)
    )
    swap = (quadrant & 1) == 1
    sin_out = jnp.where(swap, cosine, sine)
    cos_out = jnp.where(swap, sine, cosine)
    sin_out = jnp.where(quadrant >= 2, -sin_out, sin_out)
    cos_out = jnp.where((quadrant == 1) | (quadrant == 2), -cos_out, cos_out)
    return sin_out, cos_out


def sincos(angle):
    turns = jnp.round(angle * (2.0 / math.pi))
    quadrant = turns.astype(jnp.int32) & 3
    rest = angle - turns * 1.5703125
    rest = rest - turns * 4.837512969970703125e-4
    rest = rest - turns * 7.54978995489188216e-8
    return sincos_reduced(rest, quadrant)


def sincos_of_steps(steps, modulus):
    quarter = modulus // 4
    turns = (steps + quarter // 2) // quarter
    rest = (steps - turns * quarter).astype(jnp.float32) * (TWO_PI / modulus)
    return sincos_reduced(rest, turns & 3)


def pairwise_sum(values):
    while len(values) > 1:
        values = [
            values[e] + values[e + 1] if e + 1 < len(values) else values[e]
            for e in range(0, len(values), 2)
        ]
    return values[0]


def phase_parts(pixel_index, shifts, aberration, col_index):
    freq_rows = signed_frequency(SR)[:, None]
    freq_cols = (2.0 * jnp.where(col_index < SC // 2, col_index, col_index - SC).astype(jnp.float32) / SC)[:, None]
    half_rows = DROWS // 2
    half_cols = DCOLS // 2
    tilt_x = ((pixel_index // DCOLS - half_rows).astype(jnp.float32) / half_rows)[None, :]
    tilt_y = ((pixel_index % DCOLS - half_cols).astype(jnp.float32) / half_cols)[None, :]
    ramp_rows = jnp.mod(jnp.arange(SR, dtype=jnp.int32)[:, None] * shifts[:, 0][None, :], SR)
    ramp_cols = jnp.mod(col_index[:, None] * shifts[:, 1][None, :], SC)
    tilt_sq = tilt_x * tilt_x + tilt_y * tilt_y
    defocus = math.pi * aberration[0]
    spherical = math.pi * aberration[1]
    row_part = (
        TWO_PI / SR * ramp_rows.astype(jnp.float32)
        - defocus * freq_rows * freq_rows
        + spherical * (tilt_sq * tilt_sq + 4.0 * tilt_sq * tilt_x * freq_rows)
    )
    col_part = (
        TWO_PI / SC * ramp_cols.astype(jnp.float32)
        - defocus * freq_cols * freq_cols
        + spherical * (4.0 * tilt_sq * tilt_y * freq_cols)
    )
    moved_rows = (freq_rows + tilt_x) * (freq_rows + tilt_x)
    moved_cols = (freq_cols + tilt_y) * (freq_cols + tilt_y)
    return row_part, col_part, moved_rows, moved_cols, spherical


def four_point(points):
    (ar, ai), (br, bi), (cr, ci), (dr, di) = points
    s02r = ar + cr
    s02i = ai + ci
    d02r = ar - cr
    d02i = ai - ci
    s13r = br + dr
    s13i = bi + di
    d13r = br - dr
    d13i = bi - di
    return [
        (s02r + s13r, s02i + s13i),
        (d02r + d13i, d02i - d13r),
        (s02r - s13r, s02i - s13i),
        (d02r - d13i, d02i + d13r),
    ]


def fft16(points):
    twisted = {}
    for b in range(4):
        column = four_point([points[4 * a + b] for a in range(4)])
        for s1, (gr, gi) in enumerate(column):
            k = b * s1
            if k == 0:
                twisted[b, s1] = (gr, gi)
            elif k == 4:
                twisted[b, s1] = (gi, -gr)
            else:
                c = math.cos(TWO_PI * k / 16)
                d = math.sin(TWO_PI * k / 16)
                twisted[b, s1] = (gr * c + gi * d, gi * c - gr * d)
    out = [None] * 16
    for s1 in range(4):
        row = four_point([twisted[b, s1] for b in range(4)])
        for s2 in range(4):
            out[s1 + 4 * s2] = row[s2]
    return out


def spectrum_kernel(y_ref, lc_ref, ls_ref, uc_ref, us_ref, out_ref, acc_ref):
    width = lc_ref.shape[2]
    low = pl.multiple_of(pl.program_id(0) * width, width)
    high = pl.multiple_of(pl.program_id(0) * width + SC // 2, width)

    def pass_for(upper):
        def body(i, acc):
            rows = pl.ds(pl.multiple_of(i * 8, 8), 8)
            full = fft16(
                [(y_ref[r, rows, pl.ds(low, width)], y_ref[r, rows, pl.ds(high, width)]) for r in range(SR)]
            )
            out = []
            for s in range(SR):
                if upper:
                    fr, fi = full[(SR - s) % SR]
                    fi = -fi
                    tc = uc_ref[s, rows, :]
                    ts = us_ref[s, rows, :]
                else:
                    fr, fi = full[s]
                    tc = lc_ref[s, rows, :]
                    ts = ls_ref[s, rows, :]
                out.append(acc[2 * s] + (fr * tc - fi * ts))
                out.append(acc[2 * s + 1] + (fr * ts + fi * tc))
            return tuple(out)

        zero = jnp.zeros((8, width), jnp.float32)
        acc = lax.fori_loop(0, lc_ref.shape[1] // 8, body, (zero,) * (2 * SR))
        part = 1 if upper else 0
        for s in range(SR):
            acc_ref[part, 0, s] = acc[2 * s]
            acc_ref[part, 1, s] = acc[2 * s + 1]

    pass_for(False)
    pass_for(True)
    for a in range(2):
        for b in range(2):
            out_ref[a, b] = jnp.sum(acc_ref[a, b], axis=1)


def spectrum(both_col, turn_cos, turn_sin):
    pixels = both_col.shape[1]
    half = SC // 2
    block = 128
    steps = half // block
    lower = lambda j: (0, 0, j)
    upper = lambda j: (0, 0, j + steps)
    spec = pl.pallas_call(
        spectrum_kernel,
        grid=(steps,),
        in_specs=[
            pl.BlockSpec(memory_space=pltpu.VMEM),
            pl.BlockSpec((SR, pixels, block), lower),
            pl.BlockSpec((SR, pixels, block), lower),
            pl.BlockSpec((SR, pixels, block), upper),
            pl.BlockSpec((SR, pixels, block), upper),
        ],
        out_specs=pl.BlockSpec((2, 2, SR, block), lambda j: (0, 0, 0, j)),
        out_shape=jax.ShapeDtypeStruct((2, 2, SR, half), jnp.float32),
        scratch_shapes=[pltpu.VMEM((2, 2, SR, 8, block), jnp.float32)],
        compiler_params=pltpu.CompilerParams(vmem_limit_bytes=40 * 1024 * 1024),
    )(both_col, turn_cos, turn_sin, turn_cos, turn_sin)
    return spec


def local(frames, offsets, bright, aberration):
    scan_size = lax.axis_size("scan")
    det_size = lax.axis_size("det")
    rows_dev, tile, detector = frames.shape
    owned = offsets.shape[0]
    groups = detector // owned
    owner = lax.axis_index("scan") * det_size + lax.axis_index("det")
    blocks = jnp.transpose(frames.reshape(rows_dev * tile, groups, owned), (1, 0, 2))
    arrived = lax.all_to_all(blocks, ("scan", "det"), split_axis=0, concat_axis=0, tiled=True)
    images = arrived.reshape(scan_size, det_size, rows_dev, tile, owned)
    half = SC // 2
    full_cols = jnp.arange(SC, dtype=jnp.int32)
    col_sin, col_cos = sincos_of_steps(
        jnp.mod(full_cols[:, None] * full_cols[None, :half], SC), SC
    )
    alternating = jnp.where(full_cols % 2 == 0, 1.0, -1.0)
    nyquist = jnp.where(jnp.arange(128)[None, :] == 0, alternating[:, None], 0.0)
    table = jnp.concatenate([col_cos, -col_sin, nyquist], axis=1).astype(jnp.bfloat16)
    both_col = jnp.einsum(
        "abrcp,acq->brpq",
        images,
        table.reshape(scan_size, tile, table.shape[1]),
        preferred_element_type=jnp.float32,
    ).reshape(SR, owned, table.shape[1])
    full_rows = jnp.arange(SR, dtype=jnp.int32)
    angles_by_row = phase_angles(full_rows, full_rows, SR)
    row_cos = jnp.cos(angles_by_row)
    row_sin = jnp.sin(angles_by_row)
    pixel_index = owner * owned + jnp.arange(owned, dtype=jnp.int32)
    steps = jnp.arange(half, dtype=jnp.int32)
    col_index = jnp.concatenate([steps, jnp.mod(SC - steps, SC), jnp.full((1,), half, jnp.int32)])
    row_part, col_part, moved_rows, moved_cols, spherical = phase_parts(
        pixel_index, offsets, aberration, col_index
    )
    moved_sq = moved_rows[:, :, None] + moved_cols.T[None, :, :]
    phase = row_part[:, :, None] + col_part.T[None, :, :] - spherical * (moved_sq * moved_sq)
    weights = bright.astype(jnp.float32)
    keep = (jnp.arange(SC + 1) != half).astype(jnp.float32)
    turn_sin, turn_cos = sincos(phase)
    turn_cos, turn_sin = lax.optimization_barrier(
        (
            turn_cos * weights[None, :, None] * keep[None, None, :],
            turn_sin * weights[None, :, None] * keep[None, None, :],
        )
    )
    parts = spectrum(both_col, turn_cos, turn_sin)
    nyquist_col = both_col[:, :, SC]
    nyquist_real = jnp.dot(row_cos.T, nyquist_col, precision=EXACT_PRECISION)
    nyquist_imag = -jnp.dot(row_sin.T, nyquist_col, precision=EXACT_PRECISION)
    last_cos = turn_cos[:, :, SC]
    last_sin = turn_sin[:, :, SC]
    nyquist_spec_real = jnp.sum(nyquist_real * last_cos - nyquist_imag * last_sin, axis=1)
    nyquist_spec_imag = jnp.sum(nyquist_real * last_sin + nyquist_imag * last_cos, axis=1)
    spectra = jnp.stack(
        [
            jnp.concatenate([parts[0, 0], parts[1, 0], nyquist_spec_real[:, None]], axis=1),
            jnp.concatenate([parts[0, 1], parts[1, 1], nyquist_spec_imag[:, None]], axis=1),
        ]
    )
    inverse_rows = jnp.stack(
        [
            jnp.stack([row_cos.T, -row_sin.T], axis=1),
            jnp.stack([row_sin.T, row_cos.T], axis=1),
        ]
    )
    rows_both = jnp.einsum("jrks,ksq->jrq", inverse_rows, spectra, precision=EXACT_PRECISION)
    rows_real = rows_both[0]
    rows_imag = rows_both[1]
    lanes = 2 * (SC + 1)
    packed = jnp.concatenate(
        [rows_real, rows_imag, jnp.broadcast_to(jnp.sum(weights), (SR, (-lanes) % 128 or 128))],
        axis=1,
    )
    width = tile + 2 * HALO
    columns = jnp.mod(
        lax.axis_index("scan") * tile - HALO + jnp.arange(width, dtype=jnp.int32), SC
    )
    col_angles = phase_angles(col_index, columns, SC)
    final_table = lax.optimization_barrier(
        jnp.concatenate([jnp.cos(col_angles), -jnp.sin(col_angles)], axis=0)
    )
    gathered = lax.all_to_all(packed, "det", 0, 0, tiled=True)
    own = pairwise_sum([gathered[i] for i in range(det_size)])
    spread = jnp.broadcast_to(own, (scan_size,) + own.shape)
    gathered = lax.all_to_all(spread, "scan", 0, 0, tiled=True)
    total = pairwise_sum([gathered[i] for i in range(scan_size)])
    bright_sum = total[lanes]
    picture = jnp.dot(total[:lanes], final_table, precision=EXACT_PRECISION)
    return (
        (picture * (1.0 / (SR * SC)) / jnp.sqrt(bright_sum) * window_weights(width))
        .reshape(rows_dev, 1, width)
    )


def solution(mesh):
    placed = (P("det", "scan", None), P(("scan", "det"), None), P(("scan", "det")), P())
    return jax.shard_map(
        local, mesh=mesh, in_specs=placed, out_specs=P("det", "scan", None), check_vma=False
    )
```

```python
import math

import jax
import jax.numpy as jnp
from jax import lax
from jax.sharding import PartitionSpec as P
from jax.experimental import pallas as pl
from jax.experimental.pallas import tpu as pltpu

SR = 16
SC = 1024
DROWS = 128
DCOLS = 128
HALO = 16


TWO_PI = 2.0 * math.pi
EXACT_PRECISION = lax.Precision.HIGHEST


def phase_angles(first, second_operand, modulus):
    product = jnp.mod(first[:, None] * second_operand[None, :], modulus)
    return TWO_PI / modulus * product.astype(jnp.float32)


def signed_frequency(length):
    position = jnp.arange(length, dtype=jnp.int32)
    folded = jnp.where(position < length // 2, position, position - length)
    return 2.0 * folded.astype(jnp.float32) / length


def pixel_phase(pixel_index, shifts, aberration):
    freq_rows = signed_frequency(SR)[:, None, None]
    freq_cols = signed_frequency(SC)[None, :, None]
    half_rows = DROWS // 2
    half_cols = DCOLS // 2
    tilt_x = ((pixel_index // DCOLS - half_rows).astype(jnp.float32) / half_rows)[None, None, :]
    tilt_y = ((pixel_index % DCOLS - half_cols).astype(jnp.float32) / half_cols)[None, None, :]
    ramp_rows = jnp.mod(jnp.arange(SR, dtype=jnp.int32)[:, None] * shifts[:, 0][None, :], SR)
    ramp_cols = jnp.mod(jnp.arange(SC, dtype=jnp.int32)[:, None] * shifts[:, 1][None, :], SC)
    shift_phase = (
        TWO_PI / SR * ramp_rows.astype(jnp.float32)[:, None, :]
        + TWO_PI / SC * ramp_cols.astype(jnp.float32)[None, :, :]
    )
    tilt_sq = tilt_x * tilt_x + tilt_y * tilt_y
    tilt_dot = tilt_x * freq_rows + tilt_y * freq_cols
    moved_x = freq_rows + tilt_x
    moved_y = freq_cols + tilt_y
    moved_sq = moved_x * moved_x + moved_y * moved_y
    lens_phase = math.pi * (
        aberration[0] * (freq_rows * freq_rows + freq_cols * freq_cols)
        + aberration[1] * (moved_sq * moved_sq - tilt_sq * tilt_sq - 4.0 * tilt_sq * tilt_dot)
    )
    return shift_phase - lens_phase


def window_weights(width):
    position = jnp.arange(width, dtype=jnp.int32)
    nearest = jnp.minimum(position, width - 1 - position)
    ramped = 0.3 + 0.35 * (
        1.0 - jnp.cos(math.pi * (nearest.astype(jnp.float32) + 0.5) / (2 * HALO))
    )
    return jnp.where(nearest < 2 * HALO, ramped, jnp.float32(1.0))


def inverse_transform(spec_real, spec_imag, columns, rows):
    real_piece = jnp.dot(spec_real, cos_cols, precision=EXACT_PRECISION) - jnp.dot(
        spec_imag, sin_cols, precision=EXACT_PRECISION
    )
    imaginary_piece = jnp.dot(spec_real, sin_cols, precision=EXACT_PRECISION) + jnp.dot(
        spec_imag, cos_cols, precision=EXACT_PRECISION
    )
    angles_by_row = phase_angles(jnp.arange(SR, dtype=jnp.int32), rows, SR)
    row_cosines = jnp.cos(angles_by_row)
    row_sines = jnp.sin(angles_by_row)
    return jnp.dot(row_cosines.T, real_piece, precision=EXACT_PRECISION) - jnp.dot(
        row_sines.T, imaginary_piece, precision=EXACT_PRECISION
    )


def sincos_reduced(rest, quadrant):
    square = rest * rest
    sine = rest + rest * square * (
        -1.6666654611e-1 + square * (8.3321608736e-3 + square * -1.9515295891e-4)
    )
    cosine = 1.0 - 0.5 * square + square * square * (
        4.166664568298827e-2 + square * (-1.388731625493765e-3 + square * 2.443315711809948e-5)
    )
    swap = (quadrant & 1) == 1
    sin_out = jnp.where(swap, cosine, sine)
    cos_out = jnp.where(swap, sine, cosine)
    sin_out = jnp.where(quadrant >= 2, -sin_out, sin_out)
    cos_out = jnp.where((quadrant == 1) | (quadrant == 2), -cos_out, cos_out)
    return sin_out, cos_out


def sincos(angle):
    turns = jnp.round(angle * (2.0 / math.pi))
    quadrant = turns.astype(jnp.int32) & 3
    rest = angle - turns * 1.5703125
    rest = rest - turns * 4.837512969970703125e-4
    rest = rest - turns * 7.54978995489188216e-8
    return sincos_reduced(rest, quadrant)


def sincos_of_steps(steps, modulus):
    quarter = modulus // 4
    turns = (steps + quarter // 2) // quarter
    rest = (steps - turns * quarter).astype(jnp.float32) * (TWO_PI / modulus)
    return sincos_reduced(rest, turns & 3)


def pairwise_sum(values):
    while len(values) > 1:
        values = [
            values[e] + values[e + 1] if e + 1 < len(values) else values[e]
            for e in range(0, len(values), 2)
        ]
    return values[0]


def phase_parts(pixel_index, shifts, aberration, col_index):
    freq_rows = signed_frequency(SR)[:, None]
    freq_cols = (2.0 * jnp.where(col_index < SC // 2, col_index, col_index - SC).astype(jnp.float32) / SC)[:, None]
    half_rows = DROWS // 2
    half_cols = DCOLS // 2
    tilt_x = ((pixel_index // DCOLS - half_rows).astype(jnp.float32) / half_rows)[None, :]
    tilt_y = ((pixel_index % DCOLS - half_cols).astype(jnp.float32) / half_cols)[None, :]
    ramp_rows = jnp.mod(jnp.arange(SR, dtype=jnp.int32)[:, None] * shifts[:, 0][None, :], SR)
    ramp_cols = jnp.mod(col_index[:, None] * shifts[:, 1][None, :], SC)
    tilt_sq = tilt_x * tilt_x + tilt_y * tilt_y
    defocus = math.pi * aberration[0]
    spherical = math.pi * aberration[1]
    row_part = (
        TWO_PI / SR * ramp_rows.astype(jnp.float32)
        - defocus * freq_rows * freq_rows
        + spherical * (tilt_sq * tilt_sq + 4.0 * tilt_sq * tilt_x * freq_rows)
    )
    col_part = (
        TWO_PI / SC * ramp_cols.astype(jnp.float32)
        - defocus * freq_cols * freq_cols
        + spherical * (4.0 * tilt_sq * tilt_y * freq_cols)
    )
    moved_rows = (freq_rows + tilt_x) * (freq_rows + tilt_x)
    moved_cols = (freq_cols + tilt_y) * (freq_cols + tilt_y)
    return row_part, col_part, moved_rows, moved_cols, spherical


def four_point(points):
    (ar, ai), (br, bi), (cr, ci), (dr, di) = points
    s02r = ar + cr
    s02i = ai + ci
    d02r = ar - cr
    d02i = ai - ci
    s13r = br + dr
    s13i = bi + di
    d13r = br - dr
    d13i = bi - di
    return [
        (s02r + s13r, s02i + s13i),
        (d02r + d13i, d02i - d13r),
        (s02r - s13r, s02i - s13i),
        (d02r - d13i, d02i + d13r),
    ]


def fft16(points):
    twisted = {}
    for b in range(4):
        column = four_point([points[4 * a + b] for a in range(4)])
        for s1, (gr, gi) in enumerate(column):
            k = b * s1
            if k == 0:
                twisted[b, s1] = (gr, gi)
            elif k == 4:
                twisted[b, s1] = (gi, -gr)
            else:
                c = math.cos(TWO_PI * k / 16)
                d = math.sin(TWO_PI * k / 16)
                twisted[b, s1] = (gr * c + gi * d, gi * c - gr * d)
    out = [None] * 16
    for s1 in range(4):
        row = four_point([twisted[b, s1] for b in range(4)])
        for s2 in range(4):
            out[s1 + 4 * s2] = row[s2]
    return out


def spectrum_kernel(y_ref, lc_ref, ls_ref, uc_ref, us_ref, out_ref, acc_ref):
    acc_ref[...] = jnp.zeros(acc_ref.shape, acc_ref.dtype)
    width = lc_ref.shape[2]
    low = pl.multiple_of(pl.program_id(0) * width, width)
    high = pl.multiple_of(pl.program_id(0) * width + SC // 2, width)

    def body(i, carry):
        rows = pl.ds(pl.multiple_of(i * 8, 8), 8)
        full = fft16(
            [(y_ref[r, rows, pl.ds(low, width)], y_ref[r, rows, pl.ds(high, width)]) for r in range(SR)]
        )
        for s in range(SR):
            fr, fi = full[s]
            tc = lc_ref[s, rows, :]
            ts = ls_ref[s, rows, :]
            acc_ref[0, 0, s] += fr * tc - fi * ts
            acc_ref[0, 1, s] += fr * ts + fi * tc
            gr, gi = full[(SR - s) % SR]
            tc = uc_ref[s, rows, :]
            ts = us_ref[s, rows, :]
            acc_ref[1, 0, s] += gr * tc + gi * ts
            acc_ref[1, 1, s] += gr * ts - gi * tc
        return carry

    lax.fori_loop(0, lc_ref.shape[1] // 8, body, 0, unroll=2)
    for a in range(2):
        for b in range(2):
            out_ref[a, b] = jnp.sum(acc_ref[a, b], axis=1)


def spectrum(both_col, turn_cos, turn_sin):
    pixels = both_col.shape[1]
    half = SC // 2
    block = 128
    steps = half // block
    lower = lambda j: (0, 0, j)
    upper = lambda j: (0, 0, j + steps)
    spec = pl.pallas_call(
        spectrum_kernel,
        grid=(steps,),
        in_specs=[
            pl.BlockSpec(memory_space=pltpu.VMEM),
            pl.BlockSpec((SR, pixels, block), lower),
            pl.BlockSpec((SR, pixels, block), lower),
            pl.BlockSpec((SR, pixels, block), upper),
            pl.BlockSpec((SR, pixels, block), upper),
        ],
        out_specs=pl.BlockSpec((2, 2, SR, block), lambda j: (0, 0, 0, j)),
        out_shape=jax.ShapeDtypeStruct((2, 2, SR, half), jnp.float32),
        scratch_shapes=[pltpu.VMEM((2, 2, SR, 8, block), jnp.float32)],
        compiler_params=pltpu.CompilerParams(vmem_limit_bytes=40 * 1024 * 1024),
    )(both_col, turn_cos, turn_sin, turn_cos, turn_sin)
    return spec


def local(frames, offsets, bright, aberration):
    scan_size = lax.axis_size("scan")
    det_size = lax.axis_size("det")
    rows_dev, tile, detector = frames.shape
    owned = offsets.shape[0]
    groups = detector // owned
    owner = lax.axis_index("scan") * det_size + lax.axis_index("det")
    blocks = jnp.transpose(frames.reshape(rows_dev * tile, groups, owned), (1, 0, 2))
    arrived = lax.all_to_all(blocks, ("scan", "det"), split_axis=0, concat_axis=0, tiled=True)
    images = arrived.reshape(scan_size, det_size, rows_dev, tile, owned)
    half = SC // 2
    full_cols = jnp.arange(SC, dtype=jnp.int32)
    col_sin, col_cos = sincos_of_steps(
        jnp.mod(full_cols[:, None] * full_cols[None, :half], SC), SC
    )
    alternating = jnp.where(full_cols % 2 == 0, 1.0, -1.0)
    nyquist = jnp.where(jnp.arange(128)[None, :] == 0, alternating[:, None], 0.0)
    table = jnp.concatenate([col_cos, -col_sin, nyquist], axis=1).astype(jnp.bfloat16)
    both_col = jnp.einsum(
        "abrcp,acq->brpq",
        images,
        table.reshape(scan_size, tile, table.shape[1]),
        preferred_element_type=jnp.float32,
    ).reshape(SR, owned, table.shape[1])
    full_rows = jnp.arange(SR, dtype=jnp.int32)
    angles_by_row = phase_angles(full_rows, full_rows, SR)
    row_cos = jnp.cos(angles_by_row)
    row_sin = jnp.sin(angles_by_row)
    pixel_index = owner * owned + jnp.arange(owned, dtype=jnp.int32)
    steps = jnp.arange(half, dtype=jnp.int32)
    col_index = jnp.concatenate([steps, jnp.mod(SC - steps, SC), jnp.full((1,), half, jnp.int32)])
    row_part, col_part, moved_rows, moved_cols, spherical = phase_parts(
        pixel_index, offsets, aberration, col_index
    )
    moved_sq = moved_rows[:, :, None] + moved_cols.T[None, :, :]
    phase = row_part[:, :, None] + col_part.T[None, :, :] - spherical * (moved_sq * moved_sq)
    weights = bright.astype(jnp.float32)
    keep = (jnp.arange(SC + 1) != half).astype(jnp.float32)
    turn_sin, turn_cos = sincos(phase)
    turn_cos, turn_sin = lax.optimization_barrier(
        (
            turn_cos * weights[None, :, None] * keep[None, None, :],
            turn_sin * weights[None, :, None] * keep[None, None, :],
        )
    )
    parts = spectrum(both_col, turn_cos, turn_sin)
    nyquist_col = both_col[:, :, SC]
    nyquist_real = jnp.dot(row_cos.T, nyquist_col, precision=EXACT_PRECISION)
    nyquist_imag = -jnp.dot(row_sin.T, nyquist_col, precision=EXACT_PRECISION)
    last_cos = turn_cos[:, :, SC]
    last_sin = turn_sin[:, :, SC]
    nyquist_spec_real = jnp.sum(nyquist_real * last_cos - nyquist_imag * last_sin, axis=1)
    nyquist_spec_imag = jnp.sum(nyquist_real * last_sin + nyquist_imag * last_cos, axis=1)
    spectra = jnp.stack(
        [
            jnp.concatenate([parts[0, 0], parts[1, 0], nyquist_spec_real[:, None]], axis=1),
            jnp.concatenate([parts[0, 1], parts[1, 1], nyquist_spec_imag[:, None]], axis=1),
        ]
    )
    inverse_rows = jnp.stack(
        [
            jnp.stack([row_cos.T, -row_sin.T], axis=1),
            jnp.stack([row_sin.T, row_cos.T], axis=1),
        ]
    )
    rows_both = jnp.einsum("jrks,ksq->jrq", inverse_rows, spectra, precision=EXACT_PRECISION)
    rows_real = rows_both[0]
    rows_imag = rows_both[1]
    lanes = 2 * (SC + 1)
    packed = jnp.concatenate(
        [rows_real, rows_imag, jnp.broadcast_to(jnp.sum(weights), (SR, (-lanes) % 128 or 128))],
        axis=1,
    )
    width = tile + 2 * HALO
    columns = jnp.mod(
        lax.axis_index("scan") * tile - HALO + jnp.arange(width, dtype=jnp.int32), SC
    )
    col_angles = phase_angles(col_index, columns, SC)
    final_table = lax.optimization_barrier(
        jnp.concatenate([jnp.cos(col_angles), -jnp.sin(col_angles)], axis=0)
    )
    gathered = lax.all_to_all(packed, "det", 0, 0, tiled=True)
    own = pairwise_sum([gathered[i] for i in range(det_size)])
    spread = jnp.broadcast_to(own, (scan_size,) + own.shape)
    gathered = lax.all_to_all(spread, "scan", 0, 0, tiled=True)
    total = pairwise_sum([gathered[i] for i in range(scan_size)])
    bright_sum = total[lanes]
    picture = jnp.dot(total[:lanes], final_table, precision=EXACT_PRECISION)
    return (
        (picture * (1.0 / (SR * SC)) / jnp.sqrt(bright_sum) * window_weights(width))
        .reshape(rows_dev, 1, width)
    )


def solution(mesh):
    placed = (P("det", "scan", None), P(("scan", "det"), None), P(("scan", "det")), P())
    return jax.shard_map(
        local, mesh=mesh, in_specs=placed, out_specs=P("det", "scan", None), check_vma=False
    )
```

```python
import math

import jax
import jax.numpy as jnp
from jax import lax
from jax.sharding import PartitionSpec as P
from jax.experimental import pallas as pl
from jax.experimental.pallas import tpu as pltpu

SR = 16
SC = 1024
DROWS = 128
DCOLS = 128
HALO = 16


TWO_PI = 2.0 * math.pi
EXACT_PRECISION = lax.Precision.HIGHEST


def phase_angles(first, second_operand, modulus):
    product = jnp.mod(first[:, None] * second_operand[None, :], modulus)
    return TWO_PI / modulus * product.astype(jnp.float32)


def signed_frequency(length):
    position = jnp.arange(length, dtype=jnp.int32)
    folded = jnp.where(position < length // 2, position, position - length)
    return 2.0 * folded.astype(jnp.float32) / length


def pixel_phase(pixel_index, shifts, aberration):
    freq_rows = signed_frequency(SR)[:, None, None]
    freq_cols = signed_frequency(SC)[None, :, None]
    half_rows = DROWS // 2
    half_cols = DCOLS // 2
    tilt_x = ((pixel_index // DCOLS - half_rows).astype(jnp.float32) / half_rows)[None, None, :]
    tilt_y = ((pixel_index % DCOLS - half_cols).astype(jnp.float32) / half_cols)[None, None, :]
    ramp_rows = jnp.mod(jnp.arange(SR, dtype=jnp.int32)[:, None] * shifts[:, 0][None, :], SR)
    ramp_cols = jnp.mod(jnp.arange(SC, dtype=jnp.int32)[:, None] * shifts[:, 1][None, :], SC)
    shift_phase = (
        TWO_PI / SR * ramp_rows.astype(jnp.float32)[:, None, :]
        + TWO_PI / SC * ramp_cols.astype(jnp.float32)[None, :, :]
    )
    tilt_sq = tilt_x * tilt_x + tilt_y * tilt_y
    tilt_dot = tilt_x * freq_rows + tilt_y * freq_cols
    moved_x = freq_rows + tilt_x
    moved_y = freq_cols + tilt_y
    moved_sq = moved_x * moved_x + moved_y * moved_y
    lens_phase = math.pi * (
        aberration[0] * (freq_rows * freq_rows + freq_cols * freq_cols)
        + aberration[1] * (moved_sq * moved_sq - tilt_sq * tilt_sq - 4.0 * tilt_sq * tilt_dot)
    )
    return shift_phase - lens_phase


def window_weights(width):
    position = jnp.arange(width, dtype=jnp.int32)
    nearest = jnp.minimum(position, width - 1 - position)
    ramped = 0.3 + 0.35 * (
        1.0 - jnp.cos(math.pi * (nearest.astype(jnp.float32) + 0.5) / (2 * HALO))
    )
    return jnp.where(nearest < 2 * HALO, ramped, jnp.float32(1.0))


def inverse_transform(spec_real, spec_imag, columns, rows):
    real_piece = jnp.dot(spec_real, cos_cols, precision=EXACT_PRECISION) - jnp.dot(
        spec_imag, sin_cols, precision=EXACT_PRECISION
    )
    imaginary_piece = jnp.dot(spec_real, sin_cols, precision=EXACT_PRECISION) + jnp.dot(
        spec_imag, cos_cols, precision=EXACT_PRECISION
    )
    angles_by_row = phase_angles(jnp.arange(SR, dtype=jnp.int32), rows, SR)
    row_cosines = jnp.cos(angles_by_row)
    row_sines = jnp.sin(angles_by_row)
    return jnp.dot(row_cosines.T, real_piece, precision=EXACT_PRECISION) - jnp.dot(
        row_sines.T, imaginary_piece, precision=EXACT_PRECISION
    )


def sincos_reduced(rest, quadrant):
    square = rest * rest
    sine = rest + rest * square * (
        -1.6666654611e-1 + square * (8.3321608736e-3 + square * -1.9515295891e-4)
    )
    cosine = 1.0 - 0.5 * square + square * square * (
        4.166664568298827e-2 + square * (-1.388731625493765e-3 + square * 2.443315711809948e-5)
    )
    swap = (quadrant & 1) == 1
    sin_out = jnp.where(swap, cosine, sine)
    cos_out = jnp.where(swap, sine, cosine)
    sin_out = jnp.where(quadrant >= 2, -sin_out, sin_out)
    cos_out = jnp.where((quadrant == 1) | (quadrant == 2), -cos_out, cos_out)
    return sin_out, cos_out


def sincos(angle):
    turns = jnp.round(angle * (2.0 / math.pi))
    quadrant = turns.astype(jnp.int32) & 3
    rest = angle - turns * 1.5703125
    rest = rest - turns * 4.837512969970703125e-4
    rest = rest - turns * 7.54978995489188216e-8
    return sincos_reduced(rest, quadrant)


def sincos_of_steps(steps, modulus):
    quarter = modulus // 4
    turns = (steps + quarter // 2) // quarter
    rest = (steps - turns * quarter).astype(jnp.float32) * (TWO_PI / modulus)
    return sincos_reduced(rest, turns & 3)


def pairwise_sum(values):
    while len(values) > 1:
        values = [
            values[e] + values[e + 1] if e + 1 < len(values) else values[e]
            for e in range(0, len(values), 2)
        ]
    return values[0]


def phase_parts(pixel_index, shifts, aberration, col_index):
    freq_rows = signed_frequency(SR)[:, None]
    freq_cols = (2.0 * jnp.where(col_index < SC // 2, col_index, col_index - SC).astype(jnp.float32) / SC)[:, None]
    half_rows = DROWS // 2
    half_cols = DCOLS // 2
    tilt_x = ((pixel_index // DCOLS - half_rows).astype(jnp.float32) / half_rows)[None, :]
    tilt_y = ((pixel_index % DCOLS - half_cols).astype(jnp.float32) / half_cols)[None, :]
    ramp_rows = jnp.mod(jnp.arange(SR, dtype=jnp.int32)[:, None] * shifts[:, 0][None, :], SR)
    ramp_cols = jnp.mod(col_index[:, None] * shifts[:, 1][None, :], SC)
    tilt_sq = tilt_x * tilt_x + tilt_y * tilt_y
    defocus = math.pi * aberration[0]
    spherical = math.pi * aberration[1]
    row_part = (
        TWO_PI / SR * ramp_rows.astype(jnp.float32)
        - defocus * freq_rows * freq_rows
        + spherical * (tilt_sq * tilt_sq + 4.0 * tilt_sq * tilt_x * freq_rows)
    )
    col_part = (
        TWO_PI / SC * ramp_cols.astype(jnp.float32)
        - defocus * freq_cols * freq_cols
        + spherical * (4.0 * tilt_sq * tilt_y * freq_cols)
    )
    moved_rows = (freq_rows + tilt_x) * (freq_rows + tilt_x)
    moved_cols = (freq_cols + tilt_y) * (freq_cols + tilt_y)
    return row_part, col_part, moved_rows, moved_cols, spherical


def four_point(points):
    (ar, ai), (br, bi), (cr, ci), (dr, di) = points
    s02r = ar + cr
    s02i = ai + ci
    d02r = ar - cr
    d02i = ai - ci
    s13r = br + dr
    s13i = bi + di
    d13r = br - dr
    d13i = bi - di
    return [
        (s02r + s13r, s02i + s13i),
        (d02r + d13i, d02i - d13r),
        (s02r - s13r, s02i - s13i),
        (d02r - d13i, d02i + d13r),
    ]


def fft16(points):
    twisted = {}
    for b in range(4):
        column = four_point([points[4 * a + b] for a in range(4)])
        for s1, (gr, gi) in enumerate(column):
            k = b * s1
            if k == 0:
                twisted[b, s1] = (gr, gi)
            elif k == 4:
                twisted[b, s1] = (gi, -gr)
            else:
                c = math.cos(TWO_PI * k / 16)
                d = math.sin(TWO_PI * k / 16)
                twisted[b, s1] = (gr * c + gi * d, gi * c - gr * d)
    out = [None] * 16
    for s1 in range(4):
        row = four_point([twisted[b, s1] for b in range(4)])
        for s2 in range(4):
            out[s1 + 4 * s2] = row[s2]
    return out


def spectrum_kernel(y_ref, lc_ref, ls_ref, uc_ref, us_ref, out_ref, acc_ref):
    acc_ref[...] = jnp.zeros(acc_ref.shape, acc_ref.dtype)
    width = lc_ref.shape[2]
    low = pl.multiple_of(pl.program_id(0) * width, width)
    high = pl.multiple_of(pl.program_id(0) * width + SC // 2, width)

    def body(i, carry):
        rows = pl.ds(pl.multiple_of(i * 8, 8), 8)
        full = fft16(
            [(y_ref[r, rows, pl.ds(low, width)], y_ref[r, rows, pl.ds(high, width)]) for r in range(SR)]
        )
        for s in range(SR):
            fr, fi = full[s]
            tc = lc_ref[s, rows, :]
            ts = ls_ref[s, rows, :]
            acc_ref[0, 0, s] += fr * tc - fi * ts
            acc_ref[0, 1, s] += fr * ts + fi * tc
            gr, gi = full[(SR - s) % SR]
            tc = uc_ref[s, rows, :]
            ts = us_ref[s, rows, :]
            acc_ref[1, 0, s] += gr * tc + gi * ts
            acc_ref[1, 1, s] += gr * ts - gi * tc
        return carry

    lax.fori_loop(0, lc_ref.shape[1] // 8, body, 0, unroll=4)
    for a in range(2):
        for b in range(2):
            out_ref[a, b] = jnp.sum(acc_ref[a, b], axis=1)


def spectrum(both_col, turn_cos, turn_sin):
    pixels = both_col.shape[1]
    half = SC // 2
    block = 128
    steps = half // block
    lower = lambda j: (0, 0, j)
    upper = lambda j: (0, 0, j + steps)
    spec = pl.pallas_call(
        spectrum_kernel,
        grid=(steps,),
        in_specs=[
            pl.BlockSpec(memory_space=pltpu.VMEM),
            pl.BlockSpec((SR, pixels, block), lower),
            pl.BlockSpec((SR, pixels, block), lower),
            pl.BlockSpec((SR, pixels, block), upper),
            pl.BlockSpec((SR, pixels, block), upper),
        ],
        out_specs=pl.BlockSpec((2, 2, SR, block), lambda j: (0, 0, 0, j)),
        out_shape=jax.ShapeDtypeStruct((2, 2, SR, half), jnp.float32),
        scratch_shapes=[pltpu.VMEM((2, 2, SR, 8, block), jnp.float32)],
        compiler_params=pltpu.CompilerParams(vmem_limit_bytes=40 * 1024 * 1024),
    )(both_col, turn_cos, turn_sin, turn_cos, turn_sin)
    return spec


def local(frames, offsets, bright, aberration):
    scan_size = lax.axis_size("scan")
    det_size = lax.axis_size("det")
    rows_dev, tile, detector = frames.shape
    owned = offsets.shape[0]
    groups = detector // owned
    owner = lax.axis_index("scan") * det_size + lax.axis_index("det")
    blocks = jnp.transpose(frames.reshape(rows_dev * tile, groups, owned), (1, 0, 2))
    arrived = lax.all_to_all(blocks, ("scan", "det"), split_axis=0, concat_axis=0, tiled=True)
    images = arrived.reshape(scan_size, det_size, rows_dev, tile, owned)
    half = SC // 2
    full_cols = jnp.arange(SC, dtype=jnp.int32)
    col_sin, col_cos = sincos_of_steps(
        jnp.mod(full_cols[:, None] * full_cols[None, :half], SC), SC
    )
    alternating = jnp.where(full_cols % 2 == 0, 1.0, -1.0)
    nyquist = jnp.where(jnp.arange(128)[None, :] == 0, alternating[:, None], 0.0)
    table = jnp.concatenate([col_cos, -col_sin, nyquist], axis=1).astype(jnp.bfloat16)
    both_col = jnp.einsum(
        "abrcp,acq->brpq",
        images,
        table.reshape(scan_size, tile, table.shape[1]),
        preferred_element_type=jnp.float32,
    ).reshape(SR, owned, table.shape[1])
    full_rows = jnp.arange(SR, dtype=jnp.int32)
    angles_by_row = phase_angles(full_rows, full_rows, SR)
    row_cos = jnp.cos(angles_by_row)
    row_sin = jnp.sin(angles_by_row)
    pixel_index = owner * owned + jnp.arange(owned, dtype=jnp.int32)
    steps = jnp.arange(half, dtype=jnp.int32)
    col_index = jnp.concatenate([steps, jnp.mod(SC - steps, SC), jnp.full((1,), half, jnp.int32)])
    row_part, col_part, moved_rows, moved_cols, spherical = phase_parts(
        pixel_index, offsets, aberration, col_index
    )
    moved_sq = moved_rows[:, :, None] + moved_cols.T[None, :, :]
    phase = row_part[:, :, None] + col_part.T[None, :, :] - spherical * (moved_sq * moved_sq)
    weights = bright.astype(jnp.float32)
    keep = (jnp.arange(SC + 1) != half).astype(jnp.float32)
    turn_sin, turn_cos = sincos(phase)
    turn_cos, turn_sin = lax.optimization_barrier(
        (
            turn_cos * weights[None, :, None] * keep[None, None, :],
            turn_sin * weights[None, :, None] * keep[None, None, :],
        )
    )
    parts = spectrum(both_col, turn_cos, turn_sin)
    nyquist_col = both_col[:, :, SC]
    nyquist_real = jnp.dot(row_cos.T, nyquist_col, precision=EXACT_PRECISION)
    nyquist_imag = -jnp.dot(row_sin.T, nyquist_col, precision=EXACT_PRECISION)
    last_cos = turn_cos[:, :, SC]
    last_sin = turn_sin[:, :, SC]
    nyquist_spec_real = jnp.sum(nyquist_real * last_cos - nyquist_imag * last_sin, axis=1)
    nyquist_spec_imag = jnp.sum(nyquist_real * last_sin + nyquist_imag * last_cos, axis=1)
    spectra = jnp.stack(
        [
            jnp.concatenate([parts[0, 0], parts[1, 0], nyquist_spec_real[:, None]], axis=1),
            jnp.concatenate([parts[0, 1], parts[1, 1], nyquist_spec_imag[:, None]], axis=1),
        ]
    )
    inverse_rows = jnp.stack(
        [
            jnp.stack([row_cos.T, -row_sin.T], axis=1),
            jnp.stack([row_sin.T, row_cos.T], axis=1),
        ]
    )
    rows_both = jnp.einsum("jrks,ksq->jrq", inverse_rows, spectra, precision=EXACT_PRECISION)
    rows_real = rows_both[0]
    rows_imag = rows_both[1]
    lanes = 2 * (SC + 1)
    packed = jnp.concatenate(
        [rows_real, rows_imag, jnp.broadcast_to(jnp.sum(weights), (SR, (-lanes) % 128 or 128))],
        axis=1,
    )
    width = tile + 2 * HALO
    columns = jnp.mod(
        lax.axis_index("scan") * tile - HALO + jnp.arange(width, dtype=jnp.int32), SC
    )
    col_angles = phase_angles(col_index, columns, SC)
    final_table = lax.optimization_barrier(
        jnp.concatenate([jnp.cos(col_angles), -jnp.sin(col_angles)], axis=0)
    )
    gathered = lax.all_to_all(packed, "det", 0, 0, tiled=True)
    own = pairwise_sum([gathered[i] for i in range(det_size)])
    spread = jnp.broadcast_to(own, (scan_size,) + own.shape)
    gathered = lax.all_to_all(spread, "scan", 0, 0, tiled=True)
    total = pairwise_sum([gathered[i] for i in range(scan_size)])
    bright_sum = total[lanes]
    picture = jnp.dot(total[:lanes], final_table, precision=EXACT_PRECISION)
    return (
        (picture * (1.0 / (SR * SC)) / jnp.sqrt(bright_sum) * window_weights(width))
        .reshape(rows_dev, 1, width)
    )


def solution(mesh):
    placed = (P("det", "scan", None), P(("scan", "det"), None), P(("scan", "det")), P())
    return jax.shard_map(
        local, mesh=mesh, in_specs=placed, out_specs=P("det", "scan", None), check_vma=False
    )
```

```python
import math

import jax
import jax.numpy as jnp
from jax import lax
from jax.sharding import PartitionSpec as P
from jax.experimental import pallas as pl
from jax.experimental.pallas import tpu as pltpu

SR = 16
SC = 1024
DROWS = 128
DCOLS = 128
HALO = 16


TWO_PI = 2.0 * math.pi
EXACT_PRECISION = lax.Precision.HIGHEST


def phase_angles(first, second_operand, modulus):
    product = jnp.mod(first[:, None] * second_operand[None, :], modulus)
    return TWO_PI / modulus * product.astype(jnp.float32)


def signed_frequency(length):
    position = jnp.arange(length, dtype=jnp.int32)
    folded = jnp.where(position < length // 2, position, position - length)
    return 2.0 * folded.astype(jnp.float32) / length


def pixel_phase(pixel_index, shifts, aberration):
    freq_rows = signed_frequency(SR)[:, None, None]
    freq_cols = signed_frequency(SC)[None, :, None]
    half_rows = DROWS // 2
    half_cols = DCOLS // 2
    tilt_x = ((pixel_index // DCOLS - half_rows).astype(jnp.float32) / half_rows)[None, None, :]
    tilt_y = ((pixel_index % DCOLS - half_cols).astype(jnp.float32) / half_cols)[None, None, :]
    ramp_rows = jnp.mod(jnp.arange(SR, dtype=jnp.int32)[:, None] * shifts[:, 0][None, :], SR)
    ramp_cols = jnp.mod(jnp.arange(SC, dtype=jnp.int32)[:, None] * shifts[:, 1][None, :], SC)
    shift_phase = (
        TWO_PI / SR * ramp_rows.astype(jnp.float32)[:, None, :]
        + TWO_PI / SC * ramp_cols.astype(jnp.float32)[None, :, :]
    )
    tilt_sq = tilt_x * tilt_x + tilt_y * tilt_y
    tilt_dot = tilt_x * freq_rows + tilt_y * freq_cols
    moved_x = freq_rows + tilt_x
    moved_y = freq_cols + tilt_y
    moved_sq = moved_x * moved_x + moved_y * moved_y
    lens_phase = math.pi * (
        aberration[0] * (freq_rows * freq_rows + freq_cols * freq_cols)
        + aberration[1] * (moved_sq * moved_sq - tilt_sq * tilt_sq - 4.0 * tilt_sq * tilt_dot)
    )
    return shift_phase - lens_phase


def window_weights(width):
    position = jnp.arange(width, dtype=jnp.int32)
    nearest = jnp.minimum(position, width - 1 - position)
    ramped = 0.3 + 0.35 * (
        1.0 - jnp.cos(math.pi * (nearest.astype(jnp.float32) + 0.5) / (2 * HALO))
    )
    return jnp.where(nearest < 2 * HALO, ramped, jnp.float32(1.0))


def inverse_transform(spec_real, spec_imag, columns, rows):
    real_piece = jnp.dot(spec_real, cos_cols, precision=EXACT_PRECISION) - jnp.dot(
        spec_imag, sin_cols, precision=EXACT_PRECISION
    )
    imaginary_piece = jnp.dot(spec_real, sin_cols, precision=EXACT_PRECISION) + jnp.dot(
        spec_imag, cos_cols, precision=EXACT_PRECISION
    )
    angles_by_row = phase_angles(jnp.arange(SR, dtype=jnp.int32), rows, SR)
    row_cosines = jnp.cos(angles_by_row)
    row_sines = jnp.sin(angles_by_row)
    return jnp.dot(row_cosines.T, real_piece, precision=EXACT_PRECISION) - jnp.dot(
        row_sines.T, imaginary_piece, precision=EXACT_PRECISION
    )


def sincos_reduced(rest, quadrant):
    square = rest * rest
    sine = rest + rest * square * (
        -1.6666654611e-1 + square * (8.3321608736e-3 + square * -1.9515295891e-4)
    )
    cosine = 1.0 - 0.5 * square + square * square * (
        4.166664568298827e-2 + square * (-1.388731625493765e-3 + square * 2.443315711809948e-5)
    )
    swap = (quadrant & 1) == 1
    sin_out = jnp.where(swap, cosine, sine)
    cos_out = jnp.where(swap, sine, cosine)
    sin_out = jnp.where(quadrant >= 2, -sin_out, sin_out)
    cos_out = jnp.where((quadrant == 1) | (quadrant == 2), -cos_out, cos_out)
    return sin_out, cos_out


def sincos(angle):
    turns = jnp.round(angle * (2.0 / math.pi))
    quadrant = turns.astype(jnp.int32) & 3
    rest = angle - turns * 1.5703125
    rest = rest - turns * 4.837512969970703125e-4
    rest = rest - turns * 7.54978995489188216e-8
    return sincos_reduced(rest, quadrant)


def sincos_of_steps(steps, modulus):
    quarter = modulus // 4
    turns = (steps + quarter // 2) // quarter
    rest = (steps - turns * quarter).astype(jnp.float32) * (TWO_PI / modulus)
    return sincos_reduced(rest, turns & 3)


def pairwise_sum(values):
    while len(values) > 1:
        values = [
            values[e] + values[e + 1] if e + 1 < len(values) else values[e]
            for e in range(0, len(values), 2)
        ]
    return values[0]


def phase_parts(pixel_index, shifts, aberration, col_index):
    freq_rows = signed_frequency(SR)[:, None]
    freq_cols = (2.0 * jnp.where(col_index < SC // 2, col_index, col_index - SC).astype(jnp.float32) / SC)[:, None]
    half_rows = DROWS // 2
    half_cols = DCOLS // 2
    tilt_x = ((pixel_index // DCOLS - half_rows).astype(jnp.float32) / half_rows)[None, :]
    tilt_y = ((pixel_index % DCOLS - half_cols).astype(jnp.float32) / half_cols)[None, :]
    ramp_rows = jnp.mod(jnp.arange(SR, dtype=jnp.int32)[:, None] * shifts[:, 0][None, :], SR)
    ramp_cols = jnp.mod(col_index[:, None] * shifts[:, 1][None, :], SC)
    tilt_sq = tilt_x * tilt_x + tilt_y * tilt_y
    defocus = math.pi * aberration[0]
    spherical = math.pi * aberration[1]
    row_part = (
        TWO_PI / SR * ramp_rows.astype(jnp.float32)
        - defocus * freq_rows * freq_rows
        + spherical * (tilt_sq * tilt_sq + 4.0 * tilt_sq * tilt_x * freq_rows)
    )
    col_part = (
        TWO_PI / SC * ramp_cols.astype(jnp.float32)
        - defocus * freq_cols * freq_cols
        + spherical * (4.0 * tilt_sq * tilt_y * freq_cols)
    )
    moved_rows = (freq_rows + tilt_x) * (freq_rows + tilt_x)
    moved_cols = (freq_cols + tilt_y) * (freq_cols + tilt_y)
    return row_part, col_part, moved_rows, moved_cols, spherical


def four_point(points):
    (ar, ai), (br, bi), (cr, ci), (dr, di) = points
    s02r = ar + cr
    s02i = ai + ci
    d02r = ar - cr
    d02i = ai - ci
    s13r = br + dr
    s13i = bi + di
    d13r = br - dr
    d13i = bi - di
    return [
        (s02r + s13r, s02i + s13i),
        (d02r + d13i, d02i - d13r),
        (s02r - s13r, s02i - s13i),
        (d02r - d13i, d02i + d13r),
    ]


def fft16(points):
    twisted = {}
    for b in range(4):
        column = four_point([points[4 * a + b] for a in range(4)])
        for s1, (gr, gi) in enumerate(column):
            k = b * s1
            if k == 0:
                twisted[b, s1] = (gr, gi)
            elif k == 4:
                twisted[b, s1] = (gi, -gr)
            elif k == 2:
                half_root = math.sqrt(0.5)
                twisted[b, s1] = ((gr + gi) * half_root, (gi - gr) * half_root)
            elif k == 6:
                half_root = math.sqrt(0.5)
                twisted[b, s1] = ((gi - gr) * half_root, -(gi + gr) * half_root)
            else:
                c = math.cos(TWO_PI * k / 16)
                d = math.sin(TWO_PI * k / 16)
                twisted[b, s1] = (gr * c + gi * d, gi * c - gr * d)
    out = [None] * 16
    for s1 in range(4):
        row = four_point([twisted[b, s1] for b in range(4)])
        for s2 in range(4):
            out[s1 + 4 * s2] = row[s2]
    return out


def spectrum_kernel(y_ref, lc_ref, ls_ref, uc_ref, us_ref, out_ref, acc_ref):
    acc_ref[...] = jnp.zeros(acc_ref.shape, acc_ref.dtype)
    width = lc_ref.shape[2]
    low = pl.multiple_of(pl.program_id(0) * width, width)
    high = pl.multiple_of(pl.program_id(0) * width + SC // 2, width)

    def body(i, carry):
        rows = pl.ds(pl.multiple_of(i * 8, 8), 8)
        full = fft16(
            [(y_ref[r, rows, pl.ds(low, width)], y_ref[r, rows, pl.ds(high, width)]) for r in range(SR)]
        )
        for s in range(SR):
            fr, fi = full[s]
            tc = lc_ref[s, rows, :]
            ts = ls_ref[s, rows, :]
            acc_ref[0, 0, s] += fr * tc - fi * ts
            acc_ref[0, 1, s] += fr * ts + fi * tc
            gr, gi = full[(SR - s) % SR]
            tc = uc_ref[s, rows, :]
            ts = us_ref[s, rows, :]
            acc_ref[1, 0, s] += gr * tc + gi * ts
            acc_ref[1, 1, s] += gr * ts - gi * tc
        return carry

    lax.fori_loop(0, lc_ref.shape[1] // 8, body, 0, unroll=2)
    for a in range(2):
        for b in range(2):
            out_ref[a, b] = jnp.sum(acc_ref[a, b], axis=1)


def spectrum(both_col, turn_cos, turn_sin):
    pixels = both_col.shape[1]
    half = SC // 2
    block = 128
    steps = half // block
    lower = lambda j: (0, 0, j)
    upper = lambda j: (0, 0, j + steps)
    spec = pl.pallas_call(
        spectrum_kernel,
        grid=(steps,),
        in_specs=[
            pl.BlockSpec(memory_space=pltpu.VMEM),
            pl.BlockSpec((SR, pixels, block), lower),
            pl.BlockSpec((SR, pixels, block), lower),
            pl.BlockSpec((SR, pixels, block), upper),
            pl.BlockSpec((SR, pixels, block), upper),
        ],
        out_specs=pl.BlockSpec((2, 2, SR, block), lambda j: (0, 0, 0, j)),
        out_shape=jax.ShapeDtypeStruct((2, 2, SR, half), jnp.float32),
        scratch_shapes=[pltpu.VMEM((2, 2, SR, 8, block), jnp.float32)],
        compiler_params=pltpu.CompilerParams(vmem_limit_bytes=40 * 1024 * 1024),
    )(both_col, turn_cos, turn_sin, turn_cos, turn_sin)
    return spec


def local(frames, offsets, bright, aberration):
    scan_size = lax.axis_size("scan")
    det_size = lax.axis_size("det")
    rows_dev, tile, detector = frames.shape
    owned = offsets.shape[0]
    groups = detector // owned
    owner = lax.axis_index("scan") * det_size + lax.axis_index("det")
    blocks = jnp.transpose(frames.reshape(rows_dev * tile, groups, owned), (1, 0, 2))
    arrived = lax.all_to_all(blocks, ("scan", "det"), split_axis=0, concat_axis=0, tiled=True)
    images = arrived.reshape(scan_size, det_size, rows_dev, tile, owned)
    half = SC // 2
    full_cols = jnp.arange(SC, dtype=jnp.int32)
    col_sin, col_cos = sincos_of_steps(
        jnp.mod(full_cols[:, None] * full_cols[None, :half], SC), SC
    )
    alternating = jnp.where(full_cols % 2 == 0, 1.0, -1.0)
    nyquist = jnp.where(jnp.arange(128)[None, :] == 0, alternating[:, None], 0.0)
    table = jnp.concatenate([col_cos, -col_sin, nyquist], axis=1).astype(jnp.bfloat16)
    both_col = jnp.einsum(
        "abrcp,acq->brpq",
        images,
        table.reshape(scan_size, tile, table.shape[1]),
        preferred_element_type=jnp.float32,
    ).reshape(SR, owned, table.shape[1])
    full_rows = jnp.arange(SR, dtype=jnp.int32)
    angles_by_row = phase_angles(full_rows, full_rows, SR)
    row_cos = jnp.cos(angles_by_row)
    row_sin = jnp.sin(angles_by_row)
    pixel_index = owner * owned + jnp.arange(owned, dtype=jnp.int32)
    steps = jnp.arange(half, dtype=jnp.int32)
    col_index = jnp.concatenate([steps, jnp.mod(SC - steps, SC), jnp.full((1,), half, jnp.int32)])
    row_part, col_part, moved_rows, moved_cols, spherical = phase_parts(
        pixel_index, offsets, aberration, col_index
    )
    moved_sq = moved_rows[:, :, None] + moved_cols.T[None, :, :]
    phase = row_part[:, :, None] + col_part.T[None, :, :] - spherical * (moved_sq * moved_sq)
    weights = bright.astype(jnp.float32)
    keep = (jnp.arange(SC + 1) != half).astype(jnp.float32)
    turn_sin, turn_cos = sincos(phase)
    turn_cos, turn_sin = lax.optimization_barrier(
        (
            turn_cos * weights[None, :, None] * keep[None, None, :],
            turn_sin * weights[None, :, None] * keep[None, None, :],
        )
    )
    parts = spectrum(both_col, turn_cos, turn_sin)
    nyquist_col = both_col[:, :, SC]
    nyquist_real = jnp.dot(row_cos.T, nyquist_col, precision=EXACT_PRECISION)
    nyquist_imag = -jnp.dot(row_sin.T, nyquist_col, precision=EXACT_PRECISION)
    last_cos = turn_cos[:, :, SC]
    last_sin = turn_sin[:, :, SC]
    nyquist_spec_real = jnp.sum(nyquist_real * last_cos - nyquist_imag * last_sin, axis=1)
    nyquist_spec_imag = jnp.sum(nyquist_real * last_sin + nyquist_imag * last_cos, axis=1)
    spectra = jnp.stack(
        [
            jnp.concatenate([parts[0, 0], parts[1, 0], nyquist_spec_real[:, None]], axis=1),
            jnp.concatenate([parts[0, 1], parts[1, 1], nyquist_spec_imag[:, None]], axis=1),
        ]
    )
    inverse_rows = jnp.stack(
        [
            jnp.stack([row_cos.T, -row_sin.T], axis=1),
            jnp.stack([row_sin.T, row_cos.T], axis=1),
        ]
    )
    rows_both = jnp.einsum("jrks,ksq->jrq", inverse_rows, spectra, precision=EXACT_PRECISION)
    rows_real = rows_both[0]
    rows_imag = rows_both[1]
    lanes = 2 * (SC + 1)
    packed = jnp.concatenate(
        [rows_real, rows_imag, jnp.broadcast_to(jnp.sum(weights), (SR, (-lanes) % 128 or 128))],
        axis=1,
    )
    width = tile + 2 * HALO
    columns = jnp.mod(
        lax.axis_index("scan") * tile - HALO + jnp.arange(width, dtype=jnp.int32), SC
    )
    col_angles = phase_angles(col_index, columns, SC)
    final_table = lax.optimization_barrier(
        jnp.concatenate([jnp.cos(col_angles), -jnp.sin(col_angles)], axis=0)
    )
    gathered = lax.all_to_all(packed, "det", 0, 0, tiled=True)
    own = pairwise_sum([gathered[i] for i in range(det_size)])
    spread = jnp.broadcast_to(own, (scan_size,) + own.shape)
    gathered = lax.all_to_all(spread, "scan", 0, 0, tiled=True)
    total = pairwise_sum([gathered[i] for i in range(scan_size)])
    bright_sum = total[lanes]
    picture = jnp.dot(total[:lanes], final_table, precision=EXACT_PRECISION)
    return (
        (picture * (1.0 / (SR * SC)) / jnp.sqrt(bright_sum) * window_weights(width))
        .reshape(rows_dev, 1, width)
    )


def solution(mesh):
    placed = (P("det", "scan", None), P(("scan", "det"), None), P(("scan", "det")), P())
    return jax.shard_map(
        local, mesh=mesh, in_specs=placed, out_specs=P("det", "scan", None), check_vma=False
    )
```

```python
import math

import jax
import jax.numpy as jnp
from jax import lax
from jax.sharding import PartitionSpec as P
from jax.experimental import pallas as pl
from jax.experimental.pallas import tpu as pltpu

SR = 16
SC = 1024
DROWS = 128
DCOLS = 128
HALO = 16


TWO_PI = 2.0 * math.pi
EXACT_PRECISION = lax.Precision.HIGHEST


def phase_angles(first, second_operand, modulus):
    product = jnp.mod(first[:, None] * second_operand[None, :], modulus)
    return TWO_PI / modulus * product.astype(jnp.float32)


def signed_frequency(length):
    position = jnp.arange(length, dtype=jnp.int32)
    folded = jnp.where(position < length // 2, position, position - length)
    return 2.0 * folded.astype(jnp.float32) / length


def pixel_phase(pixel_index, shifts, aberration):
    freq_rows = signed_frequency(SR)[:, None, None]
    freq_cols = signed_frequency(SC)[None, :, None]
    half_rows = DROWS // 2
    half_cols = DCOLS // 2
    tilt_x = ((pixel_index // DCOLS - half_rows).astype(jnp.float32) / half_rows)[None, None, :]
    tilt_y = ((pixel_index % DCOLS - half_cols).astype(jnp.float32) / half_cols)[None, None, :]
    ramp_rows = jnp.mod(jnp.arange(SR, dtype=jnp.int32)[:, None] * shifts[:, 0][None, :], SR)
    ramp_cols = jnp.mod(jnp.arange(SC, dtype=jnp.int32)[:, None] * shifts[:, 1][None, :], SC)
    shift_phase = (
        TWO_PI / SR * ramp_rows.astype(jnp.float32)[:, None, :]
        + TWO_PI / SC * ramp_cols.astype(jnp.float32)[None, :, :]
    )
    tilt_sq = tilt_x * tilt_x + tilt_y * tilt_y
    tilt_dot = tilt_x * freq_rows + tilt_y * freq_cols
    moved_x = freq_rows + tilt_x
    moved_y = freq_cols + tilt_y
    moved_sq = moved_x * moved_x + moved_y * moved_y
    lens_phase = math.pi * (
        aberration[0] * (freq_rows * freq_rows + freq_cols * freq_cols)
        + aberration[1] * (moved_sq * moved_sq - tilt_sq * tilt_sq - 4.0 * tilt_sq * tilt_dot)
    )
    return shift_phase - lens_phase


def window_weights(width):
    position = jnp.arange(width, dtype=jnp.int32)
    nearest = jnp.minimum(position, width - 1 - position)
    ramped = 0.3 + 0.35 * (
        1.0 - jnp.cos(math.pi * (nearest.astype(jnp.float32) + 0.5) / (2 * HALO))
    )
    return jnp.where(nearest < 2 * HALO, ramped, jnp.float32(1.0))


def inverse_transform(spec_real, spec_imag, columns, rows):
    real_piece = jnp.dot(spec_real, cos_cols, precision=EXACT_PRECISION) - jnp.dot(
        spec_imag, sin_cols, precision=EXACT_PRECISION
    )
    imaginary_piece = jnp.dot(spec_real, sin_cols, precision=EXACT_PRECISION) + jnp.dot(
        spec_imag, cos_cols, precision=EXACT_PRECISION
    )
    angles_by_row = phase_angles(jnp.arange(SR, dtype=jnp.int32), rows, SR)
    row_cosines = jnp.cos(angles_by_row)
    row_sines = jnp.sin(angles_by_row)
    return jnp.dot(row_cosines.T, real_piece, precision=EXACT_PRECISION) - jnp.dot(
        row_sines.T, imaginary_piece, precision=EXACT_PRECISION
    )


def sincos_reduced(rest, quadrant):
    square = rest * rest
    sine = rest + rest * square * (
        -1.6666654611e-1 + square * (8.3321608736e-3 + square * -1.9515295891e-4)
    )
    cosine = 1.0 - 0.5 * square + square * square * (
        4.166664568298827e-2 + square * (-1.388731625493765e-3 + square * 2.443315711809948e-5)
    )
    swap = (quadrant & 1) == 1
    sin_out = jnp.where(swap, cosine, sine)
    cos_out = jnp.where(swap, sine, cosine)
    sin_out = jnp.where(quadrant >= 2, -sin_out, sin_out)
    cos_out = jnp.where((quadrant == 1) | (quadrant == 2), -cos_out, cos_out)
    return sin_out, cos_out


def sincos(angle):
    turns = jnp.round(angle * (2.0 / math.pi))
    quadrant = turns.astype(jnp.int32) & 3
    rest = angle - turns * 1.5703125
    rest = rest - turns * 4.837512969970703125e-4
    rest = rest - turns * 7.54978995489188216e-8
    return sincos_reduced(rest, quadrant)


def sincos_of_steps(steps, modulus):
    quarter = modulus // 4
    turns = (steps + quarter // 2) // quarter
    rest = (steps - turns * quarter).astype(jnp.float32) * (TWO_PI / modulus)
    return sincos_reduced(rest, turns & 3)


def pairwise_sum(values):
    while len(values) > 1:
        values = [
            values[e] + values[e + 1] if e + 1 < len(values) else values[e]
            for e in range(0, len(values), 2)
        ]
    return values[0]


def phase_parts(pixel_index, shifts, aberration, col_index):
    freq_rows = signed_frequency(SR)[:, None]
    freq_cols = (2.0 * jnp.where(col_index < SC // 2, col_index, col_index - SC).astype(jnp.float32) / SC)[:, None]
    half_rows = DROWS // 2
    half_cols = DCOLS // 2
    tilt_x = ((pixel_index // DCOLS - half_rows).astype(jnp.float32) / half_rows)[None, :]
    tilt_y = ((pixel_index % DCOLS - half_cols).astype(jnp.float32) / half_cols)[None, :]
    ramp_rows = jnp.mod(jnp.arange(SR, dtype=jnp.int32)[:, None] * shifts[:, 0][None, :], SR)
    ramp_cols = jnp.mod(col_index[:, None] * shifts[:, 1][None, :], SC)
    tilt_sq = tilt_x * tilt_x + tilt_y * tilt_y
    defocus = math.pi * aberration[0]
    spherical = math.pi * aberration[1]
    row_part = (
        TWO_PI / SR * ramp_rows.astype(jnp.float32)
        - defocus * freq_rows * freq_rows
        + spherical * (tilt_sq * tilt_sq + 4.0 * tilt_sq * tilt_x * freq_rows)
    )
    col_part = (
        TWO_PI / SC * ramp_cols.astype(jnp.float32)
        - defocus * freq_cols * freq_cols
        + spherical * (4.0 * tilt_sq * tilt_y * freq_cols)
    )
    moved_rows = (freq_rows + tilt_x) * (freq_rows + tilt_x)
    moved_cols = (freq_cols + tilt_y) * (freq_cols + tilt_y)
    return row_part, col_part, moved_rows, moved_cols, spherical


def four_point(points):
    (ar, ai), (br, bi), (cr, ci), (dr, di) = points
    s02r = ar + cr
    s02i = ai + ci
    d02r = ar - cr
    d02i = ai - ci
    s13r = br + dr
    s13i = bi + di
    d13r = br - dr
    d13i = bi - di
    return [
        (s02r + s13r, s02i + s13i),
        (d02r + d13i, d02i - d13r),
        (s02r - s13r, s02i - s13i),
        (d02r - d13i, d02i + d13r),
    ]


def fft16(points):
    twisted = {}
    for b in range(4):
        column = four_point([points[4 * a + b] for a in range(4)])
        for s1, (gr, gi) in enumerate(column):
            k = b * s1
            if k == 0:
                twisted[b, s1] = (gr, gi)
            elif k == 4:
                twisted[b, s1] = (gi, -gr)
            else:
                c = math.cos(TWO_PI * k / 16)
                d = math.sin(TWO_PI * k / 16)
                twisted[b, s1] = (gr * c + gi * d, gi * c - gr * d)
    out = [None] * 16
    for s1 in range(4):
        row = four_point([twisted[b, s1] for b in range(4)])
        for s2 in range(4):
            out[s1 + 4 * s2] = row[s2]
    return out


def spectrum_kernel(y_ref, lc_ref, ls_ref, uc_ref, us_ref, out_ref, acc_ref):
    acc_ref[...] = jnp.zeros(acc_ref.shape, acc_ref.dtype)
    width = lc_ref.shape[2]
    low = pl.multiple_of(pl.program_id(0) * width, width)
    high = pl.multiple_of(pl.program_id(0) * width + SC // 2, width)

    def body(i, carry):
        rows = pl.ds(pl.multiple_of(i * 8, 8), 8)
        full = fft16(
            [(y_ref[r, rows, pl.ds(low, width)], y_ref[r, rows, pl.ds(high, width)]) for r in range(SR)]
        )
        for s in range(SR):
            fr, fi = full[s]
            tc = lc_ref[s, rows, :]
            ts = ls_ref[s, rows, :]
            acc_ref[0, 0, s] += fr * tc - fi * ts
            acc_ref[0, 1, s] += fr * ts + fi * tc
            gr, gi = full[(SR - s) % SR]
            tc = uc_ref[s, rows, :]
            ts = us_ref[s, rows, :]
            acc_ref[1, 0, s] += gr * tc + gi * ts
            acc_ref[1, 1, s] += gr * ts - gi * tc
        return carry

    lax.fori_loop(0, lc_ref.shape[1] // 8, body, 0, unroll=8)
    for a in range(2):
        for b in range(2):
            out_ref[a, b] = jnp.sum(acc_ref[a, b], axis=1)


def spectrum(both_col, turn_cos, turn_sin):
    pixels = both_col.shape[1]
    half = SC // 2
    block = 128
    steps = half // block
    lower = lambda j: (0, 0, j)
    upper = lambda j: (0, 0, j + steps)
    spec = pl.pallas_call(
        spectrum_kernel,
        grid=(steps,),
        in_specs=[
            pl.BlockSpec(memory_space=pltpu.VMEM),
            pl.BlockSpec((SR, pixels, block), lower),
            pl.BlockSpec((SR, pixels, block), lower),
            pl.BlockSpec((SR, pixels, block), upper),
            pl.BlockSpec((SR, pixels, block), upper),
        ],
        out_specs=pl.BlockSpec((2, 2, SR, block), lambda j: (0, 0, 0, j)),
        out_shape=jax.ShapeDtypeStruct((2, 2, SR, half), jnp.float32),
        scratch_shapes=[pltpu.VMEM((2, 2, SR, 8, block), jnp.float32)],
        compiler_params=pltpu.CompilerParams(vmem_limit_bytes=40 * 1024 * 1024),
    )(both_col, turn_cos, turn_sin, turn_cos, turn_sin)
    return spec


def local(frames, offsets, bright, aberration):
    scan_size = lax.axis_size("scan")
    det_size = lax.axis_size("det")
    rows_dev, tile, detector = frames.shape
    owned = offsets.shape[0]
    groups = detector // owned
    owner = lax.axis_index("scan") * det_size + lax.axis_index("det")
    blocks = jnp.transpose(frames.reshape(rows_dev * tile, groups, owned), (1, 0, 2))
    arrived = lax.all_to_all(blocks, ("scan", "det"), split_axis=0, concat_axis=0, tiled=True)
    images = arrived.reshape(scan_size, det_size, rows_dev, tile, owned)
    half = SC // 2
    full_cols = jnp.arange(SC, dtype=jnp.int32)
    col_sin, col_cos = sincos_of_steps(
        jnp.mod(full_cols[:, None] * full_cols[None, :half], SC), SC
    )
    alternating = jnp.where(full_cols % 2 == 0, 1.0, -1.0)
    nyquist = jnp.where(jnp.arange(128)[None, :] == 0, alternating[:, None], 0.0)
    table = jnp.concatenate([col_cos, -col_sin, nyquist], axis=1).astype(jnp.bfloat16)
    both_col = jnp.einsum(
        "abrcp,acq->brpq",
        images,
        table.reshape(scan_size, tile, table.shape[1]),
        preferred_element_type=jnp.float32,
    ).reshape(SR, owned, table.shape[1])
    full_rows = jnp.arange(SR, dtype=jnp.int32)
    angles_by_row = phase_angles(full_rows, full_rows, SR)
    row_cos = jnp.cos(angles_by_row)
    row_sin = jnp.sin(angles_by_row)
    pixel_index = owner * owned + jnp.arange(owned, dtype=jnp.int32)
    steps = jnp.arange(half, dtype=jnp.int32)
    col_index = jnp.concatenate([steps, jnp.mod(SC - steps, SC), jnp.full((1,), half, jnp.int32)])
    row_part, col_part, moved_rows, moved_cols, spherical = phase_parts(
        pixel_index, offsets, aberration, col_index
    )
    moved_sq = moved_rows[:, :, None] + moved_cols.T[None, :, :]
    phase = row_part[:, :, None] + col_part.T[None, :, :] - spherical * (moved_sq * moved_sq)
    weights = bright.astype(jnp.float32)
    keep = (jnp.arange(SC + 1) != half).astype(jnp.float32)
    turn_sin, turn_cos = sincos(phase)
    turn_cos, turn_sin = lax.optimization_barrier(
        (
            turn_cos * weights[None, :, None] * keep[None, None, :],
            turn_sin * weights[None, :, None] * keep[None, None, :],
        )
    )
    parts = spectrum(both_col, turn_cos, turn_sin)
    nyquist_col = both_col[:, :, SC]
    nyquist_real = jnp.dot(row_cos.T, nyquist_col, precision=EXACT_PRECISION)
    nyquist_imag = -jnp.dot(row_sin.T, nyquist_col, precision=EXACT_PRECISION)
    last_cos = turn_cos[:, :, SC]
    last_sin = turn_sin[:, :, SC]
    nyquist_spec_real = jnp.sum(nyquist_real * last_cos - nyquist_imag * last_sin, axis=1)
    nyquist_spec_imag = jnp.sum(nyquist_real * last_sin + nyquist_imag * last_cos, axis=1)
    spectra = jnp.stack(
        [
            jnp.concatenate([parts[0, 0], parts[1, 0], nyquist_spec_real[:, None]], axis=1),
            jnp.concatenate([parts[0, 1], parts[1, 1], nyquist_spec_imag[:, None]], axis=1),
        ]
    )
    inverse_rows = jnp.stack(
        [
            jnp.stack([row_cos.T, -row_sin.T], axis=1),
            jnp.stack([row_sin.T, row_cos.T], axis=1),
        ]
    )
    rows_both = jnp.einsum("jrks,ksq->jrq", inverse_rows, spectra, precision=EXACT_PRECISION)
    rows_real = rows_both[0]
    rows_imag = rows_both[1]
    lanes = 2 * (SC + 1)
    packed = jnp.concatenate(
        [rows_real, rows_imag, jnp.broadcast_to(jnp.sum(weights), (SR, (-lanes) % 128 or 128))],
        axis=1,
    )
    width = tile + 2 * HALO
    columns = jnp.mod(
        lax.axis_index("scan") * tile - HALO + jnp.arange(width, dtype=jnp.int32), SC
    )
    col_angles = phase_angles(col_index, columns, SC)
    final_table = lax.optimization_barrier(
        jnp.concatenate([jnp.cos(col_angles), -jnp.sin(col_angles)], axis=0)
    )
    gathered = lax.all_to_all(packed, "det", 0, 0, tiled=True)
    own = pairwise_sum([gathered[i] for i in range(det_size)])
    spread = jnp.broadcast_to(own, (scan_size,) + own.shape)
    gathered = lax.all_to_all(spread, "scan", 0, 0, tiled=True)
    total = pairwise_sum([gathered[i] for i in range(scan_size)])
    bright_sum = total[lanes]
    picture = jnp.dot(total[:lanes], final_table, precision=EXACT_PRECISION)
    return (
        (picture * (1.0 / (SR * SC)) / jnp.sqrt(bright_sum) * window_weights(width))
        .reshape(rows_dev, 1, width)
    )


def solution(mesh):
    placed = (P("det", "scan", None), P(("scan", "det"), None), P(("scan", "det")), P())
    return jax.shard_map(
        local, mesh=mesh, in_specs=placed, out_specs=P("det", "scan", None), check_vma=False
    )
```
